32 devices in a mesh: gx: 4 (over y, core), gy: 8 (over z, x).
Axes of the slice: x: 2, y: 2, z: 4, core: 2. Of those that a mesh axis runs over, the one named last changes fastest.
Arguments:
- atm_state: float32 [4, 40, 64, 1024], P(None, None, 'gx', 'gy'), may hold values from -6 to 6
- metric: float32 [2, 64, 1024], P(None, 'gx', 'gy'), may hold values from 0.5 to 2
- send_idx: int32 [32, 32, 256], P(('gx', 'gy')), may hold values from 0 to 2047
- send_counts: int32 [32, 32], P(('gx', 'gy')), may hold values from 1 to 256, as said below
- ocean_tracers: float32 [2, 40, 64, 1024], P(None, None, 'gx', 'gy'), may hold values from -6 to 6
- ocean_velocity: float32 [2, 40, 64, 1024], P(None, None, 'gx', 'gy'), may hold values from -0.2 to 0.2
- remap_slots: int32 [4, 64, 1024], P(None, 'gx', 'gy'), may hold values from 0 to 8191, as said below
- remap_weights: float32 [4, 64, 1024], P(None, 'gx', 'gy'), may hold values from 0.1 to 0.5
Outputs:
- atm_out: float32 [4, 40, 64, 1024], P(None, None, 'gx', 'gy')
- ocean_out: float32 [2, 40, 64, 1024], P(None, None, 'gx', 'gy')
The draws below stay inside these ranges and needn't reach their ends.
Inputs may be any that keep to these rules, and one draw needn't show every extreme that they name: `send_counts`: each destination gets at least one data slot from every source; for a quarter of the destinations (at least one) and for the last source, every slot carries data. `remap_slots`: every entry names a slot r = s * 256 + c with c below send_counts[s, d] for the cell's own partition d.
All inputs are finite; a program needn't handle non-finite values.
Results may differ from the reference program's by a relative error of at most 0.0001.
Values sent between devices are 32-bit elements; how exact they have to be, the bound alone decides.
No kernel may reach another device: no remote copies, remote signals or barrier semaphores. Data moves between devices by JAX's collectives and lax.ppermute only.
A program may use at most 128 MiB of HBM per device.

```python
import math
import jax
import jax.numpy as jnp
import numpy as np
from jax import lax

FA = 4
ALEV = 40
EX = 4
EY = 32
SUB = 2
OX = 16
OY = 128
OLEV = 40
OSTEPS = 2
CAP = 256
NW = 4
RANKS = 32
GXA = 64
GYA = 1024
OXG = 64
OYG = 1024
N_GX = 4
N_GY = 8


def count_table(key):
    folded = jax.random.fold_in(key, 7)
    key_one, key_two = jax.random.split(folded)
    base_counts = jax.random.randint(key_one, (RANKS, RANKS), 1, CAP // 2 + 1)
    rank_order = jax.random.permutation(key_two, RANKS)
    busy_dest = rank_order < max(RANKS // 4, 1)
    count_grid = jnp.where(busy_dest[None, :], CAP, base_counts)
    count_grid = count_grid.at[RANKS - 1, :].set(CAP)
    return count_grid.astype(jnp.int32)


def draw_send_counts(key, part):
    return count_table(key)


def draw_remap_slots(key, part):
    count_grid = count_table(key)
    key_one, key_two = jax.random.split(jax.random.fold_in(key, 13))
    row_part = jnp.arange(OXG) // OX
    col_part = jnp.arange(OYG) // OY
    owner_rank = row_part[:, None] * (OYG // OY) + col_part[None, :]
    source = jax.random.randint(key_one, (NW, OXG, OYG), 0, RANKS)
    slot_limit = count_grid[source, jnp.broadcast_to(owner_rank[None], (NW, OXG, OYG))]
    slot_place = jax.random.randint(key_two, (NW, OXG, OYG), 0, slot_limit)
    slot_ids = source * CAP + slot_place
    slot_ids = slot_ids.at[0, ::OX, ::OY].set(RANKS * CAP - 1)
    slot_ids = slot_ids.at[1, ::OX, ::OY].set(0)
    return slot_ids.astype(jnp.int32)


def touch_ends(drawn, rng, low, largest):
    place = [jax.random.randint(jax.random.fold_in(rng, axis), (), 0, length) for axis, length in enumerate(drawn.shape)]
    longest = drawn.shape.index(max(drawn.shape))
    next_to = place[:longest] + [(place[longest] + 1) % drawn.shape[longest]] + place[longest + 1:]
    return drawn.at[tuple(place)].set(low).at[tuple(next_to)].set(largest)


def shard_levels(own_key, extent, cuts, low, high):
    loudness = 1.0
    for dim, parts in cuts:
        steps = jax.random.uniform(jax.random.fold_in(jax.random.fold_in(own_key, 6), dim), (parts,), jnp.float32, low / len(cuts), high / len(cuts))
        loudness = loudness * jnp.repeat(jnp.exp(steps), extent[dim] // parts).reshape((-1,) + (1,) * (len(extent) - 1 - dim))
    return loudness


def centred(own_key, shape, spread, bound, cuts=(), dtype=jnp.bfloat16):
    loudness = shard_levels(own_key, shape, cuts, -0.22, 0.18) if cuts else 1.0
    result = jax.random.normal(own_key, shape, jnp.float32) * spread * loudness
    return jnp.minimum(jnp.maximum(result, -bound), bound).astype(dtype)


def setup_inputs(seed: int = 0) -> dict:
    streams_of = jax.random.split(jax.random.key(seed), 9)
    atm_state = centred(streams_of[0], (FA, ALEV, GXA, GYA), 1.0, 6.0, ((2, 4), (3, 8)), jnp.float32)
    metric = jnp.clip(jnp.exp(math.log(2.0) - 1.3862944 * jax.random.uniform(streams_of[1], (2, GXA, GYA), jnp.float32) ** shard_levels(streams_of[1], (2, GXA, GYA), ((1, 4), (2, 8)), -0.2, 0.2)), 0.5, 2.0)
    send_idx = touch_ends(jax.random.randint(streams_of[2], (RANKS, RANKS, CAP), 0, 16 * EX * EY), jax.random.fold_in(streams_of[2], 1), 0, (16 * EX * EY) - 1).astype(jnp.int32)
    send_counts = draw_send_counts(jax.random.fold_in(streams_of[8], 71), 0)
    ocean_tracers = centred(streams_of[4], (2, OLEV, OXG, OYG), 1.0, 6.0, ((2, 4), (3, 8)), jnp.float32)
    ocean_velocity = jnp.clip(jax.random.uniform(streams_of[5], (2, OLEV, OXG, OYG), jnp.float32, -0.2, 0.2) * shard_levels(streams_of[5], (2, OLEV, OXG, OYG), ((2, 4), (3, 8)), -0.4, 0.0), -0.2, 0.2)
    remap_slots = draw_remap_slots(jax.random.fold_in(streams_of[8], 71), 0)
    remap_weights = jnp.clip(jnp.exp(math.log(0.5) - 1.609438 * jax.random.uniform(streams_of[7], (NW, OXG, OYG), jnp.float32) ** shard_levels(streams_of[7], (NW, OXG, OYG), ((1, 4), (2, 8)), -0.2, 0.2)), 0.1, 0.5)
    return dict(atm_state=atm_state, metric=metric, send_idx=send_idx, send_counts=send_counts, ocean_tracers=ocean_tracers, ocean_velocity=ocean_velocity, remap_slots=remap_slots, remap_weights=remap_weights)


visc_coef = 0.01
diff_coef = 0.2
wind_coef = 0.1
surf_coef = 0.2

def gll_tables():
    points = np.array([-1.0, -1.0 / np.sqrt(5.0), 1.0 / np.sqrt(5.0), 1.0])
    weights = np.array([1.0 / 6.0, 5.0 / 6.0, 5.0 / 6.0, 1.0 / 6.0])
    derivative = np.zeros((4, 4))
    for target in range(4):
        for source in range(4):
            if target == source:
                derivative[target, source] = np.sum([1.0 / (points[source] - points[others]) for others in range(4) if others != source])
            else:
                numer = np.prod([points[target] - points[others] for others in range(4) if others != target and others != source])
                denom = np.prod([points[source] - points[others] for others in range(4) if others != source])
                derivative[target, source] = numer / denom
    massw = np.array([1.0 / 3.0, 5.0 / 6.0, 5.0 / 6.0, 1.0 / 3.0])
    return (derivative, weights, massw)

def pair_sum(values_in, along):
    length = values_in.shape[along]
    layout = [1] * values_in.ndim
    layout[along] = length
    position = (jnp.arange(length) % 4).reshape(layout)
    before = jnp.roll(values_in, 1, along)
    after = jnp.roll(values_in, -1, along)
    return values_in + jnp.where(position == 0, before, jnp.where(position == 3, after, 0.0))

def assemble(values_in):
    return pair_sum(pair_sum(values_in, values_in.ndim - 1), values_in.ndim - 2)

def stiffness(state_in, metric, derivative, weights):
    levels, xsize, ysize = state_in.shape
    highest = lax.Precision.HIGHEST
    blocks = state_in.reshape(levels, xsize // 4, 4, ysize // 4, 4)
    metric_x = metric[0].reshape(xsize // 4, 4, ysize // 4, 4)
    metric_y = metric[1].reshape(xsize // 4, 4, ysize // 4, 4)
    weight_x = weights.reshape(4, 1, 1)
    weight_y = weights
    along_x = jnp.einsum('ab,lxbyc->lxayc', derivative, blocks, precision=highest)
    term_x = jnp.einsum('ba,lxbyc->lxayc', derivative, weight_x * metric_x * along_x, precision=highest) * weight_y
    along_y = jnp.einsum('dc,lxayc->lxayd', derivative, blocks, precision=highest)
    term_y = jnp.einsum('cd,lxayc->lxayd', derivative, weight_y * metric_y * along_y, precision=highest) * weight_x
    return (term_x + term_y).reshape(levels, xsize, ysize)

def tracer_step(tracers, velocity):
    east = jnp.roll(tracers, -1, 2)
    west = jnp.roll(tracers, 1, 2)
    north = jnp.roll(tracers, -1, 3)
    south = jnp.roll(tracers, 1, 3)
    return tracers + diff_coef * (east + west + north + south - 4.0 * tracers) - 0.5 * velocity[0] * (east - west) - 0.5 * velocity[1] * (north - south)

def reference(atm_state, metric, send_idx, send_counts, ocean_tracers, ocean_velocity, remap_slots, remap_weights):
    derivative_np, weights_np, massw_np = gll_tables()
    derivative = jnp.asarray(derivative_np, jnp.float32)
    weights = jnp.asarray(weights_np, jnp.float32)
    inv_mass = jnp.asarray(1.0 / (np.tile(massw_np, GXA // 4)[:, None] * np.tile(massw_np, GYA // 4)[None, :]), jnp.float32)

    def one_field(state_in):
        state_now = state_in
        for substep in range(SUB):
            stiff = stiffness(state_now, metric, derivative, weights)
            state_now = state_now - visc_coef * assemble(stiff) * inv_mass
        return state_now
    atm_out = lax.map(one_field, atm_state)
    bottom = atm_out[:, ALEV - 1]
    speed = jnp.sqrt(1.0 + bottom[0] * bottom[0] + bottom[1] * bottom[1])
    flux = bottom * speed
    lx_size = 4 * EX
    ly_size = 4 * EY
    flux_dev = flux.reshape(FA, N_GX, lx_size, N_GY, ly_size).transpose(1, 3, 0, 2, 4).reshape(RANKS, FA, lx_size * ly_size)
    row_part = (jnp.arange(OXG) // OX).astype(jnp.int32)
    col_part = (jnp.arange(OYG) // OY).astype(jnp.int32)
    owner_rank = row_part[:, None] * N_GY + col_part[None, :]
    source = remap_slots // CAP
    slot_place = remap_slots % CAP
    dest = jnp.broadcast_to(owner_rank[None], remap_slots.shape)
    node_ids = send_idx[source, dest, slot_place]
    keep = (slot_place < send_counts[source, dest]).astype(jnp.float32)
    values = flux_dev[source, :, node_ids]
    masked = values * keep[..., None]
    ocean_flux = jnp.moveaxis(lax.optimization_barrier(jnp.sum(remap_weights[..., None] * masked, axis=0)), -1, 0)
    velocity = ocean_velocity.at[0, 0].add(wind_coef * jnp.tanh(ocean_flux[0]))
    velocity = velocity.at[1, 0].add(wind_coef * jnp.tanh(ocean_flux[1]))
    tracers = ocean_tracers.at[0, 0].add(surf_coef * ocean_flux[2])
    tracers = tracers.at[1, 0].add(surf_coef * ocean_flux[3])
    for repeat in range(OSTEPS):
        tracers = tracer_step(tracers, velocity)
    return (atm_out, tracers)
```

```python
import math

import jax
import jax.numpy as jnp
import numpy as np
from jax import lax
from jax.experimental import pallas as pl
from jax.sharding import PartitionSpec as P

SUB = 2
OSTEPS = 2


visc_coef = 0.01
diff_coef = 0.2
wind_coef = 0.1
surf_coef = 0.2


def extended(cells, sides, width):
    for axis, dim in sides:
        count = lax.axis_size(axis)
        head = lax.slice_in_dim(cells, 0, width, axis=dim)
        tail = lax.slice_in_dim(cells, cells.shape[dim] - width, cells.shape[dim], axis=dim)
        cells = jnp.concatenate(
            [
                lax.ppermute(tail, axis, [(i, (i + 1) % count) for i in range(count)]),
                cells,
                lax.ppermute(head, axis, [((i + 1) % count, i) for i in range(count)]),
            ],
            axis=dim,
        )
    return cells


def gll_tables():
    points = np.array([-1.0, -1.0 / np.sqrt(5.0), 1.0 / np.sqrt(5.0), 1.0])
    weights = np.array([1.0 / 6.0, 5.0 / 6.0, 5.0 / 6.0, 1.0 / 6.0])
    derivative = np.zeros((4, 4))
    for target in range(4):
        for source in range(4):
            if target == source:
                derivative[target, source] = np.sum(
                    [
                        1.0 / (points[source] - points[others])
                        for others in range(4)
                        if others != source
                    ]
                )
            else:
                numer = np.prod(
                    [
                        points[target] - points[others]
                        for others in range(4)
                        if others != target and others != source
                    ]
                )
                denom = np.prod(
                    [points[source] - points[others] for others in range(4) if others != source]
                )
                derivative[target, source] = numer / denom
    massw = np.array([1.0 / 3.0, 5.0 / 6.0, 5.0 / 6.0, 1.0 / 3.0])
    return (derivative, weights, massw)


def stiffness(state_in, metric_x, metric_y, derivative_np, weights_np):
    levels, xsize, ysize = state_in.shape
    highest = lax.Precision.HIGHEST
    block_x = jnp.asarray(np.kron(np.eye(xsize // 4), derivative_np), jnp.float32)
    block_y = jnp.asarray(np.kron(np.eye(ysize // 4), derivative_np), jnp.float32)
    weight_x = jnp.asarray(np.tile(weights_np, xsize // 4), jnp.float32)[:, None]
    weight_y = jnp.asarray(np.tile(weights_np, ysize // 4), jnp.float32)[None, :]
    along_x = jnp.einsum("ab,lby->lay", block_x, state_in, precision=highest)
    term_x = (
        jnp.einsum("ba,lby->lay", block_x, weight_x * metric_x * along_x, precision=highest)
        * weight_y
    )
    along_y = jnp.einsum("lxc,dc->lxd", state_in, block_y, precision=highest)
    term_y = (
        jnp.einsum("lxc,cd->lxd", weight_y * metric_y * along_y, block_y, precision=highest)
        * weight_x
    )
    return term_x + term_y


def mass_inverse(massw_np, xsize, ysize):
    return jnp.asarray(
        1.0 / (np.tile(massw_np, xsize // 4)[:, None] * np.tile(massw_np, ysize // 4)[None, :]),
        jnp.float32,
    )


def edge_sum(padded):
    inner_y = padded.shape[2] - 2
    ypos = jnp.arange(inner_y) % 4
    centre = padded[:, :, 1:-1]
    merged = centre + jnp.where(
        ypos == 0, padded[:, :, :-2], jnp.where(ypos == 3, padded[:, :, 2:], 0.0)
    )
    inner_x = merged.shape[1] - 2
    xpos = (jnp.arange(inner_x) % 4)[:, None]
    middle = merged[:, 1:-1]
    return middle + jnp.where(xpos == 0, merged[:, :-2], jnp.where(xpos == 3, merged[:, 2:], 0.0))


def tracer_step(padded, velocity):
    centre = padded[..., 1:-1, 1:-1]
    east = padded[..., 2:, 1:-1]
    west = padded[..., :-2, 1:-1]
    north = padded[..., 1:-1, 2:]
    south = padded[..., 1:-1, :-2]
    return (
        centre
        + diff_coef * (east + west + north + south - 4.0 * centre)
        - 0.5 * velocity[0] * (east - west)
        - 0.5 * velocity[1] * (north - south)
    )


def split_bf16(values):
    first = values.astype(jnp.bfloat16)
    rest = values - first.astype(jnp.float32)
    second = rest.astype(jnp.bfloat16)
    third = (rest - second.astype(jnp.float32)).astype(jnp.bfloat16)
    return jnp.stack([first, second, third], axis=1)


def gather_kernel(index_ref, table_ref, out_ref):
    fields, rows, tile = out_ref.shape[0], table_ref.shape[1] // 3, out_ref.shape[1]
    index = index_ref[...]
    onehot = (lax.broadcasted_iota(jnp.int32, (128, tile), 0) == (index & 127)).astype(jnp.bfloat16)
    select = lax.broadcasted_iota(jnp.int32, (rows, tile), 0) == (index >> 7)
    for field in range(fields):
        picked = jnp.dot(table_ref[field], onehot, preferred_element_type=jnp.float32)
        whole = picked[:rows] + picked[rows : 2 * rows] + picked[2 * rows :]
        out_ref[pl.ds(field, 1), :] = jnp.sum(jnp.where(select, whole, 0.0), axis=0, keepdims=True)


def onehot_gather(table, index):
    fields, total = table.shape
    rows = total // 128
    parts = split_bf16(table.reshape(fields, rows, 128)).reshape(fields, 3 * rows, 128)
    flat = index.reshape(1, -1)
    count = flat.shape[1]
    tile = math.gcd(count, 1024)
    return pl.pallas_call(
        gather_kernel,
        grid=(count // tile,),
        in_specs=[
            pl.BlockSpec((1, tile), lambda step: (0, step)),
            pl.BlockSpec((fields, 3 * rows, 128), lambda step: (0, 0, 0)),
        ],
        out_specs=pl.BlockSpec((fields, tile), lambda step: (0, step)),
        out_shape=jax.ShapeDtypeStruct((fields, count), jnp.float32),
    )(flat, parts)


def per_device(
    atm_state,
    metric,
    send_idx,
    send_counts,
    ocean_tracers,
    ocean_velocity,
    remap_slots,
    remap_weights,
):
    fields, levels, xlocal, ylocal = atm_state.shape
    derivative_np, weights_np, massw_np = gll_tables()
    state_now = atm_state.reshape(fields * levels, xlocal, ylocal)
    inv_mass = mass_inverse(massw_np, xlocal, ylocal)
    for substep in range(SUB):
        stiff = stiffness(state_now, metric[0], metric[1], derivative_np, weights_np)
        padded = extended(stiff, (("gx", 1), ("gy", 2)), 1)
        state_now = state_now - visc_coef * edge_sum(padded) * inv_mass
    atm_out = state_now.reshape(fields, levels, xlocal, ylocal)
    bottom = atm_out[:, levels - 1]
    speed = jnp.sqrt(1.0 + bottom[0] * bottom[0] + bottom[1] * bottom[1])
    flux_flat = (bottom * speed).reshape(fields, xlocal * ylocal)
    node_total = xlocal * ylocal
    rank_total = send_idx.shape[1]
    slot_cap = send_idx.shape[2]
    payload = onehot_gather(flux_flat, send_idx[0]).reshape(fields, rank_total, slot_cap)
    count_row = send_counts[0]
    live_slots = (jnp.arange(slot_cap)[None, :] < count_row[:, None]).astype(jnp.float32)
    payload = payload * live_slots[None]
    received = lax.all_to_all(payload, ("gx", "gy"), split_axis=1, concat_axis=1, tiled=True)
    received = received.reshape(fields, -1)
    source_count, ocean_x, ocean_y = remap_slots.shape
    gathered = onehot_gather(received, remap_slots).reshape(fields, source_count, ocean_x, ocean_y)
    ocean_flux = jnp.sum(remap_weights[None] * gathered, axis=1)
    velocity = ocean_velocity.at[0, 0].add(wind_coef * jnp.tanh(ocean_flux[0]))
    velocity = velocity.at[1, 0].add(wind_coef * jnp.tanh(ocean_flux[1]))
    tracers = ocean_tracers.at[0, 0].add(surf_coef * ocean_flux[2])
    tracers = tracers.at[1, 0].add(surf_coef * ocean_flux[3])
    for repeat in range(OSTEPS):
        ocean_pad = extended(tracers, (("gx", 2), ("gy", 3)), 1)
        tracers = tracer_step(ocean_pad, velocity)
    return (atm_out, tracers)


def solution(mesh):
    in_specs = (
        P(None, None, "gx", "gy"),
        P(None, "gx", "gy"),
        P(("gx", "gy"), None, None),
        P(("gx", "gy"), None),
        P(None, None, "gx", "gy"),
        P(None, None, "gx", "gy"),
        P(None, "gx", "gy"),
        P(None, "gx", "gy"),
    )
    out_specs = (P(None, None, "gx", "gy"), P(None, None, "gx", "gy"))
    return jax.shard_map(
        per_device, mesh=mesh, in_specs=in_specs, out_specs=out_specs, check_vma=False
    )
```

```python
import math

import jax
import jax.numpy as jnp
import numpy as np
from jax import lax
from jax.experimental import pallas as pl
from jax.sharding import PartitionSpec as P

SUB = 2
OSTEPS = 2


visc_coef = 0.01
diff_coef = 0.2
wind_coef = 0.1
surf_coef = 0.2


def extended(cells, sides, width):
    for axis, dim in sides:
        count = lax.axis_size(axis)
        head = lax.slice_in_dim(cells, 0, width, axis=dim)
        tail = lax.slice_in_dim(cells, cells.shape[dim] - width, cells.shape[dim], axis=dim)
        cells = jnp.concatenate(
            [
                lax.ppermute(tail, axis, [(i, (i + 1) % count) for i in range(count)]),
                cells,
                lax.ppermute(head, axis, [((i + 1) % count, i) for i in range(count)]),
            ],
            axis=dim,
        )
    return cells


def gll_tables():
    points = np.array([-1.0, -1.0 / np.sqrt(5.0), 1.0 / np.sqrt(5.0), 1.0])
    weights = np.array([1.0 / 6.0, 5.0 / 6.0, 5.0 / 6.0, 1.0 / 6.0])
    derivative = np.zeros((4, 4))
    for target in range(4):
        for source in range(4):
            if target == source:
                derivative[target, source] = np.sum(
                    [
                        1.0 / (points[source] - points[others])
                        for others in range(4)
                        if others != source
                    ]
                )
            else:
                numer = np.prod(
                    [
                        points[target] - points[others]
                        for others in range(4)
                        if others != target and others != source
                    ]
                )
                denom = np.prod(
                    [points[source] - points[others] for others in range(4) if others != source]
                )
                derivative[target, source] = numer / denom
    massw = np.array([1.0 / 3.0, 5.0 / 6.0, 5.0 / 6.0, 1.0 / 3.0])
    return (derivative, weights, massw)


def stiffness(state_in, metric_x, metric_y, derivative_np, weights_np):
    levels, xsize, ysize = state_in.shape
    highest = lax.Precision.HIGHEST
    block_x = jnp.asarray(np.kron(np.eye(xsize // 4), derivative_np), jnp.float32)
    block_y = jnp.asarray(np.kron(np.eye(ysize // 4), derivative_np), jnp.float32)
    weight_x = jnp.asarray(np.tile(weights_np, xsize // 4), jnp.float32)[:, None]
    weight_y = jnp.asarray(np.tile(weights_np, ysize // 4), jnp.float32)[None, :]
    along_x = jnp.einsum("ab,lby->lay", block_x, state_in, precision=highest)
    term_x = (
        jnp.einsum("ba,lby->lay", block_x, weight_x * metric_x * along_x, precision=highest)
        * weight_y
    )
    along_y = jnp.einsum("lxc,dc->lxd", state_in, block_y, precision=highest)
    term_y = (
        jnp.einsum("lxc,cd->lxd", weight_y * metric_y * along_y, block_y, precision=highest)
        * weight_x
    )
    return term_x + term_y


def mass_inverse(massw_np, xsize, ysize):
    return jnp.asarray(
        1.0 / (np.tile(massw_np, xsize // 4)[:, None] * np.tile(massw_np, ysize // 4)[None, :]),
        jnp.float32,
    )


def edge_sum(padded):
    inner_y = padded.shape[2] - 2
    ypos = jnp.arange(inner_y) % 4
    centre = padded[:, :, 1:-1]
    merged = centre + jnp.where(
        ypos == 0, padded[:, :, :-2], jnp.where(ypos == 3, padded[:, :, 2:], 0.0)
    )
    inner_x = merged.shape[1] - 2
    xpos = (jnp.arange(inner_x) % 4)[:, None]
    middle = merged[:, 1:-1]
    return middle + jnp.where(xpos == 0, merged[:, :-2], jnp.where(xpos == 3, merged[:, 2:], 0.0))


def tracer_step(padded, velocity):
    centre = padded[..., 1:-1, 1:-1]
    east = padded[..., 2:, 1:-1]
    west = padded[..., :-2, 1:-1]
    north = padded[..., 1:-1, 2:]
    south = padded[..., 1:-1, :-2]
    return (
        centre
        + diff_coef * (east + west + north + south - 4.0 * centre)
        - 0.5 * velocity[0] * (east - west)
        - 0.5 * velocity[1] * (north - south)
    )


def gather_kernel(index_ref, table_ref, out_ref):
    fields, rows, tile = table_ref.shape[0], table_ref.shape[1], out_ref.shape[1]
    index = index_ref[...]
    onehot = (lax.broadcasted_iota(jnp.int32, (128, tile), 0) == (index & 127)).astype(jnp.bfloat16)
    select = lax.broadcasted_iota(jnp.int32, (rows, tile), 0) == (index >> 7)
    for field in range(fields):
        rest = table_ref[field]
        whole = jnp.zeros((rows, tile), jnp.float32)
        for part in range(3):
            piece = rest.astype(jnp.bfloat16)
            rest = rest - piece.astype(jnp.float32)
            whole = whole + jnp.dot(piece, onehot, preferred_element_type=jnp.float32)
        out_ref[pl.ds(field, 1), :] = jnp.sum(jnp.where(select, whole, 0.0), axis=0, keepdims=True)


def onehot_gather(table, index):
    fields, total = table.shape
    rows = total // 128
    flat = index.reshape(1, -1)
    count = flat.shape[1]
    tile = math.gcd(count, 1024)
    return pl.pallas_call(
        gather_kernel,
        grid=(count // tile,),
        in_specs=[
            pl.BlockSpec((1, tile), lambda step: (0, step)),
            pl.BlockSpec((fields, rows, 128), lambda step: (0, 0, 0)),
        ],
        out_specs=pl.BlockSpec((fields, tile), lambda step: (0, step)),
        out_shape=jax.ShapeDtypeStruct((fields, count), jnp.float32),
    )(flat, table.reshape(fields, rows, 128))


def per_device(
    atm_state,
    metric,
    send_idx,
    send_counts,
    ocean_tracers,
    ocean_velocity,
    remap_slots,
    remap_weights,
):
    fields, levels, xlocal, ylocal = atm_state.shape
    derivative_np, weights_np, massw_np = gll_tables()
    state_now = atm_state.reshape(fields * levels, xlocal, ylocal)
    inv_mass = mass_inverse(massw_np, xlocal, ylocal)
    for substep in range(SUB):
        stiff = stiffness(state_now, metric[0], metric[1], derivative_np, weights_np)
        padded = extended(stiff, (("gx", 1), ("gy", 2)), 1)
        state_now = state_now - visc_coef * edge_sum(padded) * inv_mass
    atm_out = state_now.reshape(fields, levels, xlocal, ylocal)
    bottom = atm_out[:, levels - 1]
    speed = jnp.sqrt(1.0 + bottom[0] * bottom[0] + bottom[1] * bottom[1])
    flux_flat = (bottom * speed).reshape(fields, xlocal * ylocal)
    node_total = xlocal * ylocal
    rank_total = send_idx.shape[1]
    slot_cap = send_idx.shape[2]
    payload = onehot_gather(flux_flat, send_idx[0]).reshape(fields, rank_total, slot_cap)
    count_row = send_counts[0]
    live_slots = (jnp.arange(slot_cap)[None, :] < count_row[:, None]).astype(jnp.float32)
    payload = payload * live_slots[None]
    received = lax.all_to_all(payload, ("gx", "gy"), split_axis=1, concat_axis=1, tiled=True)
    received = received.reshape(fields, -1)
    source_count, ocean_x, ocean_y = remap_slots.shape
    gathered = onehot_gather(received, remap_slots).reshape(fields, source_count, ocean_x, ocean_y)
    ocean_flux = jnp.sum(remap_weights[None] * gathered, axis=1)
    velocity = ocean_velocity.at[0, 0].add(wind_coef * jnp.tanh(ocean_flux[0]))
    velocity = velocity.at[1, 0].add(wind_coef * jnp.tanh(ocean_flux[1]))
    tracers = ocean_tracers.at[0, 0].add(surf_coef * ocean_flux[2])
    tracers = tracers.at[1, 0].add(surf_coef * ocean_flux[3])
    for repeat in range(OSTEPS):
        ocean_pad = extended(tracers, (("gx", 2), ("gy", 3)), 1)
        tracers = tracer_step(ocean_pad, velocity)
    return (atm_out, tracers)


def solution(mesh):
    in_specs = (
        P(None, None, "gx", "gy"),
        P(None, "gx", "gy"),
        P(("gx", "gy"), None, None),
        P(("gx", "gy"), None),
        P(None, None, "gx", "gy"),
        P(None, None, "gx", "gy"),
        P(None, "gx", "gy"),
        P(None, "gx", "gy"),
    )
    out_specs = (P(None, None, "gx", "gy"), P(None, None, "gx", "gy"))
    return jax.shard_map(
        per_device, mesh=mesh, in_specs=in_specs, out_specs=out_specs, check_vma=False
    )
```

```python
import math

import jax
import jax.numpy as jnp
import numpy as np
from jax import lax
from jax.experimental import pallas as pl
from jax.sharding import PartitionSpec as P

SUB = 2
OSTEPS = 2


visc_coef = 0.01
diff_coef = 0.2
wind_coef = 0.1
surf_coef = 0.2


def neighbour(values, step_x, step_y):
    count_x, count_y = lax.axis_size("gx"), lax.axis_size("gy")
    if step_y == 0:
        return lax.ppermute(values, "gx", [(i, (i + step_x) % count_x) for i in range(count_x)])
    if step_x == 0:
        return lax.ppermute(values, "gy", [(j, (j + step_y) % count_y) for j in range(count_y)])
    pairs = [
        (i * count_y + j, ((i + step_x) % count_x) * count_y + (j + step_y) % count_y)
        for i in range(count_x)
        for j in range(count_y)
    ]
    return lax.ppermute(values, ("gx", "gy"), pairs)


def shifted(values, before, after, axis):
    size = values.shape[axis]
    prev = jnp.concatenate([before, lax.slice_in_dim(values, 0, size - 1, axis=axis)], axis=axis)
    nxt = jnp.concatenate([lax.slice_in_dim(values, 1, size, axis=axis), after], axis=axis)
    return prev, nxt


def pair_merge(values, before, after, axis):
    size = values.shape[axis]
    layout = [1] * values.ndim
    layout[axis] = size
    position = (jnp.arange(size) % 4).reshape(layout)
    prev, nxt = shifted(values, before, after, axis)
    return values + jnp.where(position == 0, prev, jnp.where(position == 3, nxt, 0.0))


def assemble(stiff):
    last_x, last_y = stiff.shape[1] - 1, stiff.shape[2] - 1
    from_left = neighbour(stiff[:, :, last_y:], 0, 1)
    from_right = neighbour(stiff[:, :, :1], 0, -1)
    from_up = neighbour(stiff[:, last_x:, :], 1, 0)
    from_down = neighbour(stiff[:, :1, :], -1, 0)
    up_left = neighbour(stiff[:, last_x:, last_y:], 1, 1)
    up_right = neighbour(stiff[:, last_x:, :1], 1, -1)
    down_left = neighbour(stiff[:, :1, last_y:], -1, 1)
    down_right = neighbour(stiff[:, :1, :1], -1, -1)
    merged = pair_merge(stiff, from_left, from_right, 2)
    merged_up = pair_merge(from_up, up_left, up_right, 2)
    merged_down = pair_merge(from_down, down_left, down_right, 2)
    return pair_merge(merged, merged_up, merged_down, 1)


def stiff_kernel(state_ref, wmx_ref, wmy_ref, wx_ref, wy_ref, kx_ref, ay_ref, by_ref, out_ref):
    highest = lax.Precision.HIGHEST
    chunk = kx_ref.shape[0]
    kx = kx_ref[...]
    for part in range(state_ref.shape[0] // chunk):
        rows = pl.ds(part * chunk, chunk)
        block = state_ref[rows, :]
        along_x = jnp.dot(kx, block, precision=highest, preferred_element_type=jnp.float32)
        term_x = lax.dot_general(
            kx,
            wmx_ref[...] * along_x,
            (((0,), (0,)), ((), ())),
            precision=highest,
            preferred_element_type=jnp.float32,
        )
        along_y = jnp.dot(block, ay_ref[...], precision=highest, preferred_element_type=jnp.float32)
        term_y = jnp.dot(wmy_ref[...] * along_y, by_ref[...], precision=highest, preferred_element_type=jnp.float32)
        out_ref[rows, :] = term_x * wy_ref[...] + term_y * wx_ref[...]


def stiffness(state_in, metric, derivative_np, weights_np):
    levels, xsize, ysize = state_in.shape
    chunk = 128 if 128 % xsize == 0 else xsize
    total = levels * xsize
    tile = chunk * math.gcd(total // chunk, 5)
    weight_x = np.tile(weights_np, xsize // 4)[:, None]
    weight_y = np.tile(weights_np, ysize // 4)[None, :]
    reps = chunk // xsize
    wmx = jnp.tile(jnp.asarray(weight_x, jnp.float32) * metric[0], (reps, 1))
    wmy = jnp.tile(jnp.asarray(weight_y, jnp.float32) * metric[1], (reps, 1))
    wx = jnp.asarray(np.tile(np.broadcast_to(weight_x, (xsize, ysize)), (reps, 1)), jnp.float32)
    wy = jnp.asarray(np.tile(np.broadcast_to(weight_y, (xsize, ysize)), (reps, 1)), jnp.float32)
    kx = jnp.asarray(np.kron(np.eye(chunk // 4), derivative_np), jnp.float32)
    ay = jnp.asarray(np.kron(np.eye(ysize // 4), derivative_np.T), jnp.float32)
    by = jnp.asarray(np.kron(np.eye(ysize // 4), derivative_np), jnp.float32)
    fixed = lambda step: (0, 0)
    out = pl.pallas_call(
        stiff_kernel,
        grid=(total // tile,),
        in_specs=[pl.BlockSpec((tile, ysize), lambda step: (step, 0))]
        + [pl.BlockSpec((chunk, ysize), fixed)] * 4
        + [pl.BlockSpec((chunk, chunk), fixed), pl.BlockSpec((ysize, ysize), fixed), pl.BlockSpec((ysize, ysize), fixed)],
        out_specs=pl.BlockSpec((tile, ysize), lambda step: (step, 0)),
        out_shape=jax.ShapeDtypeStruct((total, ysize), jnp.float32),
    )(state_in.reshape(total, ysize), wmx, wmy, wx, wy, kx, ay, by)
    return out.reshape(levels, xsize, ysize)


def tracer_step(tracers, velocity):
    last_x, last_y = tracers.shape[-2] - 1, tracers.shape[-1] - 1
    from_up = neighbour(tracers[..., last_x:, :], 1, 0)
    from_down = neighbour(tracers[..., :1, :], -1, 0)
    from_left = neighbour(tracers[..., last_y:], 0, 1)
    from_right = neighbour(tracers[..., :1], 0, -1)
    west, east = shifted(tracers, from_up, from_down, tracers.ndim - 2)
    south, north = shifted(tracers, from_left, from_right, tracers.ndim - 1)
    return (
        tracers
        + diff_coef * (east + west + north + south - 4.0 * tracers)
        - 0.5 * velocity[0] * (east - west)
        - 0.5 * velocity[1] * (north - south)
    )


def gll_tables():
    points = np.array([-1.0, -1.0 / np.sqrt(5.0), 1.0 / np.sqrt(5.0), 1.0])
    weights = np.array([1.0 / 6.0, 5.0 / 6.0, 5.0 / 6.0, 1.0 / 6.0])
    derivative = np.zeros((4, 4))
    for target in range(4):
        for source in range(4):
            if target == source:
                derivative[target, source] = np.sum(
                    [
                        1.0 / (points[source] - points[others])
                        for others in range(4)
                        if others != source
                    ]
                )
            else:
                numer = np.prod(
                    [
                        points[target] - points[others]
                        for others in range(4)
                        if others != target and others != source
                    ]
                )
                denom = np.prod(
                    [points[source] - points[others] for others in range(4) if others != source]
                )
                derivative[target, source] = numer / denom
    massw = np.array([1.0 / 3.0, 5.0 / 6.0, 5.0 / 6.0, 1.0 / 3.0])
    return (derivative, weights, massw)


def mass_inverse(massw_np, xsize, ysize):
    return jnp.asarray(
        1.0 / (np.tile(massw_np, xsize // 4)[:, None] * np.tile(massw_np, ysize // 4)[None, :]),
        jnp.float32,
    )


def gather_kernel(index_ref, table_ref, out_ref):
    fields, rows, tile = table_ref.shape[0], table_ref.shape[1], out_ref.shape[1]
    index = index_ref[...]
    onehot = (lax.broadcasted_iota(jnp.int32, (128, tile), 0) == (index & 127)).astype(jnp.bfloat16)
    select = lax.broadcasted_iota(jnp.int32, (rows, tile), 0) == (index >> 7)
    for field in range(fields):
        rest = table_ref[field]
        whole = jnp.zeros((rows, tile), jnp.float32)
        for part in range(3):
            piece = rest.astype(jnp.bfloat16)
            rest = rest - piece.astype(jnp.float32)
            whole = whole + jnp.dot(piece, onehot, preferred_element_type=jnp.float32)
        out_ref[pl.ds(field, 1), :] = jnp.sum(jnp.where(select, whole, 0.0), axis=0, keepdims=True)


def onehot_gather(table, index):
    fields, total = table.shape
    rows = total // 128
    flat = index.reshape(1, -1)
    count = flat.shape[1]
    tile = math.gcd(count, 1024)
    return pl.pallas_call(
        gather_kernel,
        grid=(count // tile,),
        in_specs=[
            pl.BlockSpec((1, tile), lambda step: (0, step)),
            pl.BlockSpec((fields, rows, 128), lambda step: (0, 0, 0)),
        ],
        out_specs=pl.BlockSpec((fields, tile), lambda step: (0, step)),
        out_shape=jax.ShapeDtypeStruct((fields, count), jnp.float32),
    )(flat, table.reshape(fields, rows, 128))


def per_device(
    atm_state,
    metric,
    send_idx,
    send_counts,
    ocean_tracers,
    ocean_velocity,
    remap_slots,
    remap_weights,
):
    fields, levels, xlocal, ylocal = atm_state.shape
    derivative_np, weights_np, massw_np = gll_tables()
    state_now = atm_state.reshape(fields * levels, xlocal, ylocal)
    inv_mass = mass_inverse(massw_np, xlocal, ylocal)
    for substep in range(SUB):
        stiff = stiffness(state_now, metric, derivative_np, weights_np)
        state_now = state_now - visc_coef * assemble(stiff) * inv_mass
    atm_out = state_now.reshape(fields, levels, xlocal, ylocal)
    bottom = atm_out[:, levels - 1]
    speed = jnp.sqrt(1.0 + bottom[0] * bottom[0] + bottom[1] * bottom[1])
    flux_flat = (bottom * speed).reshape(fields, xlocal * ylocal)
    node_total = xlocal * ylocal
    rank_total = send_idx.shape[1]
    slot_cap = send_idx.shape[2]
    payload = onehot_gather(flux_flat, send_idx[0]).reshape(fields, rank_total, slot_cap)
    count_row = send_counts[0]
    live_slots = (jnp.arange(slot_cap)[None, :] < count_row[:, None]).astype(jnp.float32)
    payload = payload * live_slots[None]
    received = lax.all_to_all(payload, ("gx", "gy"), split_axis=1, concat_axis=1, tiled=True)
    received = received.reshape(fields, -1)
    source_count, ocean_x, ocean_y = remap_slots.shape
    gathered = onehot_gather(received, remap_slots).reshape(fields, source_count, ocean_x, ocean_y)
    ocean_flux = jnp.sum(remap_weights[None] * gathered, axis=1)
    velocity = ocean_velocity.at[0, 0].add(wind_coef * jnp.tanh(ocean_flux[0]))
    velocity = velocity.at[1, 0].add(wind_coef * jnp.tanh(ocean_flux[1]))
    tracers = ocean_tracers.at[0, 0].add(surf_coef * ocean_flux[2])
    tracers = tracers.at[1, 0].add(surf_coef * ocean_flux[3])
    for repeat in range(OSTEPS):
        tracers = tracer_step(tracers, velocity)
    return (atm_out, tracers)


def solution(mesh):
    in_specs = (
        P(None, None, "gx", "gy"),
        P(None, "gx", "gy"),
        P(("gx", "gy"), None, None),
        P(("gx", "gy"), None),
        P(None, None, "gx", "gy"),
        P(None, None, "gx", "gy"),
        P(None, "gx", "gy"),
        P(None, "gx", "gy"),
    )
    out_specs = (P(None, None, "gx", "gy"), P(None, None, "gx", "gy"))
    return jax.shard_map(
        per_device, mesh=mesh, in_specs=in_specs, out_specs=out_specs, check_vma=False
    )
```

```python
import math

import jax
import jax.numpy as jnp
import numpy as np
from jax import lax
from jax.experimental import pallas as pl
from jax.sharding import PartitionSpec as P

SUB = 2
OSTEPS = 2


visc_coef = 0.01
diff_coef = 0.2
wind_coef = 0.1
surf_coef = 0.2


def neighbour(values, step_x, step_y):
    count_x, count_y = lax.axis_size("gx"), lax.axis_size("gy")
    if step_y == 0:
        return lax.ppermute(values, "gx", [(i, (i + step_x) % count_x) for i in range(count_x)])
    if step_x == 0:
        return lax.ppermute(values, "gy", [(j, (j + step_y) % count_y) for j in range(count_y)])
    pairs = [
        (i * count_y + j, ((i + step_x) % count_x) * count_y + (j + step_y) % count_y)
        for i in range(count_x)
        for j in range(count_y)
    ]
    return lax.ppermute(values, ("gx", "gy"), pairs)


def shifted(values, before, after, axis):
    size = values.shape[axis]
    prev = jnp.concatenate([before, lax.slice_in_dim(values, 0, size - 1, axis=axis)], axis=axis)
    nxt = jnp.concatenate([lax.slice_in_dim(values, 1, size, axis=axis), after], axis=axis)
    return prev, nxt


def pair_merge(values, before, after, axis):
    size = values.shape[axis]
    layout = [1] * values.ndim
    layout[axis] = size
    position = (jnp.arange(size) % 4).reshape(layout)
    prev, nxt = shifted(values, before, after, axis)
    return values + jnp.where(position == 0, prev, jnp.where(position == 3, nxt, 0.0))


def packed(values):
    if values.size % 128:
        return values
    return values.reshape(-1, 128)


def exchange(values, step_x, step_y):
    return neighbour(packed(values), step_x, step_y).reshape(values.shape)


def assemble(stiff):
    last_x, last_y = stiff.shape[1] - 1, stiff.shape[2] - 1
    from_left = exchange(stiff[:, :, last_y], 0, 1)[..., None]
    from_right = exchange(stiff[:, :, 0], 0, -1)[..., None]
    merged = pair_merge(stiff, from_left, from_right, 2)
    from_up = exchange(merged[:, last_x, :], 1, 0)[:, None, :]
    from_down = exchange(merged[:, 0, :], -1, 0)[:, None, :]
    return pair_merge(merged, from_up, from_down, 1)


def stiffness(state_in, metric, derivative_np, weights_np):
    levels, xsize, ysize = state_in.shape
    highest = lax.Precision.HIGHEST
    block_x = jnp.asarray(np.kron(np.eye(xsize // 4), derivative_np), jnp.float32)
    block_y = jnp.asarray(np.kron(np.eye(ysize // 4), derivative_np), jnp.float32)
    weight_x = jnp.asarray(np.tile(weights_np, xsize // 4), jnp.float32)[:, None]
    weight_y = jnp.asarray(np.tile(weights_np, ysize // 4), jnp.float32)[None, :]
    along_x = jnp.einsum("ab,lby->lay", block_x, state_in, precision=highest)
    term_x = (
        jnp.einsum("ba,lby->lay", block_x, weight_x * metric[0] * along_x, precision=highest)
        * weight_y
    )
    along_y = jnp.einsum("lxc,dc->lxd", state_in, block_y, precision=highest)
    term_y = (
        jnp.einsum("lxc,cd->lxd", weight_y * metric[1] * along_y, block_y, precision=highest)
        * weight_x
    )
    return term_x + term_y


def tracer_step(tracers, velocity):
    last_x, last_y = tracers.shape[-2] - 1, tracers.shape[-1] - 1
    from_up = exchange(tracers[..., last_x, :], 1, 0)[..., None, :]
    from_down = exchange(tracers[..., 0, :], -1, 0)[..., None, :]
    from_left = exchange(tracers[..., last_y], 0, 1)[..., None]
    from_right = exchange(tracers[..., 0], 0, -1)[..., None]
    west, east = shifted(tracers, from_up, from_down, tracers.ndim - 2)
    south, north = shifted(tracers, from_left, from_right, tracers.ndim - 1)
    return (
        tracers
        + diff_coef * (east + west + north + south - 4.0 * tracers)
        - 0.5 * velocity[0] * (east - west)
        - 0.5 * velocity[1] * (north - south)
    )


def gll_tables():
    points = np.array([-1.0, -1.0 / np.sqrt(5.0), 1.0 / np.sqrt(5.0), 1.0])
    weights = np.array([1.0 / 6.0, 5.0 / 6.0, 5.0 / 6.0, 1.0 / 6.0])
    derivative = np.zeros((4, 4))
    for target in range(4):
        for source in range(4):
            if target == source:
                derivative[target, source] = np.sum(
                    [
                        1.0 / (points[source] - points[others])
                        for others in range(4)
                        if others != source
                    ]
                )
            else:
                numer = np.prod(
                    [
                        points[target] - points[others]
                        for others in range(4)
                        if others != target and others != source
                    ]
                )
                denom = np.prod(
                    [points[source] - points[others] for others in range(4) if others != source]
                )
                derivative[target, source] = numer / denom
    massw = np.array([1.0 / 3.0, 5.0 / 6.0, 5.0 / 6.0, 1.0 / 3.0])
    return (derivative, weights, massw)


def mass_inverse(massw_np, xsize, ysize):
    return jnp.asarray(
        1.0 / (np.tile(massw_np, xsize // 4)[:, None] * np.tile(massw_np, ysize // 4)[None, :]),
        jnp.float32,
    )


def gather_kernel(index_ref, table_ref, out_ref):
    fields, rows, tile = table_ref.shape[0], table_ref.shape[1], out_ref.shape[1]
    index = index_ref[...]
    onehot = (lax.broadcasted_iota(jnp.int32, (128, tile), 0) == (index & 127)).astype(jnp.bfloat16)
    select = lax.broadcasted_iota(jnp.int32, (rows, tile), 0) == (index >> 7)
    for field in range(fields):
        rest = table_ref[field]
        whole = jnp.zeros((rows, tile), jnp.float32)
        for part in range(3):
            piece = rest.astype(jnp.bfloat16)
            rest = rest - piece.astype(jnp.float32)
            whole = whole + jnp.dot(piece, onehot, preferred_element_type=jnp.float32)
        out_ref[pl.ds(field, 1), :] = jnp.sum(jnp.where(select, whole, 0.0), axis=0, keepdims=True)


def onehot_gather(table, index):
    fields, total = table.shape
    rows = total // 128
    flat = index.reshape(1, -1)
    count = flat.shape[1]
    tile = math.gcd(count, 1024)
    return pl.pallas_call(
        gather_kernel,
        grid=(count // tile,),
        in_specs=[
            pl.BlockSpec((1, tile), lambda step: (0, step)),
            pl.BlockSpec((fields, rows, 128), lambda step: (0, 0, 0)),
        ],
        out_specs=pl.BlockSpec((fields, tile), lambda step: (0, step)),
        out_shape=jax.ShapeDtypeStruct((fields, count), jnp.float32),
    )(flat, table.reshape(fields, rows, 128))


def per_device(
    atm_state,
    metric,
    send_idx,
    send_counts,
    ocean_tracers,
    ocean_velocity,
    remap_slots,
    remap_weights,
):
    fields, levels, xlocal, ylocal = atm_state.shape
    derivative_np, weights_np, massw_np = gll_tables()
    state_now = atm_state.reshape(fields * levels, xlocal, ylocal)
    inv_mass = mass_inverse(massw_np, xlocal, ylocal)
    for substep in range(SUB):
        stiff = stiffness(state_now, metric, derivative_np, weights_np)
        state_now = state_now - visc_coef * assemble(stiff) * inv_mass
    atm_out = state_now.reshape(fields, levels, xlocal, ylocal)
    bottom = atm_out[:, levels - 1]
    speed = jnp.sqrt(1.0 + bottom[0] * bottom[0] + bottom[1] * bottom[1])
    flux_flat = (bottom * speed).reshape(fields, xlocal * ylocal)
    node_total = xlocal * ylocal
    rank_total = send_idx.shape[1]
    slot_cap = send_idx.shape[2]
    payload = onehot_gather(flux_flat, send_idx[0]).reshape(fields, rank_total, slot_cap)
    count_row = send_counts[0]
    live_slots = (jnp.arange(slot_cap)[None, :] < count_row[:, None]).astype(jnp.float32)
    payload = payload * live_slots[None]
    received = lax.all_to_all(payload, ("gx", "gy"), split_axis=1, concat_axis=1, tiled=True)
    received = received.reshape(fields, -1)
    source_count, ocean_x, ocean_y = remap_slots.shape
    gathered = onehot_gather(received, remap_slots).reshape(fields, source_count, ocean_x, ocean_y)
    ocean_flux = jnp.sum(remap_weights[None] * gathered, axis=1)
    velocity = ocean_velocity.at[0, 0].add(wind_coef * jnp.tanh(ocean_flux[0]))
    velocity = velocity.at[1, 0].add(wind_coef * jnp.tanh(ocean_flux[1]))
    tracers = ocean_tracers.at[0, 0].add(surf_coef * ocean_flux[2])
    tracers = tracers.at[1, 0].add(surf_coef * ocean_flux[3])
    for repeat in range(OSTEPS):
        tracers = tracer_step(tracers, velocity)
    return (atm_out, tracers)


def solution(mesh):
    in_specs = (
        P(None, None, "gx", "gy"),
        P(None, "gx", "gy"),
        P(("gx", "gy"), None, None),
        P(("gx", "gy"), None),
        P(None, None, "gx", "gy"),
        P(None, None, "gx", "gy"),
        P(None, "gx", "gy"),
        P(None, "gx", "gy"),
    )
    out_specs = (P(None, None, "gx", "gy"), P(None, None, "gx", "gy"))
    return jax.shard_map(
        per_device, mesh=mesh, in_specs=in_specs, out_specs=out_specs, check_vma=False
    )
```

```python
import math

import jax
import jax.numpy as jnp
import numpy as np
from jax import lax
from jax.experimental import pallas as pl
from jax.sharding import PartitionSpec as P

SUB = 2
OSTEPS = 2


visc_coef = 0.01
diff_coef = 0.2
wind_coef = 0.1
surf_coef = 0.2


def neighbour(values, step_x, step_y):
    count_x, count_y = lax.axis_size("gx"), lax.axis_size("gy")
    if step_y == 0:
        return lax.ppermute(values, "gx", [(i, (i + step_x) % count_x) for i in range(count_x)])
    if step_x == 0:
        return lax.ppermute(values, "gy", [(j, (j + step_y) % count_y) for j in range(count_y)])
    pairs = [
        (i * count_y + j, ((i + step_x) % count_x) * count_y + (j + step_y) % count_y)
        for i in range(count_x)
        for j in range(count_y)
    ]
    return lax.ppermute(values, ("gx", "gy"), pairs)


def shifted(values, before, after, axis):
    size = values.shape[axis]
    prev = jnp.concatenate([before, lax.slice_in_dim(values, 0, size - 1, axis=axis)], axis=axis)
    nxt = jnp.concatenate([lax.slice_in_dim(values, 1, size, axis=axis), after], axis=axis)
    return prev, nxt


def pair_merge(values, before, after, axis):
    size = values.shape[axis]
    layout = [1] * values.ndim
    layout[axis] = size
    position = (jnp.arange(size) % 4).reshape(layout)
    prev, nxt = shifted(values, before, after, axis)
    return values + jnp.where(position == 0, prev, jnp.where(position == 3, nxt, 0.0))


def packed(values):
    if values.size % 128:
        return values
    return values.reshape(-1, 128)


def exchange(values, step_x, step_y):
    return neighbour(packed(values), step_x, step_y).reshape(values.shape)


def assemble(stiff):
    last_x, last_y = stiff.shape[1] - 1, stiff.shape[2] - 1
    from_left = exchange(stiff[:, :, last_y], 0, 1)[..., None]
    from_right = exchange(stiff[:, :, 0], 0, -1)[..., None]
    merged = pair_merge(stiff, from_left, from_right, 2)
    from_up = exchange(merged[:, last_x, :], 1, 0)[:, None, :]
    from_down = exchange(merged[:, 0, :], -1, 0)[:, None, :]
    return pair_merge(merged, from_up, from_down, 1)


def stiffness(state_in, metric, derivative_np, weights_np):
    levels, xsize, ysize = state_in.shape
    highest = lax.Precision.HIGHEST
    block_x = jnp.asarray(np.kron(np.eye(xsize // 4), derivative_np), jnp.float32)
    block_y = jnp.asarray(np.kron(np.eye(ysize // 4), derivative_np), jnp.float32)
    weight_x = jnp.asarray(np.tile(weights_np, xsize // 4), jnp.float32)[:, None]
    weight_y = jnp.asarray(np.tile(weights_np, ysize // 4), jnp.float32)[None, :]
    along_x = jnp.einsum("ab,lby->lay", block_x, state_in, precision=highest)
    term_x = (
        jnp.einsum("ba,lby->lay", block_x, weight_x * metric[0] * along_x, precision=highest)
        * weight_y
    )
    along_y = jnp.einsum("lxc,dc->lxd", state_in, block_y, precision=highest)
    term_y = (
        jnp.einsum("lxc,cd->lxd", weight_y * metric[1] * along_y, block_y, precision=highest)
        * weight_x
    )
    return term_x + term_y


def tracer_step(tracers, velocity):
    last_x, last_y = tracers.shape[-2] - 1, tracers.shape[-1] - 1
    from_up = exchange(tracers[..., last_x, :], 1, 0)[..., None, :]
    from_down = exchange(tracers[..., 0, :], -1, 0)[..., None, :]
    from_left = exchange(tracers[..., last_y], 0, 1)[..., None]
    from_right = exchange(tracers[..., 0], 0, -1)[..., None]
    west, east = shifted(tracers, from_up, from_down, tracers.ndim - 2)
    south, north = shifted(tracers, from_left, from_right, tracers.ndim - 1)
    return (
        tracers
        + diff_coef * (east + west + north + south - 4.0 * tracers)
        - 0.5 * velocity[0] * (east - west)
        - 0.5 * velocity[1] * (north - south)
    )


def gll_tables():
    points = np.array([-1.0, -1.0 / np.sqrt(5.0), 1.0 / np.sqrt(5.0), 1.0])
    weights = np.array([1.0 / 6.0, 5.0 / 6.0, 5.0 / 6.0, 1.0 / 6.0])
    derivative = np.zeros((4, 4))
    for target in range(4):
        for source in range(4):
            if target == source:
                derivative[target, source] = np.sum(
                    [
                        1.0 / (points[source] - points[others])
                        for others in range(4)
                        if others != source
                    ]
                )
            else:
                numer = np.prod(
                    [
                        points[target] - points[others]
                        for others in range(4)
                        if others != target and others != source
                    ]
                )
                denom = np.prod(
                    [points[source] - points[others] for others in range(4) if others != source]
                )
                derivative[target, source] = numer / denom
    massw = np.array([1.0 / 3.0, 5.0 / 6.0, 5.0 / 6.0, 1.0 / 3.0])
    return (derivative, weights, massw)


def mass_inverse(massw_np, xsize, ysize):
    return jnp.asarray(
        1.0 / (np.tile(massw_np, xsize // 4)[:, None] * np.tile(massw_np, ysize // 4)[None, :]),
        jnp.float32,
    )


def gather_kernel(index_ref, table_ref, out_ref):
    fields, rows, tile = table_ref.shape[0], table_ref.shape[1], out_ref.shape[1]
    index = index_ref[...]
    onehot = (lax.broadcasted_iota(jnp.int32, (128, tile), 0) == (index & 127)).astype(jnp.bfloat16)
    select = lax.broadcasted_iota(jnp.int32, (rows, tile), 0) == (index >> 7)
    for field in range(fields):
        rest = table_ref[field]
        whole = jnp.zeros((rows, tile), jnp.float32)
        for part in range(3):
            piece = rest.astype(jnp.bfloat16)
            rest = rest - piece.astype(jnp.float32)
            whole = whole + jnp.dot(piece, onehot, preferred_element_type=jnp.float32)
        out_ref[pl.ds(field, 1), :] = jnp.sum(jnp.where(select, whole, 0.0), axis=0, keepdims=True)


def onehot_gather(table, index):
    fields, total = table.shape
    rows = total // 128
    flat = index.reshape(1, -1)
    count = flat.shape[1]
    tile = math.gcd(count, 1024)
    return pl.pallas_call(
        gather_kernel,
        grid=(count // tile,),
        in_specs=[
            pl.BlockSpec((1, tile), lambda step: (0, step)),
            pl.BlockSpec((fields, rows, 128), lambda step: (0, 0, 0)),
        ],
        out_specs=pl.BlockSpec((fields, tile), lambda step: (0, step)),
        out_shape=jax.ShapeDtypeStruct((fields, count), jnp.float32),
    )(flat, table.reshape(fields, rows, 128))


def per_device(
    atm_state,
    metric,
    send_idx,
    send_counts,
    ocean_tracers,
    ocean_velocity,
    remap_slots,
    remap_weights,
):
    fields, levels, xlocal, ylocal = atm_state.shape
    derivative_np, weights_np, massw_np = gll_tables()
    inv_mass = mass_inverse(massw_np, xlocal, ylocal)
    bottom = atm_state[:, levels - 1]
    upper = atm_state[:, : levels - 1].reshape(fields * (levels - 1), xlocal, ylocal)
    for substep in range(SUB):
        stiff = stiffness(bottom, metric, derivative_np, weights_np)
        bottom = bottom - visc_coef * assemble(stiff) * inv_mass
        stiff = stiffness(upper, metric, derivative_np, weights_np)
        upper = upper - visc_coef * assemble(stiff) * inv_mass
    atm_out = jnp.concatenate(
        [upper.reshape(fields, levels - 1, xlocal, ylocal), bottom[:, None]], axis=1
    )
    speed = jnp.sqrt(1.0 + bottom[0] * bottom[0] + bottom[1] * bottom[1])
    flux_flat = (bottom * speed).reshape(fields, xlocal * ylocal)
    node_total = xlocal * ylocal
    rank_total = send_idx.shape[1]
    slot_cap = send_idx.shape[2]
    payload = onehot_gather(flux_flat, send_idx[0]).reshape(fields, rank_total, slot_cap)
    count_row = send_counts[0]
    live_slots = (jnp.arange(slot_cap)[None, :] < count_row[:, None]).astype(jnp.float32)
    payload = payload * live_slots[None]
    received = lax.all_to_all(payload, ("gx", "gy"), split_axis=1, concat_axis=1, tiled=True)
    received = received.reshape(fields, -1)
    source_count, ocean_x, ocean_y = remap_slots.shape
    gathered = onehot_gather(received, remap_slots).reshape(fields, source_count, ocean_x, ocean_y)
    ocean_flux = jnp.sum(remap_weights[None] * gathered, axis=1)
    velocity = ocean_velocity[:, :1]
    velocity = velocity.at[0, 0].add(wind_coef * jnp.tanh(ocean_flux[0]))
    velocity = velocity.at[1, 0].add(wind_coef * jnp.tanh(ocean_flux[1]))
    surface = ocean_tracers[:, :1]
    surface = surface.at[0, 0].add(surf_coef * ocean_flux[2])
    surface = surface.at[1, 0].add(surf_coef * ocean_flux[3])
    deep = ocean_tracers[:, 1:]
    deep_velocity = ocean_velocity[:, 1:]
    for repeat in range(OSTEPS):
        deep = tracer_step(deep, deep_velocity)
        surface = tracer_step(surface, velocity)
    tracers = jnp.concatenate([surface, deep], axis=1)
    return (atm_out, tracers)


def solution(mesh):
    in_specs = (
        P(None, None, "gx", "gy"),
        P(None, "gx", "gy"),
        P(("gx", "gy"), None, None),
        P(("gx", "gy"), None),
        P(None, None, "gx", "gy"),
        P(None, None, "gx", "gy"),
        P(None, "gx", "gy"),
        P(None, "gx", "gy"),
    )
    out_specs = (P(None, None, "gx", "gy"), P(None, None, "gx", "gy"))
    return jax.shard_map(
        per_device, mesh=mesh, in_specs=in_specs, out_specs=out_specs, check_vma=False
    )
```

```python
import math

import jax
import jax.numpy as jnp
import numpy as np
from jax import lax
from jax.experimental import pallas as pl
from jax.sharding import PartitionSpec as P

SUB = 2
OSTEPS = 2


visc_coef = 0.01
diff_coef = 0.2
wind_coef = 0.1
surf_coef = 0.2


def neighbour(values, step_x, step_y):
    count_x, count_y = lax.axis_size("gx"), lax.axis_size("gy")
    if step_y == 0:
        return lax.ppermute(values, "gx", [(i, (i + step_x) % count_x) for i in range(count_x)])
    if step_x == 0:
        return lax.ppermute(values, "gy", [(j, (j + step_y) % count_y) for j in range(count_y)])
    pairs = [
        (i * count_y + j, ((i + step_x) % count_x) * count_y + (j + step_y) % count_y)
        for i in range(count_x)
        for j in range(count_y)
    ]
    return lax.ppermute(values, ("gx", "gy"), pairs)


def shifted(values, before, after, axis):
    size = values.shape[axis]
    prev = jnp.concatenate([before, lax.slice_in_dim(values, 0, size - 1, axis=axis)], axis=axis)
    nxt = jnp.concatenate([lax.slice_in_dim(values, 1, size, axis=axis), after], axis=axis)
    return prev, nxt


def pair_merge(values, before, after, axis):
    size = values.shape[axis]
    layout = [1] * values.ndim
    layout[axis] = size
    position = (jnp.arange(size) % 4).reshape(layout)
    prev, nxt = shifted(values, before, after, axis)
    return values + jnp.where(position == 0, prev, jnp.where(position == 3, nxt, 0.0))


def packed(values):
    if values.size % 128:
        return values
    return values.reshape(-1, 128)


def exchange(values, step_x, step_y):
    return neighbour(packed(values), step_x, step_y).reshape(values.shape)


def assemble(stiff):
    last_x, last_y = stiff.shape[1] - 1, stiff.shape[2] - 1
    from_left = exchange(stiff[:, :, last_y], 0, 1)[..., None]
    from_right = exchange(stiff[:, :, 0], 0, -1)[..., None]
    merged = pair_merge(stiff, from_left, from_right, 2)
    from_up = exchange(merged[:, last_x, :], 1, 0)[:, None, :]
    from_down = exchange(merged[:, 0, :], -1, 0)[:, None, :]
    return pair_merge(merged, from_up, from_down, 1)


def stiffness(state_in, metric, derivative_np, weights_np):
    levels, xsize, ysize = state_in.shape
    highest = lax.Precision.HIGHEST
    block_x = jnp.asarray(np.kron(np.eye(xsize // 4), derivative_np), jnp.float32)
    block_y = jnp.asarray(np.kron(np.eye(ysize // 4), derivative_np), jnp.float32)
    weight_x = jnp.asarray(np.tile(weights_np, xsize // 4), jnp.float32)[:, None]
    weight_y = jnp.asarray(np.tile(weights_np, ysize // 4), jnp.float32)[None, :]
    along_x = jnp.einsum("ab,lby->lay", block_x, state_in, precision=highest)
    term_x = (
        jnp.einsum("ba,lby->lay", block_x, weight_x * metric[0] * along_x, precision=highest)
        * weight_y
    )
    along_y = jnp.einsum("lxc,dc->lxd", state_in, block_y, precision=highest)
    term_y = (
        jnp.einsum("lxc,cd->lxd", weight_y * metric[1] * along_y, block_y, precision=highest)
        * weight_x
    )
    return term_x + term_y


def tracer_step(tracers, velocity):
    last_x, last_y = tracers.shape[-2] - 1, tracers.shape[-1] - 1
    from_up = exchange(tracers[..., last_x, :], 1, 0)[..., None, :]
    from_down = exchange(tracers[..., 0, :], -1, 0)[..., None, :]
    from_left = exchange(tracers[..., last_y], 0, 1)[..., None]
    from_right = exchange(tracers[..., 0], 0, -1)[..., None]
    west, east = shifted(tracers, from_up, from_down, tracers.ndim - 2)
    south, north = shifted(tracers, from_left, from_right, tracers.ndim - 1)
    return (
        tracers
        + diff_coef * (east + west + north + south - 4.0 * tracers)
        - 0.5 * velocity[0] * (east - west)
        - 0.5 * velocity[1] * (north - south)
    )


def gll_tables():
    points = np.array([-1.0, -1.0 / np.sqrt(5.0), 1.0 / np.sqrt(5.0), 1.0])
    weights = np.array([1.0 / 6.0, 5.0 / 6.0, 5.0 / 6.0, 1.0 / 6.0])
    derivative = np.zeros((4, 4))
    for target in range(4):
        for source in range(4):
            if target == source:
                derivative[target, source] = np.sum(
                    [
                        1.0 / (points[source] - points[others])
                        for others in range(4)
                        if others != source
                    ]
                )
            else:
                numer = np.prod(
                    [
                        points[target] - points[others]
                        for others in range(4)
                        if others != target and others != source
                    ]
                )
                denom = np.prod(
                    [points[source] - points[others] for others in range(4) if others != source]
                )
                derivative[target, source] = numer / denom
    massw = np.array([1.0 / 3.0, 5.0 / 6.0, 5.0 / 6.0, 1.0 / 3.0])
    return (derivative, weights, massw)


def mass_inverse(massw_np, xsize, ysize):
    return jnp.asarray(
        1.0 / (np.tile(massw_np, xsize // 4)[:, None] * np.tile(massw_np, ysize // 4)[None, :]),
        jnp.float32,
    )


def gather_kernel(index_ref, table_ref, out_ref):
    fields, rows, tile = table_ref.shape[0], table_ref.shape[1], out_ref.shape[1]
    index = index_ref[...]
    onehot = (lax.broadcasted_iota(jnp.int32, (128, tile), 0) == (index & 127)).astype(jnp.bfloat16)
    select = lax.broadcasted_iota(jnp.int32, (rows, tile), 0) == (index >> 7)
    for field in range(fields):
        rest = table_ref[field]
        whole = jnp.zeros((rows, tile), jnp.float32)
        for part in range(3):
            piece = rest.astype(jnp.bfloat16)
            rest = rest - piece.astype(jnp.float32)
            whole = whole + jnp.dot(piece, onehot, preferred_element_type=jnp.float32)
        out_ref[pl.ds(field, 1), :] = jnp.sum(jnp.where(select, whole, 0.0), axis=0, keepdims=True)


def onehot_gather(table, index):
    fields, total = table.shape
    rows = total // 128
    flat = index.reshape(1, -1)
    count = flat.shape[1]
    tile = math.gcd(count, 1024)
    return pl.pallas_call(
        gather_kernel,
        grid=(count // tile,),
        in_specs=[
            pl.BlockSpec((1, tile), lambda step: (0, step)),
            pl.BlockSpec((fields, rows, 128), lambda step: (0, 0, 0)),
        ],
        out_specs=pl.BlockSpec((fields, tile), lambda step: (0, step)),
        out_shape=jax.ShapeDtypeStruct((fields, count), jnp.float32),
    )(flat, table.reshape(fields, rows, 128))


def per_device(
    atm_state,
    metric,
    send_idx,
    send_counts,
    ocean_tracers,
    ocean_velocity,
    remap_slots,
    remap_weights,
):
    fields, levels, xlocal, ylocal = atm_state.shape
    derivative_np, weights_np, massw_np = gll_tables()
    state_now = atm_state.reshape(fields * levels, xlocal, ylocal)
    bottom = atm_state[:, levels - 1]
    inv_mass = mass_inverse(massw_np, xlocal, ylocal)
    for substep in range(SUB):
        stiff = stiffness(bottom, metric, derivative_np, weights_np)
        bottom = bottom - visc_coef * assemble(stiff) * inv_mass
        stiff = stiffness(state_now, metric, derivative_np, weights_np)
        state_now = state_now - visc_coef * assemble(stiff) * inv_mass
    atm_out = state_now.reshape(fields, levels, xlocal, ylocal)
    speed = jnp.sqrt(1.0 + bottom[0] * bottom[0] + bottom[1] * bottom[1])
    flux_flat = (bottom * speed).reshape(fields, xlocal * ylocal)
    node_total = xlocal * ylocal
    rank_total = send_idx.shape[1]
    slot_cap = send_idx.shape[2]
    payload = onehot_gather(flux_flat, send_idx[0]).reshape(fields, rank_total, slot_cap)
    count_row = send_counts[0]
    live_slots = (jnp.arange(slot_cap)[None, :] < count_row[:, None]).astype(jnp.float32)
    payload = payload * live_slots[None]
    received = lax.all_to_all(payload, ("gx", "gy"), split_axis=1, concat_axis=1, tiled=True)
    received = received.reshape(fields, -1)
    source_count, ocean_x, ocean_y = remap_slots.shape
    gathered = onehot_gather(received, remap_slots).reshape(fields, source_count, ocean_x, ocean_y)
    ocean_flux = jnp.sum(remap_weights[None] * gathered, axis=1)
    velocity = ocean_velocity[:, :1]
    velocity = velocity.at[0, 0].add(wind_coef * jnp.tanh(ocean_flux[0]))
    velocity = velocity.at[1, 0].add(wind_coef * jnp.tanh(ocean_flux[1]))
    surface = ocean_tracers[:, :1]
    surface = surface.at[0, 0].add(surf_coef * ocean_flux[2])
    surface = surface.at[1, 0].add(surf_coef * ocean_flux[3])
    tracers = ocean_tracers
    for repeat in range(OSTEPS):
        tracers = tracer_step(tracers, ocean_velocity)
        surface = tracer_step(surface, velocity)
    tracers = lax.dynamic_update_slice_in_dim(tracers, surface, 0, axis=1)
    return (atm_out, tracers)


def solution(mesh):
    in_specs = (
        P(None, None, "gx", "gy"),
        P(None, "gx", "gy"),
        P(("gx", "gy"), None, None),
        P(("gx", "gy"), None),
        P(None, None, "gx", "gy"),
        P(None, None, "gx", "gy"),
        P(None, "gx", "gy"),
        P(None, "gx", "gy"),
    )
    out_specs = (P(None, None, "gx", "gy"), P(None, None, "gx", "gy"))
    return jax.shard_map(
        per_device, mesh=mesh, in_specs=in_specs, out_specs=out_specs, check_vma=False
    )
```

```python
import math

import jax
import jax.numpy as jnp
import numpy as np
from jax import lax
from jax.experimental import pallas as pl
from jax.sharding import PartitionSpec as P

SUB = 2
OSTEPS = 2


visc_coef = 0.01
diff_coef = 0.2
wind_coef = 0.1
surf_coef = 0.2


def neighbour(values, step_x, step_y):
    count_x, count_y = lax.axis_size("gx"), lax.axis_size("gy")
    if step_y == 0:
        return lax.ppermute(values, "gx", [(i, (i + step_x) % count_x) for i in range(count_x)])
    if step_x == 0:
        return lax.ppermute(values, "gy", [(j, (j + step_y) % count_y) for j in range(count_y)])
    pairs = [
        (i * count_y + j, ((i + step_x) % count_x) * count_y + (j + step_y) % count_y)
        for i in range(count_x)
        for j in range(count_y)
    ]
    return lax.ppermute(values, ("gx", "gy"), pairs)


def shifted(values, before, after, axis):
    size = values.shape[axis]
    layout = [1] * values.ndim
    layout[axis] = size
    position = jnp.arange(size).reshape(layout)
    prev = jnp.concatenate([lax.slice_in_dim(values, 0, 1, axis=axis), lax.slice_in_dim(values, 0, size - 1, axis=axis)], axis=axis)
    nxt = jnp.concatenate([lax.slice_in_dim(values, 1, size, axis=axis), lax.slice_in_dim(values, size - 1, size, axis=axis)], axis=axis)
    prev = jnp.where(position == 0, jnp.broadcast_to(before, values.shape), prev)
    nxt = jnp.where(position == size - 1, jnp.broadcast_to(after, values.shape), nxt)
    return prev, nxt


def pair_merge(values, before, after, axis):
    size = values.shape[axis]
    layout = [1] * values.ndim
    layout[axis] = size
    position = (jnp.arange(size) % 4).reshape(layout)
    prev, nxt = shifted(values, before, after, axis)
    return values + jnp.where(position == 0, prev, jnp.where(position == 3, nxt, 0.0))


def packed(values):
    if values.size % 128:
        return values
    return values.reshape(-1, 128)


def exchange(values, step_x, step_y):
    return neighbour(packed(values), step_x, step_y).reshape(values.shape)


def assemble(stiff):
    last_x, last_y = stiff.shape[1] - 1, stiff.shape[2] - 1
    from_left = exchange(stiff[:, :, last_y], 0, 1)[:, :, None]
    from_right = exchange(stiff[:, :, 0], 0, -1)[:, :, None]
    merged = pair_merge(stiff, from_left, from_right, 2)
    from_up = exchange(merged[:, last_x, :], 1, 0)[:, None, :]
    from_down = exchange(merged[:, 0, :], -1, 0)[:, None, :]
    return pair_merge(merged, from_up, from_down, 1)


def stiffness(state_in, metric, derivative_np, weights_np):
    levels, xsize, ysize = state_in.shape
    highest = lax.Precision.HIGHEST
    block_x = jnp.asarray(np.kron(np.eye(xsize // 4), derivative_np), jnp.float32)
    block_y = jnp.asarray(np.kron(np.eye(ysize // 4), derivative_np), jnp.float32)
    weight_x = jnp.asarray(np.tile(weights_np, xsize // 4), jnp.float32)[:, None]
    weight_y = jnp.asarray(np.tile(weights_np, ysize // 4), jnp.float32)[None, :]
    along_x = jnp.einsum("ab,lby->lay", block_x, state_in, precision=highest)
    term_x = (
        jnp.einsum("ba,lby->lay", block_x, weight_x * metric[0] * along_x, precision=highest)
        * weight_y
    )
    along_y = jnp.einsum("lxc,dc->lxd", state_in, block_y, precision=highest)
    term_y = (
        jnp.einsum("lxc,cd->lxd", weight_y * metric[1] * along_y, block_y, precision=highest)
        * weight_x
    )
    return term_x + term_y


def tracer_step(tracers, velocity):
    last_x, last_y = tracers.shape[-2] - 1, tracers.shape[-1] - 1
    from_up = exchange(tracers[..., last_x, :], 1, 0)[..., None, :]
    from_down = exchange(tracers[..., 0, :], -1, 0)[..., None, :]
    from_left = exchange(tracers[..., last_y], 0, 1)[..., None]
    from_right = exchange(tracers[..., 0], 0, -1)[..., None]
    west, east = shifted(tracers, from_up, from_down, tracers.ndim - 2)
    south, north = shifted(tracers, from_left, from_right, tracers.ndim - 1)
    return (
        tracers
        + diff_coef * (east + west + north + south - 4.0 * tracers)
        - 0.5 * velocity[0] * (east - west)
        - 0.5 * velocity[1] * (north - south)
    )


def gll_tables():
    points = np.array([-1.0, -1.0 / np.sqrt(5.0), 1.0 / np.sqrt(5.0), 1.0])
    weights = np.array([1.0 / 6.0, 5.0 / 6.0, 5.0 / 6.0, 1.0 / 6.0])
    derivative = np.zeros((4, 4))
    for target in range(4):
        for source in range(4):
            if target == source:
                derivative[target, source] = np.sum(
                    [
                        1.0 / (points[source] - points[others])
                        for others in range(4)
                        if others != source
                    ]
                )
            else:
                numer = np.prod(
                    [
                        points[target] - points[others]
                        for others in range(4)
                        if others != target and others != source
                    ]
                )
                denom = np.prod(
                    [points[source] - points[others] for others in range(4) if others != source]
                )
                derivative[target, source] = numer / denom
    massw = np.array([1.0 / 3.0, 5.0 / 6.0, 5.0 / 6.0, 1.0 / 3.0])
    return (derivative, weights, massw)


def mass_inverse(massw_np, xsize, ysize):
    return jnp.asarray(
        1.0 / (np.tile(massw_np, xsize // 4)[:, None] * np.tile(massw_np, ysize // 4)[None, :]),
        jnp.float32,
    )


def gather_kernel(index_ref, table_ref, out_ref):
    fields, rows, tile = table_ref.shape[0], table_ref.shape[1], out_ref.shape[1]
    index = index_ref[...]
    onehot = (lax.broadcasted_iota(jnp.int32, (128, tile), 0) == (index & 127)).astype(jnp.bfloat16)
    select = lax.broadcasted_iota(jnp.int32, (rows, tile), 0) == (index >> 7)
    for field in range(fields):
        rest = table_ref[field]
        whole = jnp.zeros((rows, tile), jnp.float32)
        for part in range(3):
            piece = rest.astype(jnp.bfloat16)
            rest = rest - piece.astype(jnp.float32)
            whole = whole + jnp.dot(piece, onehot, preferred_element_type=jnp.float32)
        out_ref[pl.ds(field, 1), :] = jnp.sum(jnp.where(select, whole, 0.0), axis=0, keepdims=True)


def onehot_gather(table, index):
    fields, total = table.shape
    rows = total // 128
    flat = index.reshape(1, -1)
    count = flat.shape[1]
    tile = math.gcd(count, 1024)
    return pl.pallas_call(
        gather_kernel,
        grid=(count // tile,),
        in_specs=[
            pl.BlockSpec((1, tile), lambda step: (0, step)),
            pl.BlockSpec((fields, rows, 128), lambda step: (0, 0, 0)),
        ],
        out_specs=pl.BlockSpec((fields, tile), lambda step: (0, step)),
        out_shape=jax.ShapeDtypeStruct((fields, count), jnp.float32),
    )(flat, table.reshape(fields, rows, 128))


def per_device(
    atm_state,
    metric,
    send_idx,
    send_counts,
    ocean_tracers,
    ocean_velocity,
    remap_slots,
    remap_weights,
):
    fields, levels, xlocal, ylocal = atm_state.shape
    derivative_np, weights_np, massw_np = gll_tables()
    state_now = atm_state.reshape(fields * levels, xlocal, ylocal)
    inv_mass = mass_inverse(massw_np, xlocal, ylocal)
    for substep in range(SUB):
        stiff = stiffness(state_now, metric, derivative_np, weights_np)
        state_now = state_now - visc_coef * assemble(stiff) * inv_mass
    atm_out = state_now.reshape(fields, levels, xlocal, ylocal)
    bottom = atm_out[:, levels - 1]
    speed = jnp.sqrt(1.0 + bottom[0] * bottom[0] + bottom[1] * bottom[1])
    flux_flat = (bottom * speed).reshape(fields, xlocal * ylocal)
    node_total = xlocal * ylocal
    rank_total = send_idx.shape[1]
    slot_cap = send_idx.shape[2]
    payload = onehot_gather(flux_flat, send_idx[0]).reshape(fields, rank_total, slot_cap)
    count_row = send_counts[0]
    live_slots = (jnp.arange(slot_cap)[None, :] < count_row[:, None]).astype(jnp.float32)
    payload = payload * live_slots[None]
    received = lax.all_to_all(payload, ("gx", "gy"), split_axis=1, concat_axis=1, tiled=True)
    received = received.reshape(fields, -1)
    source_count, ocean_x, ocean_y = remap_slots.shape
    gathered = onehot_gather(received, remap_slots).reshape(fields, source_count, ocean_x, ocean_y)
    ocean_flux = jnp.sum(remap_weights[None] * gathered, axis=1)
    velocity = ocean_velocity.at[0, 0].add(wind_coef * jnp.tanh(ocean_flux[0]))
    velocity = velocity.at[1, 0].add(wind_coef * jnp.tanh(ocean_flux[1]))
    tracers = ocean_tracers.at[0, 0].add(surf_coef * ocean_flux[2])
    tracers = tracers.at[1, 0].add(surf_coef * ocean_flux[3])
    for repeat in range(OSTEPS):
        tracers = tracer_step(tracers, velocity)
    return (atm_out, tracers)


def solution(mesh):
    in_specs = (
        P(None, None, "gx", "gy"),
        P(None, "gx", "gy"),
        P(("gx", "gy"), None, None),
        P(("gx", "gy"), None),
        P(None, None, "gx", "gy"),
        P(None, None, "gx", "gy"),
        P(None, "gx", "gy"),
        P(None, "gx", "gy"),
    )
    out_specs = (P(None, None, "gx", "gy"), P(None, None, "gx", "gy"))
    return jax.shard_map(
        per_device, mesh=mesh, in_specs=in_specs, out_specs=out_specs, check_vma=False
    )
```

```python
import math

import jax
import jax.numpy as jnp
import numpy as np
from jax import lax
from jax.experimental import pallas as pl
from jax.sharding import PartitionSpec as P

SUB = 2
OSTEPS = 2


visc_coef = 0.01
diff_coef = 0.2
wind_coef = 0.1
surf_coef = 0.2


def neighbour(values, step_x, step_y):
    count_x, count_y = lax.axis_size("gx"), lax.axis_size("gy")
    if step_y == 0:
        return lax.ppermute(values, "gx", [(i, (i + step_x) % count_x) for i in range(count_x)])
    if step_x == 0:
        return lax.ppermute(values, "gy", [(j, (j + step_y) % count_y) for j in range(count_y)])
    pairs = [
        (i * count_y + j, ((i + step_x) % count_x) * count_y + (j + step_y) % count_y)
        for i in range(count_x)
        for j in range(count_y)
    ]
    return lax.ppermute(values, ("gx", "gy"), pairs)


def shifted(values, before, after, axis):
    size = values.shape[axis]
    layout = [1] * values.ndim
    layout[axis] = size
    position = jnp.arange(size).reshape(layout)
    prev = jnp.concatenate([lax.slice_in_dim(values, 0, 1, axis=axis), lax.slice_in_dim(values, 0, size - 1, axis=axis)], axis=axis)
    nxt = jnp.concatenate([lax.slice_in_dim(values, 1, size, axis=axis), lax.slice_in_dim(values, size - 1, size, axis=axis)], axis=axis)
    prev = jnp.where(position == 0, jnp.broadcast_to(before, values.shape), prev)
    nxt = jnp.where(position == size - 1, jnp.broadcast_to(after, values.shape), nxt)
    return prev, nxt


def pair_merge(values, before, after, axis):
    size = values.shape[axis]
    layout = [1] * values.ndim
    layout[axis] = size
    position = (jnp.arange(size) % 4).reshape(layout)
    prev, nxt = shifted(values, before, after, axis)
    return values + jnp.where(position == 0, prev, jnp.where(position == 3, nxt, 0.0))


def packed(values):
    if values.size % 128:
        return values
    return values.reshape(-1, 128)


def exchange(values, step_x, step_y):
    return neighbour(packed(values), step_x, step_y).reshape(values.shape)


def assemble(stiff):
    last_x, last_y = stiff.shape[1] - 1, stiff.shape[2] - 1
    from_left = exchange(stiff[:, :, last_y], 0, 1)[:, :, None]
    from_right = exchange(stiff[:, :, 0], 0, -1)[:, :, None]
    merged = pair_merge(stiff, from_left, from_right, 2)
    from_up = exchange(merged[:, last_x, :], 1, 0)[:, None, :]
    from_down = exchange(merged[:, 0, :], -1, 0)[:, None, :]
    return pair_merge(merged, from_up, from_down, 1)


def stiffness(state_in, metric, derivative_np, weights_np):
    levels, xsize, ysize = state_in.shape
    precision = lax.Precision.HIGH
    block_x = jnp.asarray(np.kron(np.eye(xsize // 4), derivative_np), jnp.float32)
    block_y = jnp.asarray(np.kron(np.eye(ysize // 4), derivative_np), jnp.float32)
    weight_x = jnp.asarray(np.tile(weights_np, xsize // 4), jnp.float32)[:, None]
    weight_y = jnp.asarray(np.tile(weights_np, ysize // 4), jnp.float32)[None, :]
    along_x = jnp.einsum("ab,lby->lay", block_x, state_in, precision=precision)
    term_x = (
        jnp.einsum("ba,lby->lay", block_x, weight_x * metric[0] * along_x, precision=precision)
        * weight_y
    )
    along_y = jnp.einsum("lxc,dc->lxd", state_in, block_y, precision=precision)
    term_y = (
        jnp.einsum("lxc,cd->lxd", weight_y * metric[1] * along_y, block_y, precision=precision)
        * weight_x
    )
    return term_x + term_y


def tracer_step(tracers, velocity):
    last_x, last_y = tracers.shape[-2] - 1, tracers.shape[-1] - 1
    from_up = exchange(tracers[..., last_x, :], 1, 0)[..., None, :]
    from_down = exchange(tracers[..., 0, :], -1, 0)[..., None, :]
    from_left = exchange(tracers[..., last_y], 0, 1)[..., None]
    from_right = exchange(tracers[..., 0], 0, -1)[..., None]
    west, east = shifted(tracers, from_up, from_down, tracers.ndim - 2)
    south, north = shifted(tracers, from_left, from_right, tracers.ndim - 1)
    return (
        tracers
        + diff_coef * (east + west + north + south - 4.0 * tracers)
        - 0.5 * velocity[0] * (east - west)
        - 0.5 * velocity[1] * (north - south)
    )


def gll_tables():
    points = np.array([-1.0, -1.0 / np.sqrt(5.0), 1.0 / np.sqrt(5.0), 1.0])
    weights = np.array([1.0 / 6.0, 5.0 / 6.0, 5.0 / 6.0, 1.0 / 6.0])
    derivative = np.zeros((4, 4))
    for target in range(4):
        for source in range(4):
            if target == source:
                derivative[target, source] = np.sum(
                    [
                        1.0 / (points[source] - points[others])
                        for others in range(4)
                        if others != source
                    ]
                )
            else:
                numer = np.prod(
                    [
                        points[target] - points[others]
                        for others in range(4)
                        if others != target and others != source
                    ]
                )
                denom = np.prod(
                    [points[source] - points[others] for others in range(4) if others != source]
                )
                derivative[target, source] = numer / denom
    massw = np.array([1.0 / 3.0, 5.0 / 6.0, 5.0 / 6.0, 1.0 / 3.0])
    return (derivative, weights, massw)


def mass_inverse(massw_np, xsize, ysize):
    return jnp.asarray(
        1.0 / (np.tile(massw_np, xsize // 4)[:, None] * np.tile(massw_np, ysize // 4)[None, :]),
        jnp.float32,
    )


def gather_kernel(index_ref, table_ref, out_ref):
    fields, rows, tile = table_ref.shape[0], table_ref.shape[1], out_ref.shape[1]
    index = index_ref[...]
    onehot = (lax.broadcasted_iota(jnp.int32, (128, tile), 0) == (index & 127)).astype(jnp.bfloat16)
    select = lax.broadcasted_iota(jnp.int32, (rows, tile), 0) == (index >> 7)
    for field in range(fields):
        rest = table_ref[field]
        whole = jnp.zeros((rows, tile), jnp.float32)
        for part in range(3):
            piece = rest.astype(jnp.bfloat16)
            rest = rest - piece.astype(jnp.float32)
            whole = whole + jnp.dot(piece, onehot, preferred_element_type=jnp.float32)
        out_ref[pl.ds(field, 1), :] = jnp.sum(jnp.where(select, whole, 0.0), axis=0, keepdims=True)


def onehot_gather(table, index):
    fields, total = table.shape
    rows = total // 128
    flat = index.reshape(1, -1)
    count = flat.shape[1]
    tile = math.gcd(count, 1024)
    return pl.pallas_call(
        gather_kernel,
        grid=(count // tile,),
        in_specs=[
            pl.BlockSpec((1, tile), lambda step: (0, step)),
            pl.BlockSpec((fields, rows, 128), lambda step: (0, 0, 0)),
        ],
        out_specs=pl.BlockSpec((fields, tile), lambda step: (0, step)),
        out_shape=jax.ShapeDtypeStruct((fields, count), jnp.float32),
    )(flat, table.reshape(fields, rows, 128))


def per_device(
    atm_state,
    metric,
    send_idx,
    send_counts,
    ocean_tracers,
    ocean_velocity,
    remap_slots,
    remap_weights,
):
    fields, levels, xlocal, ylocal = atm_state.shape
    derivative_np, weights_np, massw_np = gll_tables()
    state_now = atm_state.reshape(fields * levels, xlocal, ylocal)
    inv_mass = mass_inverse(massw_np, xlocal, ylocal)
    for substep in range(SUB):
        stiff = stiffness(state_now, metric, derivative_np, weights_np)
        state_now = state_now - visc_coef * assemble(stiff) * inv_mass
    atm_out = state_now.reshape(fields, levels, xlocal, ylocal)
    bottom = atm_out[:, levels - 1]
    speed = jnp.sqrt(1.0 + bottom[0] * bottom[0] + bottom[1] * bottom[1])
    flux_flat = (bottom * speed).reshape(fields, xlocal * ylocal)
    node_total = xlocal * ylocal
    rank_total = send_idx.shape[1]
    slot_cap = send_idx.shape[2]
    payload = onehot_gather(flux_flat, send_idx[0]).reshape(fields, rank_total, slot_cap)
    count_row = send_counts[0]
    live_slots = (jnp.arange(slot_cap)[None, :] < count_row[:, None]).astype(jnp.float32)
    payload = payload * live_slots[None]
    received = lax.all_to_all(payload, ("gx", "gy"), split_axis=1, concat_axis=1, tiled=True)
    received = received.reshape(fields, -1)
    source_count, ocean_x, ocean_y = remap_slots.shape
    gathered = onehot_gather(received, remap_slots).reshape(fields, source_count, ocean_x, ocean_y)
    ocean_flux = jnp.sum(remap_weights[None] * gathered, axis=1)
    velocity = ocean_velocity.at[0, 0].add(wind_coef * jnp.tanh(ocean_flux[0]))
    velocity = velocity.at[1, 0].add(wind_coef * jnp.tanh(ocean_flux[1]))
    tracers = ocean_tracers.at[0, 0].add(surf_coef * ocean_flux[2])
    tracers = tracers.at[1, 0].add(surf_coef * ocean_flux[3])
    for repeat in range(OSTEPS):
        tracers = tracer_step(tracers, velocity)
    return (atm_out, tracers)


def solution(mesh):
    in_specs = (
        P(None, None, "gx", "gy"),
        P(None, "gx", "gy"),
        P(("gx", "gy"), None, None),
        P(("gx", "gy"), None),
        P(None, None, "gx", "gy"),
        P(None, None, "gx", "gy"),
        P(None, "gx", "gy"),
        P(None, "gx", "gy"),
    )
    out_specs = (P(None, None, "gx", "gy"), P(None, None, "gx", "gy"))
    return jax.shard_map(
        per_device, mesh=mesh, in_specs=in_specs, out_specs=out_specs, check_vma=False
    )
```

```python
import math

import jax
import jax.numpy as jnp
import numpy as np
from jax import lax
from jax.experimental import pallas as pl
from jax.sharding import PartitionSpec as P

SUB = 2
OSTEPS = 2


visc_coef = 0.01
diff_coef = 0.2
wind_coef = 0.1
surf_coef = 0.2


def neighbour(values, step_x, step_y):
    count_x, count_y = lax.axis_size("gx"), lax.axis_size("gy")
    if step_y == 0:
        return lax.ppermute(values, "gx", [(i, (i + step_x) % count_x) for i in range(count_x)])
    if step_x == 0:
        return lax.ppermute(values, "gy", [(j, (j + step_y) % count_y) for j in range(count_y)])
    pairs = [
        (i * count_y + j, ((i + step_x) % count_x) * count_y + (j + step_y) % count_y)
        for i in range(count_x)
        for j in range(count_y)
    ]
    return lax.ppermute(values, ("gx", "gy"), pairs)


def shifted(values, before, after, axis):
    size = values.shape[axis]
    layout = [1] * values.ndim
    layout[axis] = size
    position = jnp.arange(size).reshape(layout)
    prev = jnp.concatenate([lax.slice_in_dim(values, 0, 1, axis=axis), lax.slice_in_dim(values, 0, size - 1, axis=axis)], axis=axis)
    nxt = jnp.concatenate([lax.slice_in_dim(values, 1, size, axis=axis), lax.slice_in_dim(values, size - 1, size, axis=axis)], axis=axis)
    prev = jnp.where(position == 0, jnp.broadcast_to(before, values.shape), prev)
    nxt = jnp.where(position == size - 1, jnp.broadcast_to(after, values.shape), nxt)
    return prev, nxt


def packed(values):
    if values.size % 128:
        return values
    return values.reshape(-1, 128)


def exchange(values, step_x, step_y):
    return neighbour(packed(values), step_x, step_y).reshape(values.shape)


def pair_matrix(size):
    position = np.arange(size)
    starts = position[position % 4 == 0][1:]
    ends = position[position % 4 == 3][:-1]
    pair = np.eye(size)
    pair[starts - 1, starts] = 1.0
    pair[ends + 1, ends] = 1.0
    return pair


def substep(state_in, metric, derivative_np, weights_np, inv_mass):
    levels, xsize, ysize = state_in.shape
    precision = lax.Precision.HIGH
    block_x = np.kron(np.eye(xsize // 4), derivative_np)
    block_y = np.kron(np.eye(ysize // 4), derivative_np)
    weight_x = np.tile(weights_np, xsize // 4)
    weight_y = np.tile(weights_np, ysize // 4)
    pair_y = pair_matrix(ysize)
    term_x_right = jnp.asarray(weight_y[:, None] * pair_y, jnp.float32)
    term_y_right = jnp.asarray(block_y @ pair_y, jnp.float32)
    pair_x = jnp.asarray(pair_matrix(xsize).T, jnp.float32)
    block_x = jnp.asarray(block_x, jnp.float32)
    along_x = jnp.einsum("ab,lby->lay", block_x, state_in, precision=precision)
    scaled_x = jnp.asarray(weight_x[:, None], jnp.float32) * metric[0] * along_x
    term_x = jnp.einsum("ba,lby->lay", block_x, scaled_x, precision=precision)
    along_y = jnp.einsum("lxc,dc->lxd", state_in, jnp.asarray(block_y, jnp.float32), precision=precision)
    scaled_y = jnp.asarray(weight_y[None, :], jnp.float32) * metric[1] * along_y
    merged = jnp.einsum("lxc,cd->lxd", term_x, term_x_right, precision=precision) + jnp.einsum(
        "lxc,cd->lxd", scaled_y, term_y_right, precision=precision
    ) * jnp.asarray(weight_x[:, None], jnp.float32)
    last_x, last_y = xsize - 1, ysize - 1
    from_left = exchange(merged[:, :, last_y], 0, 1)[:, :, None]
    from_right = exchange(merged[:, :, 0], 0, -1)[:, :, None]
    column = jnp.arange(ysize)
    merged = merged + jnp.where(column == 0, from_left, jnp.where(column == last_y, from_right, 0.0))
    from_up = exchange(merged[:, last_x, :], 1, 0)[:, None, :]
    from_down = exchange(merged[:, 0, :], -1, 0)[:, None, :]
    row = jnp.arange(xsize)[:, None]
    total = jnp.einsum("ab,lby->lay", pair_x, merged, precision=precision) + jnp.where(
        row == 0, from_up, jnp.where(row == last_x, from_down, 0.0)
    )
    return state_in - visc_coef * total * inv_mass


def tracer_step(tracers, velocity):
    last_x, last_y = tracers.shape[-2] - 1, tracers.shape[-1] - 1
    from_up = exchange(tracers[..., last_x, :], 1, 0)[..., None, :]
    from_down = exchange(tracers[..., 0, :], -1, 0)[..., None, :]
    from_left = exchange(tracers[..., last_y], 0, 1)[..., None]
    from_right = exchange(tracers[..., 0], 0, -1)[..., None]
    west, east = shifted(tracers, from_up, from_down, tracers.ndim - 2)
    south, north = shifted(tracers, from_left, from_right, tracers.ndim - 1)
    return (
        tracers
        + diff_coef * (east + west + north + south - 4.0 * tracers)
        - 0.5 * velocity[0] * (east - west)
        - 0.5 * velocity[1] * (north - south)
    )


def gll_tables():
    points = np.array([-1.0, -1.0 / np.sqrt(5.0), 1.0 / np.sqrt(5.0), 1.0])
    weights = np.array([1.0 / 6.0, 5.0 / 6.0, 5.0 / 6.0, 1.0 / 6.0])
    derivative = np.zeros((4, 4))
    for target in range(4):
        for source in range(4):
            if target == source:
                derivative[target, source] = np.sum(
                    [
                        1.0 / (points[source] - points[others])
                        for others in range(4)
                        if others != source
                    ]
                )
            else:
                numer = np.prod(
                    [
                        points[target] - points[others]
                        for others in range(4)
                        if others != target and others != source
                    ]
                )
                denom = np.prod(
                    [points[source] - points[others] for others in range(4) if others != source]
                )
                derivative[target, source] = numer / denom
    massw = np.array([1.0 / 3.0, 5.0 / 6.0, 5.0 / 6.0, 1.0 / 3.0])
    return (derivative, weights, massw)


def mass_inverse(massw_np, xsize, ysize):
    return jnp.asarray(
        1.0 / (np.tile(massw_np, xsize // 4)[:, None] * np.tile(massw_np, ysize // 4)[None, :]),
        jnp.float32,
    )


def gather_kernel(index_ref, table_ref, out_ref):
    fields, rows, tile = table_ref.shape[0], table_ref.shape[1], out_ref.shape[1]
    index = index_ref[...]
    onehot = (lax.broadcasted_iota(jnp.int32, (128, tile), 0) == (index & 127)).astype(jnp.bfloat16)
    select = lax.broadcasted_iota(jnp.int32, (rows, tile), 0) == (index >> 7)
    for field in range(fields):
        rest = table_ref[field]
        whole = jnp.zeros((rows, tile), jnp.float32)
        for part in range(3):
            piece = rest.astype(jnp.bfloat16)
            rest = rest - piece.astype(jnp.float32)
            whole = whole + jnp.dot(piece, onehot, preferred_element_type=jnp.float32)
        out_ref[pl.ds(field, 1), :] = jnp.sum(jnp.where(select, whole, 0.0), axis=0, keepdims=True)


def onehot_gather(table, index):
    fields, total = table.shape
    rows = total // 128
    flat = index.reshape(1, -1)
    count = flat.shape[1]
    tile = math.gcd(count, 1024)
    return pl.pallas_call(
        gather_kernel,
        grid=(count // tile,),
        in_specs=[
            pl.BlockSpec((1, tile), lambda step: (0, step)),
            pl.BlockSpec((fields, rows, 128), lambda step: (0, 0, 0)),
        ],
        out_specs=pl.BlockSpec((fields, tile), lambda step: (0, step)),
        out_shape=jax.ShapeDtypeStruct((fields, count), jnp.float32),
    )(flat, table.reshape(fields, rows, 128))


def per_device(
    atm_state,
    metric,
    send_idx,
    send_counts,
    ocean_tracers,
    ocean_velocity,
    remap_slots,
    remap_weights,
):
    fields, levels, xlocal, ylocal = atm_state.shape
    derivative_np, weights_np, massw_np = gll_tables()
    state_now = atm_state.reshape(fields * levels, xlocal, ylocal)
    inv_mass = mass_inverse(massw_np, xlocal, ylocal)
    for repeat in range(SUB):
        state_now = substep(state_now, metric, derivative_np, weights_np, inv_mass)
    atm_out = state_now.reshape(fields, levels, xlocal, ylocal)
    bottom = atm_out[:, levels - 1]
    speed = jnp.sqrt(1.0 + bottom[0] * bottom[0] + bottom[1] * bottom[1])
    flux_flat = (bottom * speed).reshape(fields, xlocal * ylocal)
    node_total = xlocal * ylocal
    rank_total = send_idx.shape[1]
    slot_cap = send_idx.shape[2]
    payload = onehot_gather(flux_flat, send_idx[0]).reshape(fields, rank_total, slot_cap)
    count_row = send_counts[0]
    live_slots = (jnp.arange(slot_cap)[None, :] < count_row[:, None]).astype(jnp.float32)
    payload = payload * live_slots[None]
    received = lax.all_to_all(payload, ("gx", "gy"), split_axis=1, concat_axis=1, tiled=True)
    received = received.reshape(fields, -1)
    source_count, ocean_x, ocean_y = remap_slots.shape
    gathered = onehot_gather(received, remap_slots).reshape(fields, source_count, ocean_x, ocean_y)
    ocean_flux = jnp.sum(remap_weights[None] * gathered, axis=1)
    velocity = ocean_velocity.at[0, 0].add(wind_coef * jnp.tanh(ocean_flux[0]))
    velocity = velocity.at[1, 0].add(wind_coef * jnp.tanh(ocean_flux[1]))
    tracers = ocean_tracers.at[0, 0].add(surf_coef * ocean_flux[2])
    tracers = tracers.at[1, 0].add(surf_coef * ocean_flux[3])
    for repeat in range(OSTEPS):
        tracers = tracer_step(tracers, velocity)
    return (atm_out, tracers)


def solution(mesh):
    in_specs = (
        P(None, None, "gx", "gy"),
        P(None, "gx", "gy"),
        P(("gx", "gy"), None, None),
        P(("gx", "gy"), None),
        P(None, None, "gx", "gy"),
        P(None, None, "gx", "gy"),
        P(None, "gx", "gy"),
        P(None, "gx", "gy"),
    )
    out_specs = (P(None, None, "gx", "gy"), P(None, None, "gx", "gy"))
    return jax.shard_map(
        per_device, mesh=mesh, in_specs=in_specs, out_specs=out_specs, check_vma=False
    )
```

```python
import math

import jax
import jax.numpy as jnp
import numpy as np
from jax import lax
from jax.experimental import pallas as pl
from jax.sharding import PartitionSpec as P

SUB = 2
OSTEPS = 2


visc_coef = 0.01
diff_coef = 0.2
wind_coef = 0.1
surf_coef = 0.2


def neighbour(values, step_x, step_y):
    count_x, count_y = lax.axis_size("gx"), lax.axis_size("gy")
    if step_y == 0:
        return lax.ppermute(values, "gx", [(i, (i + step_x) % count_x) for i in range(count_x)])
    if step_x == 0:
        return lax.ppermute(values, "gy", [(j, (j + step_y) % count_y) for j in range(count_y)])
    pairs = [
        (i * count_y + j, ((i + step_x) % count_x) * count_y + (j + step_y) % count_y)
        for i in range(count_x)
        for j in range(count_y)
    ]
    return lax.ppermute(values, ("gx", "gy"), pairs)


def shifted(values, before, after, axis):
    size = values.shape[axis]
    layout = [1] * values.ndim
    layout[axis] = size
    position = jnp.arange(size).reshape(layout)
    prev = jnp.concatenate([lax.slice_in_dim(values, 0, 1, axis=axis), lax.slice_in_dim(values, 0, size - 1, axis=axis)], axis=axis)
    nxt = jnp.concatenate([lax.slice_in_dim(values, 1, size, axis=axis), lax.slice_in_dim(values, size - 1, size, axis=axis)], axis=axis)
    prev = jnp.where(position == 0, jnp.broadcast_to(before, values.shape), prev)
    nxt = jnp.where(position == size - 1, jnp.broadcast_to(after, values.shape), nxt)
    return prev, nxt


def packed(values):
    if values.size % 128:
        return values
    return values.reshape(-1, 128)


def exchange(values, step_x, step_y):
    return neighbour(packed(values), step_x, step_y).reshape(values.shape)


def pair_matrix(size):
    position = np.arange(size)
    starts = position[position % 4 == 0][1:]
    ends = position[position % 4 == 3][:-1]
    pair = np.eye(size)
    pair[starts - 1, starts] = 1.0
    pair[ends + 1, ends] = 1.0
    return pair


def substep(state_in, metric, derivative_np, weights_np, inv_mass):
    levels, xsize, ysize = state_in.shape
    precision = lax.Precision.HIGH
    block_x = np.kron(np.eye(xsize // 4), derivative_np)
    block_y = np.kron(np.eye(ysize // 4), derivative_np)
    weight_x = np.tile(weights_np, xsize // 4)
    weight_y = np.tile(weights_np, ysize // 4)
    pair_y = pair_matrix(ysize)
    term_x_right = jnp.asarray(weight_y[:, None] * pair_y, jnp.float32)
    term_y_right = jnp.asarray(block_y @ pair_y, jnp.float32)
    pair_x = jnp.asarray(pair_matrix(xsize).T, jnp.float32)
    block_x = jnp.asarray(block_x, jnp.float32)
    along_x = jnp.einsum("ab,lby->lay", block_x, state_in, precision=precision)
    scaled_x = jnp.asarray(weight_x[:, None], jnp.float32) * metric[0] * along_x
    term_x = jnp.einsum("ba,lby->lay", block_x, scaled_x, precision=precision)
    along_y = jnp.einsum("lxc,dc->lxd", state_in, jnp.asarray(block_y, jnp.float32), precision=precision)
    scaled_y = jnp.asarray(weight_y[None, :], jnp.float32) * metric[1] * along_y
    merged = jnp.einsum("lxc,cd->lxd", term_x, term_x_right, precision=precision) + jnp.einsum(
        "lxc,cd->lxd", scaled_y, term_y_right, precision=precision
    ) * jnp.asarray(weight_x[:, None], jnp.float32)
    last_x, last_y = xsize - 1, ysize - 1
    from_left = exchange(merged[:, :, last_y], 0, 1)[:, :, None]
    from_right = exchange(merged[:, :, 0], 0, -1)[:, :, None]
    column = jnp.arange(ysize)
    merged = merged + jnp.where(column == 0, from_left, jnp.where(column == last_y, from_right, 0.0))
    from_up = exchange(merged[:, last_x, :], 1, 0)[:, None, :]
    from_down = exchange(merged[:, 0, :], -1, 0)[:, None, :]
    row = jnp.arange(xsize)[:, None]
    total = jnp.einsum("ab,lby->lay", pair_x, merged, precision=precision) + jnp.where(
        row == 0, from_up, jnp.where(row == last_x, from_down, 0.0)
    )
    return state_in - visc_coef * total * inv_mass


def tracer_step(tracers, velocity):
    last_x, last_y = tracers.shape[-2] - 1, tracers.shape[-1] - 1
    from_up = exchange(tracers[..., last_x, :], 1, 0)[..., None, :]
    from_down = exchange(tracers[..., 0, :], -1, 0)[..., None, :]
    from_left = exchange(tracers[..., last_y], 0, 1)[..., None]
    from_right = exchange(tracers[..., 0], 0, -1)[..., None]
    west, east = shifted(tracers, from_up, from_down, tracers.ndim - 2)
    south, north = shifted(tracers, from_left, from_right, tracers.ndim - 1)
    return (
        tracers
        + diff_coef * (east + west + north + south - 4.0 * tracers)
        - 0.5 * velocity[0] * (east - west)
        - 0.5 * velocity[1] * (north - south)
    )


def gll_tables():
    points = np.array([-1.0, -1.0 / np.sqrt(5.0), 1.0 / np.sqrt(5.0), 1.0])
    weights = np.array([1.0 / 6.0, 5.0 / 6.0, 5.0 / 6.0, 1.0 / 6.0])
    derivative = np.zeros((4, 4))
    for target in range(4):
        for source in range(4):
            if target == source:
                derivative[target, source] = np.sum(
                    [
                        1.0 / (points[source] - points[others])
                        for others in range(4)
                        if others != source
                    ]
                )
            else:
                numer = np.prod(
                    [
                        points[target] - points[others]
                        for others in range(4)
                        if others != target and others != source
                    ]
                )
                denom = np.prod(
                    [points[source] - points[others] for others in range(4) if others != source]
                )
                derivative[target, source] = numer / denom
    massw = np.array([1.0 / 3.0, 5.0 / 6.0, 5.0 / 6.0, 1.0 / 3.0])
    return (derivative, weights, massw)


def mass_inverse(massw_np, xsize, ysize):
    return jnp.asarray(
        1.0 / (np.tile(massw_np, xsize // 4)[:, None] * np.tile(massw_np, ysize // 4)[None, :]),
        jnp.float32,
    )


def gather_kernel(index_ref, table_ref, out_ref):
    fields, rows, tile = table_ref.shape[0], table_ref.shape[1], out_ref.shape[1]
    index = index_ref[...]
    onehot = (lax.broadcasted_iota(jnp.int32, (128, tile), 0) == (index & 127)).astype(jnp.bfloat16)
    select = lax.broadcasted_iota(jnp.int32, (rows, tile), 0) == (index >> 7)
    for field in range(fields):
        rest = table_ref[field]
        whole = jnp.zeros((rows, tile), jnp.float32)
        for part in range(3):
            piece = rest.astype(jnp.bfloat16)
            rest = rest - piece.astype(jnp.float32)
            whole = whole + jnp.dot(piece, onehot, preferred_element_type=jnp.float32)
        out_ref[pl.ds(field, 1), :] = jnp.sum(jnp.where(select, whole, 0.0), axis=0, keepdims=True)


def onehot_gather(table, index):
    fields, total = table.shape
    rows = total // 128
    flat = index.reshape(1, -1)
    count = flat.shape[1]
    tile = math.gcd(count, 1024)
    return pl.pallas_call(
        gather_kernel,
        grid=(count // tile,),
        in_specs=[
            pl.BlockSpec((1, tile), lambda step: (0, step)),
            pl.BlockSpec((fields, rows, 128), lambda step: (0, 0, 0)),
        ],
        out_specs=pl.BlockSpec((fields, tile), lambda step: (0, step)),
        out_shape=jax.ShapeDtypeStruct((fields, count), jnp.float32),
    )(flat, table.reshape(fields, rows, 128))


def per_device(
    atm_state,
    metric,
    send_idx,
    send_counts,
    ocean_tracers,
    ocean_velocity,
    remap_slots,
    remap_weights,
):
    fields, levels, xlocal, ylocal = atm_state.shape
    derivative_np, weights_np, massw_np = gll_tables()
    state_now = atm_state.reshape(fields * levels, xlocal, ylocal)
    inv_mass = mass_inverse(massw_np, xlocal, ylocal)
    for repeat in range(SUB):
        state_now = substep(state_now, metric, derivative_np, weights_np, inv_mass)
    atm_out = state_now.reshape(fields, levels, xlocal, ylocal)
    bottom = atm_out[:, levels - 1]
    speed = jnp.sqrt(1.0 + bottom[0] * bottom[0] + bottom[1] * bottom[1])
    flux_flat = (bottom * speed).reshape(fields, xlocal * ylocal)
    node_total = xlocal * ylocal
    rank_total = send_idx.shape[1]
    slot_cap = send_idx.shape[2]
    payload = onehot_gather(flux_flat, send_idx[0]).reshape(fields, rank_total, slot_cap)
    count_row = send_counts[0]
    live_slots = (jnp.arange(slot_cap)[None, :] < count_row[:, None]).astype(jnp.float32)
    payload = payload * live_slots[None]
    staged = payload.reshape(fields, lax.axis_size("gx"), lax.axis_size("gy"), slot_cap)
    staged = lax.all_to_all(staged, "gy", split_axis=2, concat_axis=2, tiled=True)
    staged = lax.all_to_all(staged, "gx", split_axis=1, concat_axis=1, tiled=True)
    received = staged.reshape(fields, -1)
    source_count, ocean_x, ocean_y = remap_slots.shape
    gathered = onehot_gather(received, remap_slots).reshape(fields, source_count, ocean_x, ocean_y)
    ocean_flux = jnp.sum(remap_weights[None] * gathered, axis=1)
    velocity = ocean_velocity.at[0, 0].add(wind_coef * jnp.tanh(ocean_flux[0]))
    velocity = velocity.at[1, 0].add(wind_coef * jnp.tanh(ocean_flux[1]))
    tracers = ocean_tracers.at[0, 0].add(surf_coef * ocean_flux[2])
    tracers = tracers.at[1, 0].add(surf_coef * ocean_flux[3])
    for repeat in range(OSTEPS):
        tracers = tracer_step(tracers, velocity)
    return (atm_out, tracers)


def solution(mesh):
    in_specs = (
        P(None, None, "gx", "gy"),
        P(None, "gx", "gy"),
        P(("gx", "gy"), None, None),
        P(("gx", "gy"), None),
        P(None, None, "gx", "gy"),
        P(None, None, "gx", "gy"),
        P(None, "gx", "gy"),
        P(None, "gx", "gy"),
    )
    out_specs = (P(None, None, "gx", "gy"), P(None, None, "gx", "gy"))
    return jax.shard_map(
        per_device, mesh=mesh, in_specs=in_specs, out_specs=out_specs, check_vma=False
    )
```

```python
import math

import jax
import jax.numpy as jnp
import numpy as np
from jax import lax
from jax.experimental import pallas as pl
from jax.sharding import PartitionSpec as P

SUB = 2
OSTEPS = 2


visc_coef = 0.01
diff_coef = 0.2
wind_coef = 0.1
surf_coef = 0.2


def neighbour(values, step_x, step_y):
    count_x, count_y = lax.axis_size("gx"), lax.axis_size("gy")
    if step_y == 0:
        return lax.ppermute(values, "gx", [(i, (i + step_x) % count_x) for i in range(count_x)])
    if step_x == 0:
        return lax.ppermute(values, "gy", [(j, (j + step_y) % count_y) for j in range(count_y)])
    pairs = [
        (i * count_y + j, ((i + step_x) % count_x) * count_y + (j + step_y) % count_y)
        for i in range(count_x)
        for j in range(count_y)
    ]
    return lax.ppermute(values, ("gx", "gy"), pairs)


def shifted(values, before, after, axis):
    size = values.shape[axis]
    layout = [1] * values.ndim
    layout[axis] = size
    position = jnp.arange(size).reshape(layout)
    prev = jnp.concatenate([lax.slice_in_dim(values, 0, 1, axis=axis), lax.slice_in_dim(values, 0, size - 1, axis=axis)], axis=axis)
    nxt = jnp.concatenate([lax.slice_in_dim(values, 1, size, axis=axis), lax.slice_in_dim(values, size - 1, size, axis=axis)], axis=axis)
    prev = jnp.where(position == 0, jnp.broadcast_to(before, values.shape), prev)
    nxt = jnp.where(position == size - 1, jnp.broadcast_to(after, values.shape), nxt)
    return prev, nxt


def packed(values):
    if values.size % 128:
        return values
    return values.reshape(-1, 128)


def exchange(values, step_x, step_y):
    return neighbour(packed(values), step_x, step_y).reshape(values.shape)


def pair_matrix(size):
    position = np.arange(size)
    starts = position[position % 4 == 0][1:]
    ends = position[position % 4 == 3][:-1]
    pair = np.eye(size)
    pair[starts - 1, starts] = 1.0
    pair[ends + 1, ends] = 1.0
    return pair


def substep(state_in, metric, derivative_np, weights_np, inv_mass):
    levels, xsize, ysize = state_in.shape
    precision = lax.Precision.HIGH
    block_x = np.kron(np.eye(xsize // 4), derivative_np)
    block_y = np.kron(np.eye(ysize // 4), derivative_np)
    weight_x = np.tile(weights_np, xsize // 4)
    weight_y = np.tile(weights_np, ysize // 4)
    pair_y = pair_matrix(ysize)
    term_x_right = jnp.asarray(weight_y[:, None] * pair_y, jnp.float32)
    term_y_right = jnp.asarray(block_y @ pair_y, jnp.float32)
    pair_x = jnp.asarray(pair_matrix(xsize).T, jnp.float32)
    block_x = jnp.asarray(block_x, jnp.float32)
    along_x = jnp.einsum("ab,lby->lay", block_x, state_in, precision=precision)
    scaled_x = jnp.asarray(weight_x[:, None], jnp.float32) * metric[0] * along_x
    term_x = jnp.einsum("ba,lby->lay", block_x, scaled_x, precision=precision)
    along_y = jnp.einsum("lxc,dc->lxd", state_in, jnp.asarray(block_y, jnp.float32), precision=precision)
    scaled_y = jnp.asarray(weight_y[None, :], jnp.float32) * metric[1] * along_y
    merged = jnp.einsum("lxc,cd->lxd", term_x, term_x_right, precision=precision) + jnp.einsum(
        "lxc,cd->lxd", scaled_y, term_y_right, precision=precision
    ) * jnp.asarray(weight_x[:, None], jnp.float32)
    last_x, last_y = xsize - 1, ysize - 1
    from_left = exchange(merged[:, :, last_y], 0, 1)[:, :, None]
    from_right = exchange(merged[:, :, 0], 0, -1)[:, :, None]
    column = jnp.arange(ysize)
    merged = merged + jnp.where(column == 0, from_left, jnp.where(column == last_y, from_right, 0.0))
    from_up = exchange(merged[:, last_x, :], 1, 0)[:, None, :]
    from_down = exchange(merged[:, 0, :], -1, 0)[:, None, :]
    row = jnp.arange(xsize)[:, None]
    total = jnp.einsum("ab,lby->lay", pair_x, merged, precision=precision) + jnp.where(
        row == 0, from_up, jnp.where(row == last_x, from_down, 0.0)
    )
    return state_in - visc_coef * total * inv_mass


def tracer_step(tracers, velocity):
    xsize, ysize = tracers.shape[-2], tracers.shape[-1]
    last_x, last_y = xsize - 1, ysize - 1
    precision = lax.Precision.HIGH
    from_up = exchange(tracers[..., last_x, :], 1, 0)[..., None, :]
    from_down = exchange(tracers[..., 0, :], -1, 0)[..., None, :]
    from_left = exchange(tracers[..., last_y], 0, 1)[..., None]
    from_right = exchange(tracers[..., 0], 0, -1)[..., None]
    above_x = np.eye(xsize, k=1)
    above_y = np.eye(ysize, k=1)
    sum_x = jnp.asarray(above_x + above_x.T, jnp.float32)
    diff_x = jnp.asarray(above_x - above_x.T, jnp.float32)
    sum_y = jnp.asarray(above_y + above_y.T, jnp.float32)
    diff_y = jnp.asarray(above_y.T - above_y, jnp.float32)
    row = jnp.arange(xsize)[:, None]
    column = jnp.arange(ysize)
    east = jnp.where(row == last_x, from_down, 0.0)
    west = jnp.where(row == 0, from_up, 0.0)
    north = jnp.where(column == last_y, from_right, 0.0)
    south = jnp.where(column == 0, from_left, 0.0)
    across_x = jnp.einsum("ab,...by->...ay", sum_x, tracers, precision=precision) + (east + west)
    slope_x = jnp.einsum("ab,...by->...ay", diff_x, tracers, precision=precision) + (east - west)
    across_y = jnp.einsum("...xc,cd->...xd", tracers, sum_y, precision=precision) + (north + south)
    slope_y = jnp.einsum("...xc,cd->...xd", tracers, diff_y, precision=precision) + (north - south)
    return (
        tracers
        + diff_coef * (across_x + across_y - 4.0 * tracers)
        - 0.5 * velocity[0] * slope_x
        - 0.5 * velocity[1] * slope_y
    )


def gll_tables():
    points = np.array([-1.0, -1.0 / np.sqrt(5.0), 1.0 / np.sqrt(5.0), 1.0])
    weights = np.array([1.0 / 6.0, 5.0 / 6.0, 5.0 / 6.0, 1.0 / 6.0])
    derivative = np.zeros((4, 4))
    for target in range(4):
        for source in range(4):
            if target == source:
                derivative[target, source] = np.sum(
                    [
                        1.0 / (points[source] - points[others])
                        for others in range(4)
                        if others != source
                    ]
                )
            else:
                numer = np.prod(
                    [
                        points[target] - points[others]
                        for others in range(4)
                        if others != target and others != source
                    ]
                )
                denom = np.prod(
                    [points[source] - points[others] for others in range(4) if others != source]
                )
                derivative[target, source] = numer / denom
    massw = np.array([1.0 / 3.0, 5.0 / 6.0, 5.0 / 6.0, 1.0 / 3.0])
    return (derivative, weights, massw)


def mass_inverse(massw_np, xsize, ysize):
    return jnp.asarray(
        1.0 / (np.tile(massw_np, xsize // 4)[:, None] * np.tile(massw_np, ysize // 4)[None, :]),
        jnp.float32,
    )


def gather_kernel(index_ref, table_ref, out_ref):
    fields, rows, tile = table_ref.shape[0], table_ref.shape[1], out_ref.shape[1]
    index = index_ref[...]
    onehot = (lax.broadcasted_iota(jnp.int32, (128, tile), 0) == (index & 127)).astype(jnp.bfloat16)
    select = lax.broadcasted_iota(jnp.int32, (rows, tile), 0) == (index >> 7)
    for field in range(fields):
        rest = table_ref[field]
        whole = jnp.zeros((rows, tile), jnp.float32)
        for part in range(3):
            piece = rest.astype(jnp.bfloat16)
            rest = rest - piece.astype(jnp.float32)
            whole = whole + jnp.dot(piece, onehot, preferred_element_type=jnp.float32)
        out_ref[pl.ds(field, 1), :] = jnp.sum(jnp.where(select, whole, 0.0), axis=0, keepdims=True)


def onehot_gather(table, index):
    fields, total = table.shape
    rows = total // 128
    flat = index.reshape(1, -1)
    count = flat.shape[1]
    tile = math.gcd(count, 1024)
    return pl.pallas_call(
        gather_kernel,
        grid=(count // tile,),
        in_specs=[
            pl.BlockSpec((1, tile), lambda step: (0, step)),
            pl.BlockSpec((fields, rows, 128), lambda step: (0, 0, 0)),
        ],
        out_specs=pl.BlockSpec((fields, tile), lambda step: (0, step)),
        out_shape=jax.ShapeDtypeStruct((fields, count), jnp.float32),
    )(flat, table.reshape(fields, rows, 128))


def per_device(
    atm_state,
    metric,
    send_idx,
    send_counts,
    ocean_tracers,
    ocean_velocity,
    remap_slots,
    remap_weights,
):
    fields, levels, xlocal, ylocal = atm_state.shape
    derivative_np, weights_np, massw_np = gll_tables()
    state_now = atm_state.reshape(fields * levels, xlocal, ylocal)
    inv_mass = mass_inverse(massw_np, xlocal, ylocal)
    for repeat in range(SUB):
        state_now = substep(state_now, metric, derivative_np, weights_np, inv_mass)
    atm_out = state_now.reshape(fields, levels, xlocal, ylocal)
    bottom = atm_out[:, levels - 1]
    speed = jnp.sqrt(1.0 + bottom[0] * bottom[0] + bottom[1] * bottom[1])
    flux_flat = (bottom * speed).reshape(fields, xlocal * ylocal)
    node_total = xlocal * ylocal
    rank_total = send_idx.shape[1]
    slot_cap = send_idx.shape[2]
    payload = onehot_gather(flux_flat, send_idx[0]).reshape(fields, rank_total, slot_cap)
    count_row = send_counts[0]
    live_slots = (jnp.arange(slot_cap)[None, :] < count_row[:, None]).astype(jnp.float32)
    payload = payload * live_slots[None]
    received = lax.all_to_all(payload, ("gx", "gy"), split_axis=1, concat_axis=1, tiled=True)
    received = received.reshape(fields, -1)
    source_count, ocean_x, ocean_y = remap_slots.shape
    gathered = onehot_gather(received, remap_slots).reshape(fields, source_count, ocean_x, ocean_y)
    ocean_flux = jnp.sum(remap_weights[None] * gathered, axis=1)
    velocity = ocean_velocity.at[0, 0].add(wind_coef * jnp.tanh(ocean_flux[0]))
    velocity = velocity.at[1, 0].add(wind_coef * jnp.tanh(ocean_flux[1]))
    tracers = ocean_tracers.at[0, 0].add(surf_coef * ocean_flux[2])
    tracers = tracers.at[1, 0].add(surf_coef * ocean_flux[3])
    for repeat in range(OSTEPS):
        tracers = tracer_step(tracers, velocity)
    return (atm_out, tracers)


def solution(mesh):
    in_specs = (
        P(None, None, "gx", "gy"),
        P(None, "gx", "gy"),
        P(("gx", "gy"), None, None),
        P(("gx", "gy"), None),
        P(None, None, "gx", "gy"),
        P(None, None, "gx", "gy"),
        P(None, "gx", "gy"),
        P(None, "gx", "gy"),
    )
    out_specs = (P(None, None, "gx", "gy"), P(None, None, "gx", "gy"))
    return jax.shard_map(
        per_device, mesh=mesh, in_specs=in_specs, out_specs=out_specs, check_vma=False
    )
```

```python
import math

import jax
import jax.numpy as jnp
import numpy as np
from jax import lax
from jax.experimental import pallas as pl
from jax.sharding import PartitionSpec as P

SUB = 2
OSTEPS = 2


visc_coef = 0.01
diff_coef = 0.2
wind_coef = 0.1
surf_coef = 0.2


def neighbour(values, step_x, step_y):
    count_x, count_y = lax.axis_size("gx"), lax.axis_size("gy")
    if step_y == 0:
        return lax.ppermute(values, "gx", [(i, (i + step_x) % count_x) for i in range(count_x)])
    if step_x == 0:
        return lax.ppermute(values, "gy", [(j, (j + step_y) % count_y) for j in range(count_y)])
    pairs = [
        (i * count_y + j, ((i + step_x) % count_x) * count_y + (j + step_y) % count_y)
        for i in range(count_x)
        for j in range(count_y)
    ]
    return lax.ppermute(values, ("gx", "gy"), pairs)


def shifted(values, before, after, axis):
    size = values.shape[axis]
    layout = [1] * values.ndim
    layout[axis] = size
    position = jnp.arange(size).reshape(layout)
    prev = jnp.concatenate([lax.slice_in_dim(values, 0, 1, axis=axis), lax.slice_in_dim(values, 0, size - 1, axis=axis)], axis=axis)
    nxt = jnp.concatenate([lax.slice_in_dim(values, 1, size, axis=axis), lax.slice_in_dim(values, size - 1, size, axis=axis)], axis=axis)
    prev = jnp.where(position == 0, jnp.broadcast_to(before, values.shape), prev)
    nxt = jnp.where(position == size - 1, jnp.broadcast_to(after, values.shape), nxt)
    return prev, nxt


def packed(values):
    if values.size % 128:
        return values
    return values.reshape(-1, 128)


def exchange(values, step_x, step_y):
    return neighbour(packed(values), step_x, step_y).reshape(values.shape)


def pair_matrix(size):
    position = np.arange(size)
    starts = position[position % 4 == 0][1:]
    ends = position[position % 4 == 3][:-1]
    pair = np.eye(size)
    pair[starts - 1, starts] = 1.0
    pair[ends + 1, ends] = 1.0
    return pair


def substep(state_in, metric, derivative_np, weights_np, inv_mass):
    levels, xsize, ysize = state_in.shape
    precision = lax.Precision.HIGH
    block_x = np.kron(np.eye(xsize // 4), derivative_np)
    block_y = np.kron(np.eye(ysize // 4), derivative_np)
    weight_x = np.tile(weights_np, xsize // 4)
    weight_y = np.tile(weights_np, ysize // 4)
    pair_y = pair_matrix(ysize)
    term_x_right = jnp.asarray(weight_y[:, None] * pair_y, jnp.float32)
    term_y_right = jnp.asarray(block_y @ pair_y, jnp.float32)
    pair_x = jnp.asarray(pair_matrix(xsize).T, jnp.float32)
    block_x = jnp.asarray(block_x, jnp.float32)
    along_x = jnp.einsum("ab,lby->lay", block_x, state_in, precision=precision)
    scaled_x = jnp.asarray(weight_x[:, None], jnp.float32) * metric[0] * along_x
    term_x = jnp.einsum("ba,lby->lay", block_x, scaled_x, precision=precision)
    along_y = jnp.einsum("lxc,dc->lxd", state_in, jnp.asarray(block_y, jnp.float32), precision=precision)
    scaled_y = jnp.asarray(weight_y[None, :], jnp.float32) * metric[1] * along_y
    merged = jnp.einsum("lxc,cd->lxd", term_x, term_x_right, precision=precision) + jnp.einsum(
        "lxc,cd->lxd", scaled_y, term_y_right, precision=precision
    ) * jnp.asarray(weight_x[:, None], jnp.float32)
    last_x, last_y = xsize - 1, ysize - 1
    from_left = exchange(merged[:, :, last_y], 0, 1)[:, :, None]
    from_right = exchange(merged[:, :, 0], 0, -1)[:, :, None]
    column = jnp.arange(ysize)
    merged = merged + jnp.where(column == 0, from_left, jnp.where(column == last_y, from_right, 0.0))
    from_up = exchange(merged[:, last_x, :], 1, 0)[:, None, :]
    from_down = exchange(merged[:, 0, :], -1, 0)[:, None, :]
    row = jnp.arange(xsize)[:, None]
    total = jnp.einsum("ab,lby->lay", pair_x, merged, precision=precision) + jnp.where(
        row == 0, from_up, jnp.where(row == last_x, from_down, 0.0)
    )
    return state_in - visc_coef * total * inv_mass


def tracer_step(tracers, velocity):
    xsize, ysize = tracers.shape[-2], tracers.shape[-1]
    last_x, last_y = xsize - 1, ysize - 1
    precision = lax.Precision.HIGH
    from_up = exchange(tracers[..., last_x, :], 1, 0)[..., None, :]
    from_down = exchange(tracers[..., 0, :], -1, 0)[..., None, :]
    from_left = exchange(tracers[..., last_y], 0, 1)[..., None]
    from_right = exchange(tracers[..., 0], 0, -1)[..., None]
    above_x = np.eye(xsize, k=1)
    above_y = np.eye(ysize, k=1)
    sum_x = jnp.asarray(above_x + above_x.T, jnp.float32)
    diff_x = jnp.asarray(above_x - above_x.T, jnp.float32)
    sum_y = jnp.asarray(above_y + above_y.T, jnp.float32)
    diff_y = jnp.asarray(above_y.T - above_y, jnp.float32)
    row = jnp.arange(xsize)[:, None]
    column = jnp.arange(ysize)
    east = jnp.where(row == last_x, from_down, 0.0)
    west = jnp.where(row == 0, from_up, 0.0)
    north = jnp.where(column == last_y, from_right, 0.0)
    south = jnp.where(column == 0, from_left, 0.0)
    across_x = jnp.einsum("ab,...by->...ay", sum_x, tracers, precision=precision) + (east + west)
    slope_x = jnp.einsum("ab,...by->...ay", diff_x, tracers, precision=precision) + (east - west)
    across_y = jnp.einsum("...xc,cd->...xd", tracers, sum_y, precision=precision) + (north + south)
    slope_y = jnp.einsum("...xc,cd->...xd", tracers, diff_y, precision=precision) + (north - south)
    return (
        tracers
        + diff_coef * (across_x + across_y - 4.0 * tracers)
        - 0.5 * velocity[0] * slope_x
        - 0.5 * velocity[1] * slope_y
    )


def gll_tables():
    points = np.array([-1.0, -1.0 / np.sqrt(5.0), 1.0 / np.sqrt(5.0), 1.0])
    weights = np.array([1.0 / 6.0, 5.0 / 6.0, 5.0 / 6.0, 1.0 / 6.0])
    derivative = np.zeros((4, 4))
    for target in range(4):
        for source in range(4):
            if target == source:
                derivative[target, source] = np.sum(
                    [
                        1.0 / (points[source] - points[others])
                        for others in range(4)
                        if others != source
                    ]
                )
            else:
                numer = np.prod(
                    [
                        points[target] - points[others]
                        for others in range(4)
                        if others != target and others != source
                    ]
                )
                denom = np.prod(
                    [points[source] - points[others] for others in range(4) if others != source]
                )
                derivative[target, source] = numer / denom
    massw = np.array([1.0 / 3.0, 5.0 / 6.0, 5.0 / 6.0, 1.0 / 3.0])
    return (derivative, weights, massw)


def mass_inverse(massw_np, xsize, ysize):
    return jnp.asarray(
        1.0 / (np.tile(massw_np, xsize // 4)[:, None] * np.tile(massw_np, ysize // 4)[None, :]),
        jnp.float32,
    )


def gather_kernel(index_ref, table_ref, out_ref):
    fields, rows, tile = table_ref.shape[0], table_ref.shape[1], out_ref.shape[1]
    index = index_ref[...]
    onehot = (lax.broadcasted_iota(jnp.int32, (128, tile), 0) == (index & 127)).astype(jnp.bfloat16)
    select = lax.broadcasted_iota(jnp.int32, (rows, tile), 0) == (index >> 7)
    rest = table_ref[...]
    parts = []
    for part in range(3):
        piece = rest.astype(jnp.bfloat16)
        rest = rest - piece.astype(jnp.float32)
        parts.append(piece)
    stacked = jnp.concatenate(parts, axis=1).reshape(fields * 3 * rows, 128)
    picked = jnp.dot(stacked, onehot, preferred_element_type=jnp.float32)
    for field in range(fields):
        base = field * 3 * rows
        whole = picked[base : base + rows] + picked[base + rows : base + 2 * rows] + picked[base + 2 * rows : base + 3 * rows]
        out_ref[pl.ds(field, 1), :] = jnp.sum(jnp.where(select, whole, 0.0), axis=0, keepdims=True)


def onehot_gather(table, index):
    fields, total = table.shape
    rows = total // 128
    flat = index.reshape(1, -1)
    count = flat.shape[1]
    tile = 128
    while tile < 2048 and count % (2 * tile) == 0 and fields * 3 * rows * tile * 8 <= 4 * 2**20:
        tile *= 2
    return pl.pallas_call(
        gather_kernel,
        grid=(count // tile,),
        in_specs=[
            pl.BlockSpec((1, tile), lambda step: (0, step)),
            pl.BlockSpec((fields, rows, 128), lambda step: (0, 0, 0)),
        ],
        out_specs=pl.BlockSpec((fields, tile), lambda step: (0, step)),
        out_shape=jax.ShapeDtypeStruct((fields, count), jnp.float32),
    )(flat, table.reshape(fields, rows, 128))


def per_device(
    atm_state,
    metric,
    send_idx,
    send_counts,
    ocean_tracers,
    ocean_velocity,
    remap_slots,
    remap_weights,
):
    fields, levels, xlocal, ylocal = atm_state.shape
    derivative_np, weights_np, massw_np = gll_tables()
    state_now = atm_state.reshape(fields * levels, xlocal, ylocal)
    inv_mass = mass_inverse(massw_np, xlocal, ylocal)
    for repeat in range(SUB):
        state_now = substep(state_now, metric, derivative_np, weights_np, inv_mass)
    atm_out = state_now.reshape(fields, levels, xlocal, ylocal)
    bottom = atm_out[:, levels - 1]
    speed = jnp.sqrt(1.0 + bottom[0] * bottom[0] + bottom[1] * bottom[1])
    flux_flat = (bottom * speed).reshape(fields, xlocal * ylocal)
    node_total = xlocal * ylocal
    rank_total = send_idx.shape[1]
    slot_cap = send_idx.shape[2]
    payload = onehot_gather(flux_flat, send_idx[0]).reshape(fields, rank_total, slot_cap)
    count_row = send_counts[0]
    live_slots = (jnp.arange(slot_cap)[None, :] < count_row[:, None]).astype(jnp.float32)
    payload = payload * live_slots[None]
    received = lax.all_to_all(payload, ("gx", "gy"), split_axis=1, concat_axis=1, tiled=True)
    received = received.reshape(fields, -1)
    source_count, ocean_x, ocean_y = remap_slots.shape
    gathered = onehot_gather(received, remap_slots).reshape(fields, source_count, ocean_x, ocean_y)
    ocean_flux = jnp.sum(remap_weights[None] * gathered, axis=1)
    velocity = ocean_velocity.at[0, 0].add(wind_coef * jnp.tanh(ocean_flux[0]))
    velocity = velocity.at[1, 0].add(wind_coef * jnp.tanh(ocean_flux[1]))
    tracers = ocean_tracers.at[0, 0].add(surf_coef * ocean_flux[2])
    tracers = tracers.at[1, 0].add(surf_coef * ocean_flux[3])
    for repeat in range(OSTEPS):
        tracers = tracer_step(tracers, velocity)
    return (atm_out, tracers)


def solution(mesh):
    in_specs = (
        P(None, None, "gx", "gy"),
        P(None, "gx", "gy"),
        P(("gx", "gy"), None, None),
        P(("gx", "gy"), None),
        P(None, None, "gx", "gy"),
        P(None, None, "gx", "gy"),
        P(None, "gx", "gy"),
        P(None, "gx", "gy"),
    )
    out_specs = (P(None, None, "gx", "gy"), P(None, None, "gx", "gy"))
    return jax.shard_map(
        per_device, mesh=mesh, in_specs=in_specs, out_specs=out_specs, check_vma=False
    )
```

```python
import math

import jax
import jax.numpy as jnp
import numpy as np
from jax import lax
from jax.experimental import pallas as pl
from jax.sharding import PartitionSpec as P

SUB = 2
OSTEPS = 2


visc_coef = 0.01
diff_coef = 0.2
wind_coef = 0.1
surf_coef = 0.2


def neighbour(values, step_x, step_y):
    count_x, count_y = lax.axis_size("gx"), lax.axis_size("gy")
    if step_y == 0:
        return lax.ppermute(values, "gx", [(i, (i + step_x) % count_x) for i in range(count_x)])
    if step_x == 0:
        return lax.ppermute(values, "gy", [(j, (j + step_y) % count_y) for j in range(count_y)])
    pairs = [
        (i * count_y + j, ((i + step_x) % count_x) * count_y + (j + step_y) % count_y)
        for i in range(count_x)
        for j in range(count_y)
    ]
    return lax.ppermute(values, ("gx", "gy"), pairs)


def shifted(values, before, after, axis):
    size = values.shape[axis]
    layout = [1] * values.ndim
    layout[axis] = size
    position = jnp.arange(size).reshape(layout)
    prev = jnp.concatenate([lax.slice_in_dim(values, 0, 1, axis=axis), lax.slice_in_dim(values, 0, size - 1, axis=axis)], axis=axis)
    nxt = jnp.concatenate([lax.slice_in_dim(values, 1, size, axis=axis), lax.slice_in_dim(values, size - 1, size, axis=axis)], axis=axis)
    prev = jnp.where(position == 0, jnp.broadcast_to(before, values.shape), prev)
    nxt = jnp.where(position == size - 1, jnp.broadcast_to(after, values.shape), nxt)
    return prev, nxt


def packed(values):
    if values.size % 128:
        return values
    return values.reshape(-1, 128)


def exchange(values, step_x, step_y):
    return neighbour(packed(values), step_x, step_y).reshape(values.shape)


def pair_matrix(size):
    position = np.arange(size)
    starts = position[position % 4 == 0][1:]
    ends = position[position % 4 == 3][:-1]
    pair = np.eye(size)
    pair[starts - 1, starts] = 1.0
    pair[ends + 1, ends] = 1.0
    return pair


def substep(state_in, metric, derivative_np, weights_np, inv_mass):
    levels, xsize, ysize = state_in.shape
    precision = lax.Precision.HIGH
    block_x = np.kron(np.eye(xsize // 4), derivative_np)
    block_y = np.kron(np.eye(ysize // 4), derivative_np)
    weight_x = np.tile(weights_np, xsize // 4)
    weight_y = np.tile(weights_np, ysize // 4)
    pair_y = pair_matrix(ysize)
    term_x_right = jnp.asarray(weight_y[:, None] * pair_y, jnp.float32)
    term_y_right = jnp.asarray(block_y @ pair_y, jnp.float32)
    pair_x = jnp.asarray(pair_matrix(xsize).T, jnp.float32)
    block_x = jnp.asarray(block_x, jnp.float32)
    along_x = jnp.einsum("ab,lby->lay", block_x, state_in, precision=precision)
    scaled_x = jnp.asarray(weight_x[:, None], jnp.float32) * metric[0] * along_x
    term_x = jnp.einsum("ba,lby->lay", block_x, scaled_x, precision=precision)
    along_y = jnp.einsum("lxc,dc->lxd", state_in, jnp.asarray(block_y, jnp.float32), precision=precision)
    scaled_y = jnp.asarray(weight_y[None, :], jnp.float32) * metric[1] * along_y
    merged = jnp.einsum("lxc,cd->lxd", term_x, term_x_right, precision=precision) + jnp.einsum(
        "lxc,cd->lxd", scaled_y, term_y_right, precision=precision
    ) * jnp.asarray(weight_x[:, None], jnp.float32)
    last_x, last_y = xsize - 1, ysize - 1
    from_left = exchange(merged[:, :, last_y], 0, 1)[:, :, None]
    from_right = exchange(merged[:, :, 0], 0, -1)[:, :, None]
    column = jnp.arange(ysize)
    merged = merged + jnp.where(column == 0, from_left, jnp.where(column == last_y, from_right, 0.0))
    from_up = exchange(merged[:, last_x, :], 1, 0)[:, None, :]
    from_down = exchange(merged[:, 0, :], -1, 0)[:, None, :]
    row = jnp.arange(xsize)[:, None]
    total = jnp.einsum("ab,lby->lay", pair_x, merged, precision=precision) + jnp.where(
        row == 0, from_up, jnp.where(row == last_x, from_down, 0.0)
    )
    return state_in - visc_coef * total * inv_mass


def tracer_step(tracers, velocity):
    xsize, ysize = tracers.shape[-2], tracers.shape[-1]
    last_x, last_y = xsize - 1, ysize - 1
    precision = lax.Precision.HIGH
    from_up = exchange(tracers[..., last_x, :], 1, 0)[..., None, :]
    from_down = exchange(tracers[..., 0, :], -1, 0)[..., None, :]
    from_left = exchange(tracers[..., last_y], 0, 1)[..., None]
    from_right = exchange(tracers[..., 0], 0, -1)[..., None]
    above_x = np.eye(xsize, k=1)
    above_y = np.eye(ysize, k=1)
    sum_x = jnp.asarray(above_x + above_x.T, jnp.float32)
    diff_x = jnp.asarray(above_x - above_x.T, jnp.float32)
    sum_y = jnp.asarray(above_y + above_y.T, jnp.float32)
    diff_y = jnp.asarray(above_y.T - above_y, jnp.float32)
    row = jnp.arange(xsize)[:, None]
    column = jnp.arange(ysize)
    east = jnp.where(row == last_x, from_down, 0.0)
    west = jnp.where(row == 0, from_up, 0.0)
    north = jnp.where(column == last_y, from_right, 0.0)
    south = jnp.where(column == 0, from_left, 0.0)
    across_x = jnp.einsum("ab,...by->...ay", sum_x, tracers, precision=precision) + (east + west)
    slope_x = jnp.einsum("ab,...by->...ay", diff_x, tracers, precision=precision) + (east - west)
    across_y = jnp.einsum("...xc,cd->...xd", tracers, sum_y, precision=precision) + (north + south)
    slope_y = jnp.einsum("...xc,cd->...xd", tracers, diff_y, precision=precision) + (north - south)
    return (
        tracers
        + diff_coef * (across_x + across_y - 4.0 * tracers)
        - 0.5 * velocity[0] * slope_x
        - 0.5 * velocity[1] * slope_y
    )


def gll_tables():
    points = np.array([-1.0, -1.0 / np.sqrt(5.0), 1.0 / np.sqrt(5.0), 1.0])
    weights = np.array([1.0 / 6.0, 5.0 / 6.0, 5.0 / 6.0, 1.0 / 6.0])
    derivative = np.zeros((4, 4))
    for target in range(4):
        for source in range(4):
            if target == source:
                derivative[target, source] = np.sum(
                    [
                        1.0 / (points[source] - points[others])
                        for others in range(4)
                        if others != source
                    ]
                )
            else:
                numer = np.prod(
                    [
                        points[target] - points[others]
                        for others in range(4)
                        if others != target and others != source
                    ]
                )
                denom = np.prod(
                    [points[source] - points[others] for others in range(4) if others != source]
                )
                derivative[target, source] = numer / denom
    massw = np.array([1.0 / 3.0, 5.0 / 6.0, 5.0 / 6.0, 1.0 / 3.0])
    return (derivative, weights, massw)


def mass_inverse(massw_np, xsize, ysize):
    return jnp.asarray(
        1.0 / (np.tile(massw_np, xsize // 4)[:, None] * np.tile(massw_np, ysize // 4)[None, :]),
        jnp.float32,
    )


def gather_kernel(index_ref, table_ref, out_ref):
    fields, rows, tile = table_ref.shape[0], table_ref.shape[1], out_ref.shape[1]
    index = index_ref[...]
    onehot = (lax.broadcasted_iota(jnp.int32, (128, tile), 0) == (index & 127)).astype(jnp.bfloat16)
    select = lax.broadcasted_iota(jnp.int32, (rows, tile), 0) == (index >> 7)
    rest = table_ref[...]
    parts = []
    for part in range(3):
        piece = rest.astype(jnp.bfloat16)
        rest = rest - piece.astype(jnp.float32)
        parts.append(piece)
    stacked = jnp.concatenate(parts, axis=2).reshape(fields * rows, 3 * 128)
    picked = jnp.dot(stacked, jnp.concatenate([onehot] * 3, axis=0), preferred_element_type=jnp.float32)
    for field in range(fields):
        whole = picked[field * rows : (field + 1) * rows]
        out_ref[pl.ds(field, 1), :] = jnp.sum(jnp.where(select, whole, 0.0), axis=0, keepdims=True)


def onehot_gather(table, index):
    fields, total = table.shape
    rows = total // 128
    flat = index.reshape(1, -1)
    count = flat.shape[1]
    tile = 128
    while tile < 2048 and count % (2 * tile) == 0 and fields * 3 * rows * tile * 8 <= 4 * 2**20:
        tile *= 2
    return pl.pallas_call(
        gather_kernel,
        grid=(count // tile,),
        in_specs=[
            pl.BlockSpec((1, tile), lambda step: (0, step)),
            pl.BlockSpec((fields, rows, 128), lambda step: (0, 0, 0)),
        ],
        out_specs=pl.BlockSpec((fields, tile), lambda step: (0, step)),
        out_shape=jax.ShapeDtypeStruct((fields, count), jnp.float32),
    )(flat, table.reshape(fields, rows, 128))


def per_device(
    atm_state,
    metric,
    send_idx,
    send_counts,
    ocean_tracers,
    ocean_velocity,
    remap_slots,
    remap_weights,
):
    fields, levels, xlocal, ylocal = atm_state.shape
    derivative_np, weights_np, massw_np = gll_tables()
    state_now = atm_state.reshape(fields * levels, xlocal, ylocal)
    inv_mass = mass_inverse(massw_np, xlocal, ylocal)
    for repeat in range(SUB):
        state_now = substep(state_now, metric, derivative_np, weights_np, inv_mass)
    atm_out = state_now.reshape(fields, levels, xlocal, ylocal)
    bottom = atm_out[:, levels - 1]
    speed = jnp.sqrt(1.0 + bottom[0] * bottom[0] + bottom[1] * bottom[1])
    flux_flat = (bottom * speed).reshape(fields, xlocal * ylocal)
    node_total = xlocal * ylocal
    rank_total = send_idx.shape[1]
    slot_cap = send_idx.shape[2]
    payload = onehot_gather(flux_flat, send_idx[0]).reshape(fields, rank_total, slot_cap)
    count_row = send_counts[0]
    live_slots = (jnp.arange(slot_cap)[None, :] < count_row[:, None]).astype(jnp.float32)
    payload = payload * live_slots[None]
    received = lax.all_to_all(payload, ("gx", "gy"), split_axis=1, concat_axis=1, tiled=True)
    received = received.reshape(fields, -1)
    source_count, ocean_x, ocean_y = remap_slots.shape
    gathered = onehot_gather(received, remap_slots).reshape(fields, source_count, ocean_x, ocean_y)
    ocean_flux = jnp.sum(remap_weights[None] * gathered, axis=1)
    velocity = ocean_velocity.at[0, 0].add(wind_coef * jnp.tanh(ocean_flux[0]))
    velocity = velocity.at[1, 0].add(wind_coef * jnp.tanh(ocean_flux[1]))
    tracers = ocean_tracers.at[0, 0].add(surf_coef * ocean_flux[2])
    tracers = tracers.at[1, 0].add(surf_coef * ocean_flux[3])
    for repeat in range(OSTEPS):
        tracers = tracer_step(tracers, velocity)
    return (atm_out, tracers)


def solution(mesh):
    in_specs = (
        P(None, None, "gx", "gy"),
        P(None, "gx", "gy"),
        P(("gx", "gy"), None, None),
        P(("gx", "gy"), None),
        P(None, None, "gx", "gy"),
        P(None, None, "gx", "gy"),
        P(None, "gx", "gy"),
        P(None, "gx", "gy"),
    )
    out_specs = (P(None, None, "gx", "gy"), P(None, None, "gx", "gy"))
    return jax.shard_map(
        per_device, mesh=mesh, in_specs=in_specs, out_specs=out_specs, check_vma=False
    )
```

```python
import math

import jax
import jax.numpy as jnp
import numpy as np
from jax import lax
from jax.experimental import pallas as pl
from jax.sharding import PartitionSpec as P

SUB = 2
OSTEPS = 2


visc_coef = 0.01
diff_coef = 0.2
wind_coef = 0.1
surf_coef = 0.2


def neighbour(values, step_x, step_y):
    count_x, count_y = lax.axis_size("gx"), lax.axis_size("gy")
    if step_y == 0:
        return lax.ppermute(values, "gx", [(i, (i + step_x) % count_x) for i in range(count_x)])
    if step_x == 0:
        return lax.ppermute(values, "gy", [(j, (j + step_y) % count_y) for j in range(count_y)])
    pairs = [
        (i * count_y + j, ((i + step_x) % count_x) * count_y + (j + step_y) % count_y)
        for i in range(count_x)
        for j in range(count_y)
    ]
    return lax.ppermute(values, ("gx", "gy"), pairs)


def shifted(values, before, after, axis):
    size = values.shape[axis]
    layout = [1] * values.ndim
    layout[axis] = size
    position = jnp.arange(size).reshape(layout)
    prev = jnp.concatenate([lax.slice_in_dim(values, 0, 1, axis=axis), lax.slice_in_dim(values, 0, size - 1, axis=axis)], axis=axis)
    nxt = jnp.concatenate([lax.slice_in_dim(values, 1, size, axis=axis), lax.slice_in_dim(values, size - 1, size, axis=axis)], axis=axis)
    prev = jnp.where(position == 0, jnp.broadcast_to(before, values.shape), prev)
    nxt = jnp.where(position == size - 1, jnp.broadcast_to(after, values.shape), nxt)
    return prev, nxt


def packed(values):
    if values.size % 128:
        return values
    return values.reshape(-1, 128)


def exchange(values, step_x, step_y):
    return neighbour(packed(values), step_x, step_y).reshape(values.shape)


def exchange_many(pieces, step_x, step_y):
    flat = [piece.reshape(-1, piece.shape[-1]) for piece in pieces]
    got = neighbour(jnp.concatenate(flat, axis=0), step_x, step_y)
    out, start = [], 0
    for piece, part in zip(pieces, flat):
        out.append(got[start : start + part.shape[0]].reshape(piece.shape))
        start += part.shape[0]
    return out


def pair_matrix(size):
    position = np.arange(size)
    starts = position[position % 4 == 0][1:]
    ends = position[position % 4 == 3][:-1]
    pair = np.eye(size)
    pair[starts - 1, starts] = 1.0
    pair[ends + 1, ends] = 1.0
    return pair


def substep(state_in, metric, derivative_np, weights_np, inv_mass, tracers, velocity):
    levels, xsize, ysize = state_in.shape
    precision = lax.Precision.HIGH
    block_x = np.kron(np.eye(xsize // 4), derivative_np)
    block_y = np.kron(np.eye(ysize // 4), derivative_np)
    weight_x = np.tile(weights_np, xsize // 4)
    weight_y = np.tile(weights_np, ysize // 4)
    pair_y = pair_matrix(ysize)
    term_x_right = jnp.asarray(weight_y[:, None] * pair_y, jnp.float32)
    term_y_right = jnp.asarray(block_y @ pair_y, jnp.float32)
    pair_x = jnp.asarray(pair_matrix(xsize).T, jnp.float32)
    block_x = jnp.asarray(block_x, jnp.float32)
    along_x = jnp.einsum("ab,lby->lay", block_x, state_in, precision=precision)
    scaled_x = jnp.asarray(weight_x[:, None], jnp.float32) * metric[0] * along_x
    term_x = jnp.einsum("ba,lby->lay", block_x, scaled_x, precision=precision)
    along_y = jnp.einsum("lxc,dc->lxd", state_in, jnp.asarray(block_y, jnp.float32), precision=precision)
    scaled_y = jnp.asarray(weight_y[None, :], jnp.float32) * metric[1] * along_y
    merged = jnp.einsum("lxc,cd->lxd", term_x, term_x_right, precision=precision) + jnp.einsum(
        "lxc,cd->lxd", scaled_y, term_y_right, precision=precision
    ) * jnp.asarray(weight_x[:, None], jnp.float32)
    last_x, last_y = xsize - 1, ysize - 1
    ocean_x, ocean_y = tracers.shape[-2] - 1, tracers.shape[-1] - 1
    from_left, sea_left = exchange_many([merged[:, :, last_y], tracers[..., ocean_y]], 0, 1)
    from_right, sea_right = exchange_many([merged[:, :, 0], tracers[..., 0]], 0, -1)
    column = jnp.arange(ysize)
    merged = merged + jnp.where(column == 0, from_left[:, :, None], jnp.where(column == last_y, from_right[:, :, None], 0.0))
    from_up, sea_up = exchange_many([merged[:, last_x, :], tracers[..., ocean_x, :]], 1, 0)
    from_down, sea_down = exchange_many([merged[:, 0, :], tracers[..., 0, :]], -1, 0)
    from_up, from_down = from_up[:, None, :], from_down[:, None, :]
    halos = (sea_up[..., None, :], sea_down[..., None, :], sea_left[..., None], sea_right[..., None])
    tracers = tracer_step(tracers, velocity, halos)
    row = jnp.arange(xsize)[:, None]
    total = jnp.einsum("ab,lby->lay", pair_x, merged, precision=precision) + jnp.where(
        row == 0, from_up, jnp.where(row == last_x, from_down, 0.0)
    )
    return state_in - visc_coef * total * inv_mass, tracers


def tracer_step(tracers, velocity, halos=None):
    xsize, ysize = tracers.shape[-2], tracers.shape[-1]
    last_x, last_y = xsize - 1, ysize - 1
    precision = lax.Precision.HIGH
    if halos is None:
        halos = (
            exchange(tracers[..., last_x, :], 1, 0)[..., None, :],
            exchange(tracers[..., 0, :], -1, 0)[..., None, :],
            exchange(tracers[..., last_y], 0, 1)[..., None],
            exchange(tracers[..., 0], 0, -1)[..., None],
        )
    from_up, from_down, from_left, from_right = halos
    above_x = np.eye(xsize, k=1)
    above_y = np.eye(ysize, k=1)
    sum_x = jnp.asarray(above_x + above_x.T, jnp.float32)
    diff_x = jnp.asarray(above_x - above_x.T, jnp.float32)
    sum_y = jnp.asarray(above_y + above_y.T, jnp.float32)
    diff_y = jnp.asarray(above_y.T - above_y, jnp.float32)
    row = jnp.arange(xsize)[:, None]
    column = jnp.arange(ysize)
    east = jnp.where(row == last_x, from_down, 0.0)
    west = jnp.where(row == 0, from_up, 0.0)
    north = jnp.where(column == last_y, from_right, 0.0)
    south = jnp.where(column == 0, from_left, 0.0)
    across_x = jnp.einsum("ab,...by->...ay", sum_x, tracers, precision=precision) + (east + west)
    slope_x = jnp.einsum("ab,...by->...ay", diff_x, tracers, precision=precision) + (east - west)
    across_y = jnp.einsum("...xc,cd->...xd", tracers, sum_y, precision=precision) + (north + south)
    slope_y = jnp.einsum("...xc,cd->...xd", tracers, diff_y, precision=precision) + (north - south)
    return (
        tracers
        + diff_coef * (across_x + across_y - 4.0 * tracers)
        - 0.5 * velocity[0] * slope_x
        - 0.5 * velocity[1] * slope_y
    )


def gll_tables():
    points = np.array([-1.0, -1.0 / np.sqrt(5.0), 1.0 / np.sqrt(5.0), 1.0])
    weights = np.array([1.0 / 6.0, 5.0 / 6.0, 5.0 / 6.0, 1.0 / 6.0])
    derivative = np.zeros((4, 4))
    for target in range(4):
        for source in range(4):
            if target == source:
                derivative[target, source] = np.sum(
                    [
                        1.0 / (points[source] - points[others])
                        for others in range(4)
                        if others != source
                    ]
                )
            else:
                numer = np.prod(
                    [
                        points[target] - points[others]
                        for others in range(4)
                        if others != target and others != source
                    ]
                )
                denom = np.prod(
                    [points[source] - points[others] for others in range(4) if others != source]
                )
                derivative[target, source] = numer / denom
    massw = np.array([1.0 / 3.0, 5.0 / 6.0, 5.0 / 6.0, 1.0 / 3.0])
    return (derivative, weights, massw)


def mass_inverse(massw_np, xsize, ysize):
    return jnp.asarray(
        1.0 / (np.tile(massw_np, xsize // 4)[:, None] * np.tile(massw_np, ysize // 4)[None, :]),
        jnp.float32,
    )


def gather_kernel(index_ref, table_ref, out_ref):
    fields, rows, tile = table_ref.shape[0], table_ref.shape[1], out_ref.shape[1]
    index = index_ref[...]
    onehot = (lax.broadcasted_iota(jnp.int32, (128, tile), 0) == (index & 127)).astype(jnp.bfloat16)
    select = lax.broadcasted_iota(jnp.int32, (rows, tile), 0) == (index >> 7)
    rest = table_ref[...]
    parts = []
    for part in range(3):
        piece = rest.astype(jnp.bfloat16)
        rest = rest - piece.astype(jnp.float32)
        parts.append(piece)
    stacked = jnp.concatenate(parts, axis=2).reshape(fields * rows, 3 * 128)
    picked = jnp.dot(stacked, jnp.concatenate([onehot] * 3, axis=0), preferred_element_type=jnp.float32)
    for field in range(fields):
        whole = picked[field * rows : (field + 1) * rows]
        out_ref[pl.ds(field, 1), :] = jnp.sum(jnp.where(select, whole, 0.0), axis=0, keepdims=True)


def onehot_gather(table, index):
    fields, total = table.shape
    rows = total // 128
    flat = index.reshape(1, -1)
    count = flat.shape[1]
    tile = 128
    while tile < 2048 and count % (2 * tile) == 0 and fields * 3 * rows * tile * 8 <= 4 * 2**20:
        tile *= 2
    return pl.pallas_call(
        gather_kernel,
        grid=(count // tile,),
        in_specs=[
            pl.BlockSpec((1, tile), lambda step: (0, step)),
            pl.BlockSpec((fields, rows, 128), lambda step: (0, 0, 0)),
        ],
        out_specs=pl.BlockSpec((fields, tile), lambda step: (0, step)),
        out_shape=jax.ShapeDtypeStruct((fields, count), jnp.float32),
    )(flat, table.reshape(fields, rows, 128))


def per_device(
    atm_state,
    metric,
    send_idx,
    send_counts,
    ocean_tracers,
    ocean_velocity,
    remap_slots,
    remap_weights,
):
    fields, levels, xlocal, ylocal = atm_state.shape
    derivative_np, weights_np, massw_np = gll_tables()
    state_now = atm_state.reshape(fields * levels, xlocal, ylocal)
    inv_mass = mass_inverse(massw_np, xlocal, ylocal)
    deep = ocean_tracers
    for repeat in range(SUB):
        if repeat < OSTEPS:
            state_now, deep = substep(state_now, metric, derivative_np, weights_np, inv_mass, deep, ocean_velocity)
        else:
            state_now, unused = substep(state_now, metric, derivative_np, weights_np, inv_mass, deep[:, :0], ocean_velocity[:, :0])
    for repeat in range(SUB, OSTEPS):
        deep = tracer_step(deep, ocean_velocity)
    atm_out = state_now.reshape(fields, levels, xlocal, ylocal)
    bottom = atm_out[:, levels - 1]
    speed = jnp.sqrt(1.0 + bottom[0] * bottom[0] + bottom[1] * bottom[1])
    flux_flat = (bottom * speed).reshape(fields, xlocal * ylocal)
    node_total = xlocal * ylocal
    rank_total = send_idx.shape[1]
    slot_cap = send_idx.shape[2]
    payload = onehot_gather(flux_flat, send_idx[0]).reshape(fields, rank_total, slot_cap)
    count_row = send_counts[0]
    live_slots = (jnp.arange(slot_cap)[None, :] < count_row[:, None]).astype(jnp.float32)
    payload = payload * live_slots[None]
    received = lax.all_to_all(payload, ("gx", "gy"), split_axis=1, concat_axis=1, tiled=True)
    received = received.reshape(fields, -1)
    source_count, ocean_x, ocean_y = remap_slots.shape
    gathered = onehot_gather(received, remap_slots).reshape(fields, source_count, ocean_x, ocean_y)
    ocean_flux = jnp.sum(remap_weights[None] * gathered, axis=1)
    velocity = ocean_velocity[:, :1]
    velocity = velocity.at[0, 0].add(wind_coef * jnp.tanh(ocean_flux[0]))
    velocity = velocity.at[1, 0].add(wind_coef * jnp.tanh(ocean_flux[1]))
    surface = ocean_tracers[:, :1]
    surface = surface.at[0, 0].add(surf_coef * ocean_flux[2])
    surface = surface.at[1, 0].add(surf_coef * ocean_flux[3])
    for repeat in range(OSTEPS):
        surface = tracer_step(surface, velocity)
    tracers = lax.dynamic_update_slice_in_dim(deep, surface, 0, axis=1)
    return (atm_out, tracers)


def solution(mesh):
    in_specs = (
        P(None, None, "gx", "gy"),
        P(None, "gx", "gy"),
        P(("gx", "gy"), None, None),
        P(("gx", "gy"), None),
        P(None, None, "gx", "gy"),
        P(None, None, "gx", "gy"),
        P(None, "gx", "gy"),
        P(None, "gx", "gy"),
    )
    out_specs = (P(None, None, "gx", "gy"), P(None, None, "gx", "gy"))
    return jax.shard_map(
        per_device, mesh=mesh, in_specs=in_specs, out_specs=out_specs, check_vma=False
    )
```

```python
import math

import jax
import jax.numpy as jnp
import numpy as np
from jax import lax
from jax.experimental import pallas as pl
from jax.sharding import PartitionSpec as P

SUB = 2
OSTEPS = 2


visc_coef = 0.01
diff_coef = 0.2
wind_coef = 0.1
surf_coef = 0.2


def neighbour(values, step_x, step_y):
    count_x, count_y = lax.axis_size("gx"), lax.axis_size("gy")
    if step_y == 0:
        return lax.ppermute(values, "gx", [(i, (i + step_x) % count_x) for i in range(count_x)])
    if step_x == 0:
        return lax.ppermute(values, "gy", [(j, (j + step_y) % count_y) for j in range(count_y)])
    pairs = [
        (i * count_y + j, ((i + step_x) % count_x) * count_y + (j + step_y) % count_y)
        for i in range(count_x)
        for j in range(count_y)
    ]
    return lax.ppermute(values, ("gx", "gy"), pairs)


def shifted(values, before, after, axis):
    size = values.shape[axis]
    layout = [1] * values.ndim
    layout[axis] = size
    position = jnp.arange(size).reshape(layout)
    prev = jnp.concatenate([lax.slice_in_dim(values, 0, 1, axis=axis), lax.slice_in_dim(values, 0, size - 1, axis=axis)], axis=axis)
    nxt = jnp.concatenate([lax.slice_in_dim(values, 1, size, axis=axis), lax.slice_in_dim(values, size - 1, size, axis=axis)], axis=axis)
    prev = jnp.where(position == 0, jnp.broadcast_to(before, values.shape), prev)
    nxt = jnp.where(position == size - 1, jnp.broadcast_to(after, values.shape), nxt)
    return prev, nxt


def packed(values):
    if values.size % 128:
        return values
    return values.reshape(-1, 128)


def exchange(values, step_x, step_y):
    return neighbour(packed(values), step_x, step_y).reshape(values.shape)


def pair_matrix(size):
    position = np.arange(size)
    starts = position[position % 4 == 0][1:]
    ends = position[position % 4 == 3][:-1]
    pair = np.eye(size)
    pair[starts - 1, starts] = 1.0
    pair[ends + 1, ends] = 1.0
    return pair


def substep(state_in, metric, derivative_np, weights_np, inv_mass):
    levels, xsize, ysize = state_in.shape
    precision = lax.Precision.HIGH
    block_x = np.kron(np.eye(xsize // 4), derivative_np)
    block_y = np.kron(np.eye(ysize // 4), derivative_np)
    weight_x = np.tile(weights_np, xsize // 4)
    weight_y = np.tile(weights_np, ysize // 4)
    pair_y = pair_matrix(ysize)
    term_x_right = jnp.asarray(weight_y[:, None] * pair_y, jnp.float32)
    term_y_right = jnp.asarray(block_y @ pair_y, jnp.float32)
    pair_x = jnp.asarray(pair_matrix(xsize).T, jnp.float32)
    block_x = jnp.asarray(block_x, jnp.float32)
    along_x = jnp.einsum("ab,lby->lay", block_x, state_in, precision=precision)
    scaled_x = jnp.asarray(weight_x[:, None], jnp.float32) * metric[0] * along_x
    term_x = jnp.einsum("ba,lby->lay", block_x, scaled_x, precision=precision)
    along_y = jnp.einsum("lxc,dc->lxd", state_in, jnp.asarray(block_y, jnp.float32), precision=precision)
    scaled_y = jnp.asarray(weight_y[None, :], jnp.float32) * metric[1] * along_y
    merged = jnp.einsum("lxc,cd->lxd", term_x, term_x_right, precision=precision) + jnp.einsum(
        "lxc,cd->lxd", scaled_y, term_y_right, precision=precision
    ) * jnp.asarray(weight_x[:, None], jnp.float32)
    last_x, last_y = xsize - 1, ysize - 1
    from_left = exchange(merged[:, :, last_y], 0, 1)[:, :, None]
    from_right = exchange(merged[:, :, 0], 0, -1)[:, :, None]
    column = jnp.arange(ysize)
    merged = merged + jnp.where(column == 0, from_left, jnp.where(column == last_y, from_right, 0.0))
    from_up = exchange(merged[:, last_x, :], 1, 0)[:, None, :]
    from_down = exchange(merged[:, 0, :], -1, 0)[:, None, :]
    row = jnp.arange(xsize)[:, None]
    total = jnp.einsum("ab,lby->lay", pair_x, merged, precision=precision) + jnp.where(
        row == 0, from_up, jnp.where(row == last_x, from_down, 0.0)
    )
    return state_in - visc_coef * total * inv_mass


def tracer_step(tracers, velocity):
    xsize, ysize = tracers.shape[-2], tracers.shape[-1]
    last_x, last_y = xsize - 1, ysize - 1
    precision = lax.Precision.HIGH
    from_up = exchange(tracers[..., last_x, :], 1, 0)[..., None, :]
    from_down = exchange(tracers[..., 0, :], -1, 0)[..., None, :]
    from_left = exchange(tracers[..., last_y], 0, 1)[..., None]
    from_right = exchange(tracers[..., 0], 0, -1)[..., None]
    above_x = np.eye(xsize, k=1)
    above_y = np.eye(ysize, k=1)
    sum_x = jnp.asarray(above_x + above_x.T, jnp.float32)
    diff_x = jnp.asarray(above_x - above_x.T, jnp.float32)
    sum_y = jnp.asarray(above_y + above_y.T, jnp.float32)
    diff_y = jnp.asarray(above_y.T - above_y, jnp.float32)
    row = jnp.arange(xsize)[:, None]
    column = jnp.arange(ysize)
    east = jnp.where(row == last_x, from_down, 0.0)
    west = jnp.where(row == 0, from_up, 0.0)
    north = jnp.where(column == last_y, from_right, 0.0)
    south = jnp.where(column == 0, from_left, 0.0)
    across_x = jnp.einsum("ab,...by->...ay", sum_x, tracers, precision=precision) + (east + west)
    slope_x = jnp.einsum("ab,...by->...ay", diff_x, tracers, precision=precision) + (east - west)
    across_y = jnp.einsum("...xc,cd->...xd", tracers, sum_y, precision=precision) + (north + south)
    slope_y = jnp.einsum("...xc,cd->...xd", tracers, diff_y, precision=precision) + (north - south)
    return (
        tracers
        + diff_coef * (across_x + across_y - 4.0 * tracers)
        - 0.5 * velocity[0] * slope_x
        - 0.5 * velocity[1] * slope_y
    )


def gll_tables():
    points = np.array([-1.0, -1.0 / np.sqrt(5.0), 1.0 / np.sqrt(5.0), 1.0])
    weights = np.array([1.0 / 6.0, 5.0 / 6.0, 5.0 / 6.0, 1.0 / 6.0])
    derivative = np.zeros((4, 4))
    for target in range(4):
        for source in range(4):
            if target == source:
                derivative[target, source] = np.sum(
                    [
                        1.0 / (points[source] - points[others])
                        for others in range(4)
                        if others != source
                    ]
                )
            else:
                numer = np.prod(
                    [
                        points[target] - points[others]
                        for others in range(4)
                        if others != target and others != source
                    ]
                )
                denom = np.prod(
                    [points[source] - points[others] for others in range(4) if others != source]
                )
                derivative[target, source] = numer / denom
    massw = np.array([1.0 / 3.0, 5.0 / 6.0, 5.0 / 6.0, 1.0 / 3.0])
    return (derivative, weights, massw)


def mass_inverse(massw_np, xsize, ysize):
    return jnp.asarray(
        1.0 / (np.tile(massw_np, xsize // 4)[:, None] * np.tile(massw_np, ysize // 4)[None, :]),
        jnp.float32,
    )


def gather_kernel(index_ref, scale_ref, table_ref, out_ref):
    fields, rows, tile = table_ref.shape[0], table_ref.shape[1], out_ref.shape[1]
    index = index_ref[...]
    onehot = (lax.broadcasted_iota(jnp.int32, (128, tile), 0) == (index & 127)).astype(jnp.bfloat16)
    select = lax.broadcasted_iota(jnp.int32, (rows, tile), 0) == (index >> 7)
    rest = table_ref[...]
    parts = []
    for part in range(3):
        piece = rest.astype(jnp.bfloat16)
        rest = rest - piece.astype(jnp.float32)
        parts.append(piece)
    stacked = jnp.concatenate(parts, axis=2).reshape(fields * rows, 3 * 128)
    picked = jnp.dot(stacked, jnp.concatenate([onehot] * 3, axis=0), preferred_element_type=jnp.float32)
    scale = scale_ref[...]
    values = jnp.concatenate(
        [jnp.sum(jnp.where(select, picked[f * rows : (f + 1) * rows], 0.0), axis=0, keepdims=True) for f in range(fields)],
        axis=0,
    ) * scale

    @pl.when(pl.program_id(1) == 0)
    def first():
        out_ref[...] = values

    @pl.when(pl.program_id(1) > 0)
    def rest_steps():
        out_ref[...] = out_ref[...] + values


def onehot_gather(table, index, scale, groups):
    fields, total = table.shape
    rows = total // 128
    flat = index.reshape(1, -1)
    count = flat.shape[1]
    width = count // groups
    tile = 128
    while tile < 2048 and width % (2 * tile) == 0 and fields * rows * tile * 8 <= 4 * 2**20:
        tile *= 2
    blocks = width // tile
    return pl.pallas_call(
        gather_kernel,
        grid=(blocks, groups),
        in_specs=[
            pl.BlockSpec((1, tile), lambda step, group: (0, group * blocks + step)),
            pl.BlockSpec((1, tile), lambda step, group: (0, group * blocks + step)),
            pl.BlockSpec((fields, rows, 128), lambda step, group: (0, 0, 0)),
        ],
        out_specs=pl.BlockSpec((fields, tile), lambda step, group: (0, step)),
        out_shape=jax.ShapeDtypeStruct((fields, width), jnp.float32),
    )(flat, scale.reshape(1, -1), table.reshape(fields, rows, 128))


def per_device(
    atm_state,
    metric,
    send_idx,
    send_counts,
    ocean_tracers,
    ocean_velocity,
    remap_slots,
    remap_weights,
):
    fields, levels, xlocal, ylocal = atm_state.shape
    derivative_np, weights_np, massw_np = gll_tables()
    state_now = atm_state.reshape(fields * levels, xlocal, ylocal)
    inv_mass = mass_inverse(massw_np, xlocal, ylocal)
    for repeat in range(SUB):
        state_now = substep(state_now, metric, derivative_np, weights_np, inv_mass)
    atm_out = state_now.reshape(fields, levels, xlocal, ylocal)
    bottom = atm_out[:, levels - 1]
    speed = jnp.sqrt(1.0 + bottom[0] * bottom[0] + bottom[1] * bottom[1])
    flux_flat = (bottom * speed).reshape(fields, xlocal * ylocal)
    node_total = xlocal * ylocal
    rank_total = send_idx.shape[1]
    slot_cap = send_idx.shape[2]
    count_row = send_counts[0]
    live_slots = (jnp.arange(slot_cap)[None, :] < count_row[:, None]).astype(jnp.float32)
    payload = onehot_gather(flux_flat, send_idx[0], live_slots, 1).reshape(fields, rank_total, slot_cap)
    received = lax.all_to_all(payload, ("gx", "gy"), split_axis=1, concat_axis=1, tiled=True)
    received = received.reshape(fields, -1)
    source_count, ocean_x, ocean_y = remap_slots.shape
    ocean_flux = onehot_gather(received, remap_slots, remap_weights, source_count).reshape(fields, ocean_x, ocean_y)
    velocity = ocean_velocity.at[0, 0].add(wind_coef * jnp.tanh(ocean_flux[0]))
    velocity = velocity.at[1, 0].add(wind_coef * jnp.tanh(ocean_flux[1]))
    tracers = ocean_tracers.at[0, 0].add(surf_coef * ocean_flux[2])
    tracers = tracers.at[1, 0].add(surf_coef * ocean_flux[3])
    for repeat in range(OSTEPS):
        tracers = tracer_step(tracers, velocity)
    return (atm_out, tracers)


def solution(mesh):
    in_specs = (
        P(None, None, "gx", "gy"),
        P(None, "gx", "gy"),
        P(("gx", "gy"), None, None),
        P(("gx", "gy"), None),
        P(None, None, "gx", "gy"),
        P(None, None, "gx", "gy"),
        P(None, "gx", "gy"),
        P(None, "gx", "gy"),
    )
    out_specs = (P(None, None, "gx", "gy"), P(None, None, "gx", "gy"))
    return jax.shard_map(
        per_device, mesh=mesh, in_specs=in_specs, out_specs=out_specs, check_vma=False
    )
```

```python
import math

import jax
import jax.numpy as jnp
import numpy as np
from jax import lax
from jax.experimental import pallas as pl
from jax.sharding import PartitionSpec as P

SUB = 2
OSTEPS = 2


visc_coef = 0.01
diff_coef = 0.2
wind_coef = 0.1
surf_coef = 0.2


def neighbour(values, step_x, step_y):
    count_x, count_y = lax.axis_size("gx"), lax.axis_size("gy")
    if step_y == 0:
        return lax.ppermute(values, "gx", [(i, (i + step_x) % count_x) for i in range(count_x)])
    if step_x == 0:
        return lax.ppermute(values, "gy", [(j, (j + step_y) % count_y) for j in range(count_y)])
    pairs = [
        (i * count_y + j, ((i + step_x) % count_x) * count_y + (j + step_y) % count_y)
        for i in range(count_x)
        for j in range(count_y)
    ]
    return lax.ppermute(values, ("gx", "gy"), pairs)


def shifted(values, before, after, axis):
    size = values.shape[axis]
    layout = [1] * values.ndim
    layout[axis] = size
    position = jnp.arange(size).reshape(layout)
    prev = jnp.concatenate([lax.slice_in_dim(values, 0, 1, axis=axis), lax.slice_in_dim(values, 0, size - 1, axis=axis)], axis=axis)
    nxt = jnp.concatenate([lax.slice_in_dim(values, 1, size, axis=axis), lax.slice_in_dim(values, size - 1, size, axis=axis)], axis=axis)
    prev = jnp.where(position == 0, jnp.broadcast_to(before, values.shape), prev)
    nxt = jnp.where(position == size - 1, jnp.broadcast_to(after, values.shape), nxt)
    return prev, nxt


def packed(values):
    if values.size % 128:
        return values
    return values.reshape(-1, 128)


def exchange(values, step_x, step_y):
    return neighbour(packed(values), step_x, step_y).reshape(values.shape)


def pair_matrix(size):
    position = np.arange(size)
    starts = position[position % 4 == 0][1:]
    ends = position[position % 4 == 3][:-1]
    pair = np.eye(size)
    pair[starts - 1, starts] = 1.0
    pair[ends + 1, ends] = 1.0
    return pair


def substep(state_in, metric, derivative_np, weights_np, inv_mass):
    levels, xsize, ysize = state_in.shape
    precision = lax.Precision.HIGH
    block_x = np.kron(np.eye(xsize // 4), derivative_np)
    block_y = np.kron(np.eye(ysize // 4), derivative_np)
    weight_x = np.tile(weights_np, xsize // 4)
    weight_y = np.tile(weights_np, ysize // 4)
    pair_y = pair_matrix(ysize)
    term_x_right = jnp.asarray(weight_y[:, None] * pair_y, jnp.float32)
    term_y_right = jnp.asarray(block_y @ pair_y, jnp.float32)
    pair_x = jnp.asarray(pair_matrix(xsize).T, jnp.float32)
    block_x = jnp.asarray(block_x, jnp.float32)
    along_x = jnp.einsum("ab,lby->lay", block_x, state_in, precision=precision)
    scaled_x = jnp.asarray(weight_x[:, None], jnp.float32) * metric[0] * along_x
    term_x = jnp.einsum("ba,lby->lay", block_x, scaled_x, precision=precision)
    along_y = jnp.einsum("lxc,dc->lxd", state_in, jnp.asarray(block_y, jnp.float32), precision=precision)
    scaled_y = jnp.asarray(weight_y[None, :], jnp.float32) * metric[1] * along_y
    merged = jnp.einsum("lxc,cd->lxd", term_x, term_x_right, precision=precision) + jnp.einsum(
        "lxc,cd->lxd", scaled_y, term_y_right, precision=precision
    ) * jnp.asarray(weight_x[:, None], jnp.float32)
    last_x, last_y = xsize - 1, ysize - 1
    from_left = exchange(merged[:, :, last_y], 0, 1)[:, :, None]
    from_right = exchange(merged[:, :, 0], 0, -1)[:, :, None]
    column = jnp.arange(ysize)
    merged = merged + jnp.where(column == 0, from_left, jnp.where(column == last_y, from_right, 0.0))
    from_up = exchange(merged[:, last_x, :], 1, 0)[:, None, :]
    from_down = exchange(merged[:, 0, :], -1, 0)[:, None, :]
    row = jnp.arange(xsize)[:, None]
    total = jnp.einsum("ab,lby->lay", pair_x, merged, precision=precision) + jnp.where(
        row == 0, from_up, jnp.where(row == last_x, from_down, 0.0)
    )
    return state_in - visc_coef * total * inv_mass


def tracer_step(tracers, velocity):
    xsize, ysize = tracers.shape[-2], tracers.shape[-1]
    last_x, last_y = xsize - 1, ysize - 1
    precision = lax.Precision.HIGH
    from_up = exchange(tracers[..., last_x, :], 1, 0)[..., None, :]
    from_down = exchange(tracers[..., 0, :], -1, 0)[..., None, :]
    from_left = exchange(tracers[..., last_y], 0, 1)[..., None]
    from_right = exchange(tracers[..., 0], 0, -1)[..., None]
    above_x = np.eye(xsize, k=1)
    above_y = np.eye(ysize, k=1)
    sum_x = jnp.asarray(above_x + above_x.T, jnp.float32)
    diff_x = jnp.asarray(above_x - above_x.T, jnp.float32)
    sum_y = jnp.asarray(above_y + above_y.T, jnp.float32)
    diff_y = jnp.asarray(above_y.T - above_y, jnp.float32)
    row = jnp.arange(xsize)[:, None]
    column = jnp.arange(ysize)
    east = jnp.where(row == last_x, from_down, 0.0)
    west = jnp.where(row == 0, from_up, 0.0)
    north = jnp.where(column == last_y, from_right, 0.0)
    south = jnp.where(column == 0, from_left, 0.0)
    across_x = jnp.einsum("ab,...by->...ay", sum_x, tracers, precision=precision) + (east + west)
    slope_x = jnp.einsum("ab,...by->...ay", diff_x, tracers, precision=precision) + (east - west)
    across_y = jnp.einsum("...xc,cd->...xd", tracers, sum_y, precision=precision) + (north + south)
    slope_y = jnp.einsum("...xc,cd->...xd", tracers, diff_y, precision=precision) + (north - south)
    return (
        tracers
        + diff_coef * (across_x + across_y - 4.0 * tracers)
        - 0.5 * velocity[0] * slope_x
        - 0.5 * velocity[1] * slope_y
    )


def gll_tables():
    points = np.array([-1.0, -1.0 / np.sqrt(5.0), 1.0 / np.sqrt(5.0), 1.0])
    weights = np.array([1.0 / 6.0, 5.0 / 6.0, 5.0 / 6.0, 1.0 / 6.0])
    derivative = np.zeros((4, 4))
    for target in range(4):
        for source in range(4):
            if target == source:
                derivative[target, source] = np.sum(
                    [
                        1.0 / (points[source] - points[others])
                        for others in range(4)
                        if others != source
                    ]
                )
            else:
                numer = np.prod(
                    [
                        points[target] - points[others]
                        for others in range(4)
                        if others != target and others != source
                    ]
                )
                denom = np.prod(
                    [points[source] - points[others] for others in range(4) if others != source]
                )
                derivative[target, source] = numer / denom
    massw = np.array([1.0 / 3.0, 5.0 / 6.0, 5.0 / 6.0, 1.0 / 3.0])
    return (derivative, weights, massw)


def mass_inverse(massw_np, xsize, ysize):
    return jnp.asarray(
        1.0 / (np.tile(massw_np, xsize // 4)[:, None] * np.tile(massw_np, ysize // 4)[None, :]),
        jnp.float32,
    )


def gather_kernel(index_ref, scale_ref, table_ref, out_ref):
    fields, rows, lanes = table_ref.shape
    tile = out_ref.shape[1]
    index = index_ref[...]
    onehot = (lax.broadcasted_iota(jnp.int32, (lanes, tile), 0) == (index % lanes)).astype(jnp.bfloat16)
    select = lax.broadcasted_iota(jnp.int32, (rows, tile), 0) == (index // lanes)
    rest = table_ref[...]
    parts = []
    for part in range(3):
        piece = rest.astype(jnp.bfloat16)
        rest = rest - piece.astype(jnp.float32)
        parts.append(piece)
    stacked = jnp.concatenate(parts, axis=2).reshape(fields * rows, 3 * lanes)
    picked = jnp.dot(stacked, jnp.concatenate([onehot] * 3, axis=0), preferred_element_type=jnp.float32)
    scale = scale_ref[...]
    values = jnp.concatenate(
        [jnp.sum(jnp.where(select, picked[f * rows : (f + 1) * rows], 0.0), axis=0, keepdims=True) for f in range(fields)],
        axis=0,
    ) * scale

    @pl.when(pl.program_id(1) == 0)
    def first():
        out_ref[...] = values

    @pl.when(pl.program_id(1) > 0)
    def rest_steps():
        out_ref[...] = out_ref[...] + values


def onehot_gather(table, index, scale, groups):
    fields, rows, lanes = table.shape
    flat = index.reshape(1, -1)
    count = flat.shape[1]
    width = count // groups
    tile = 128
    while tile < 2048 and width % (2 * tile) == 0 and fields * rows * tile * 8 <= 4 * 2**20:
        tile *= 2
    blocks = width // tile
    return pl.pallas_call(
        gather_kernel,
        grid=(blocks, groups),
        in_specs=[
            pl.BlockSpec((1, tile), lambda step, group: (0, group * blocks + step)),
            pl.BlockSpec((1, tile), lambda step, group: (0, group * blocks + step)),
            pl.BlockSpec((fields, rows, lanes), lambda step, group: (0, 0, 0)),
        ],
        out_specs=pl.BlockSpec((fields, tile), lambda step, group: (0, step)),
        out_shape=jax.ShapeDtypeStruct((fields, width), jnp.float32),
    )(flat, scale.reshape(1, -1), table)


def per_device(
    atm_state,
    metric,
    send_idx,
    send_counts,
    ocean_tracers,
    ocean_velocity,
    remap_slots,
    remap_weights,
):
    fields, levels, xlocal, ylocal = atm_state.shape
    derivative_np, weights_np, massw_np = gll_tables()
    state_now = atm_state.reshape(fields * levels, xlocal, ylocal)
    inv_mass = mass_inverse(massw_np, xlocal, ylocal)
    for repeat in range(SUB):
        state_now = substep(state_now, metric, derivative_np, weights_np, inv_mass)
    atm_out = state_now.reshape(fields, levels, xlocal, ylocal)
    bottom = atm_out[:, levels - 1]
    speed = jnp.sqrt(1.0 + bottom[0] * bottom[0] + bottom[1] * bottom[1])
    flux_flat = (bottom * speed).reshape(fields, xlocal * ylocal)
    node_total = xlocal * ylocal
    rank_total = send_idx.shape[1]
    slot_cap = send_idx.shape[2]
    count_row = send_counts[0]
    live_slots = (jnp.arange(slot_cap)[None, :] < count_row[:, None]).astype(jnp.float32)
    flux_table = flux_flat.reshape(fields, node_total // 128, 128)
    payload = onehot_gather(flux_table, send_idx[0], live_slots, 1).reshape(fields, rank_total, slot_cap)
    received = lax.all_to_all(payload, ("gx", "gy"), split_axis=1, concat_axis=1, tiled=True)
    source_count, ocean_x, ocean_y = remap_slots.shape
    ocean_flux = onehot_gather(received, remap_slots, remap_weights, source_count).reshape(fields, ocean_x, ocean_y)
    velocity = ocean_velocity.at[0, 0].add(wind_coef * jnp.tanh(ocean_flux[0]))
    velocity = velocity.at[1, 0].add(wind_coef * jnp.tanh(ocean_flux[1]))
    tracers = ocean_tracers.at[0, 0].add(surf_coef * ocean_flux[2])
    tracers = tracers.at[1, 0].add(surf_coef * ocean_flux[3])
    for repeat in range(OSTEPS):
        tracers = tracer_step(tracers, velocity)
    return (atm_out, tracers)


def solution(mesh):
    in_specs = (
        P(None, None, "gx", "gy"),
        P(None, "gx", "gy"),
        P(("gx", "gy"), None, None),
        P(("gx", "gy"), None),
        P(None, None, "gx", "gy"),
        P(None, None, "gx", "gy"),
        P(None, "gx", "gy"),
        P(None, "gx", "gy"),
    )
    out_specs = (P(None, None, "gx", "gy"), P(None, None, "gx", "gy"))
    return jax.shard_map(
        per_device, mesh=mesh, in_specs=in_specs, out_specs=out_specs, check_vma=False
    )
```

```python
import functools
import math

import jax
import jax.numpy as jnp
import numpy as np
from jax import lax
from jax.experimental import pallas as pl
from jax.sharding import PartitionSpec as P

SUB = 2
OSTEPS = 2


visc_coef = 0.01
diff_coef = 0.2
wind_coef = 0.1
surf_coef = 0.2


def neighbour(values, step_x, step_y):
    count_x, count_y = lax.axis_size("gx"), lax.axis_size("gy")
    if step_y == 0:
        return lax.ppermute(values, "gx", [(i, (i + step_x) % count_x) for i in range(count_x)])
    if step_x == 0:
        return lax.ppermute(values, "gy", [(j, (j + step_y) % count_y) for j in range(count_y)])
    pairs = [
        (i * count_y + j, ((i + step_x) % count_x) * count_y + (j + step_y) % count_y)
        for i in range(count_x)
        for j in range(count_y)
    ]
    return lax.ppermute(values, ("gx", "gy"), pairs)


def shifted(values, before, after, axis):
    size = values.shape[axis]
    layout = [1] * values.ndim
    layout[axis] = size
    position = jnp.arange(size).reshape(layout)
    prev = jnp.concatenate([lax.slice_in_dim(values, 0, 1, axis=axis), lax.slice_in_dim(values, 0, size - 1, axis=axis)], axis=axis)
    nxt = jnp.concatenate([lax.slice_in_dim(values, 1, size, axis=axis), lax.slice_in_dim(values, size - 1, size, axis=axis)], axis=axis)
    prev = jnp.where(position == 0, jnp.broadcast_to(before, values.shape), prev)
    nxt = jnp.where(position == size - 1, jnp.broadcast_to(after, values.shape), nxt)
    return prev, nxt


def packed(values):
    if values.size % 128:
        return values
    return values.reshape(-1, 128)


def exchange(values, step_x, step_y):
    return neighbour(packed(values), step_x, step_y).reshape(values.shape)


def pair_matrix(size):
    position = np.arange(size)
    starts = position[position % 4 == 0][1:]
    ends = position[position % 4 == 3][:-1]
    pair = np.eye(size)
    pair[starts - 1, starts] = 1.0
    pair[ends + 1, ends] = 1.0
    return pair


def substep(state_in, metric, derivative_np, weights_np, inv_mass):
    levels, xsize, ysize = state_in.shape
    precision = lax.Precision.HIGH
    block_x = np.kron(np.eye(xsize // 4), derivative_np)
    block_y = np.kron(np.eye(ysize // 4), derivative_np)
    weight_x = np.tile(weights_np, xsize // 4)
    weight_y = np.tile(weights_np, ysize // 4)
    pair_y = pair_matrix(ysize)
    term_x_right = jnp.asarray(weight_y[:, None] * pair_y, jnp.float32)
    term_y_right = jnp.asarray(block_y @ pair_y, jnp.float32)
    pair_x = jnp.asarray(pair_matrix(xsize).T, jnp.float32)
    block_x = jnp.asarray(block_x, jnp.float32)
    along_x = jnp.einsum("ab,lby->lay", block_x, state_in, precision=precision)
    scaled_x = jnp.asarray(weight_x[:, None], jnp.float32) * metric[0] * along_x
    term_x = jnp.einsum("ba,lby->lay", block_x, scaled_x, precision=precision)
    along_y = jnp.einsum("lxc,dc->lxd", state_in, jnp.asarray(block_y, jnp.float32), precision=precision)
    scaled_y = jnp.asarray(weight_y[None, :], jnp.float32) * metric[1] * along_y
    merged = jnp.einsum("lxc,cd->lxd", term_x, term_x_right, precision=precision) + jnp.einsum(
        "lxc,cd->lxd", scaled_y, term_y_right, precision=precision
    ) * jnp.asarray(weight_x[:, None], jnp.float32)
    last_x, last_y = xsize - 1, ysize - 1
    from_left = exchange(merged[:, :, last_y], 0, 1)[:, :, None]
    from_right = exchange(merged[:, :, 0], 0, -1)[:, :, None]
    column = jnp.arange(ysize)
    merged = merged + jnp.where(column == 0, from_left, jnp.where(column == last_y, from_right, 0.0))
    from_up = exchange(merged[:, last_x, :], 1, 0)[:, None, :]
    from_down = exchange(merged[:, 0, :], -1, 0)[:, None, :]
    row = jnp.arange(xsize)[:, None]
    total = jnp.einsum("ab,lby->lay", pair_x, merged, precision=precision) + jnp.where(
        row == 0, from_up, jnp.where(row == last_x, from_down, 0.0)
    )
    return state_in - visc_coef * total * inv_mass


def tracer_step(tracers, velocity):
    xsize, ysize = tracers.shape[-2], tracers.shape[-1]
    last_x, last_y = xsize - 1, ysize - 1
    precision = lax.Precision.HIGH
    from_up = exchange(tracers[..., last_x, :], 1, 0)[..., None, :]
    from_down = exchange(tracers[..., 0, :], -1, 0)[..., None, :]
    from_left = exchange(tracers[..., last_y], 0, 1)[..., None]
    from_right = exchange(tracers[..., 0], 0, -1)[..., None]
    above_x = np.eye(xsize, k=1)
    above_y = np.eye(ysize, k=1)
    sum_x = jnp.asarray(above_x + above_x.T, jnp.float32)
    diff_x = jnp.asarray(above_x - above_x.T, jnp.float32)
    sum_y = jnp.asarray(above_y + above_y.T, jnp.float32)
    diff_y = jnp.asarray(above_y.T - above_y, jnp.float32)
    row = jnp.arange(xsize)[:, None]
    column = jnp.arange(ysize)
    east = jnp.where(row == last_x, from_down, 0.0)
    west = jnp.where(row == 0, from_up, 0.0)
    north = jnp.where(column == last_y, from_right, 0.0)
    south = jnp.where(column == 0, from_left, 0.0)
    across_x = jnp.einsum("ab,...by->...ay", sum_x, tracers, precision=precision) + (east + west)
    slope_x = jnp.einsum("ab,...by->...ay", diff_x, tracers, precision=precision) + (east - west)
    across_y = jnp.einsum("...xc,cd->...xd", tracers, sum_y, precision=precision) + (north + south)
    slope_y = jnp.einsum("...xc,cd->...xd", tracers, diff_y, precision=precision) + (north - south)
    return (
        tracers
        + diff_coef * (across_x + across_y - 4.0 * tracers)
        - 0.5 * velocity[0] * slope_x
        - 0.5 * velocity[1] * slope_y
    )


def gll_tables():
    points = np.array([-1.0, -1.0 / np.sqrt(5.0), 1.0 / np.sqrt(5.0), 1.0])
    weights = np.array([1.0 / 6.0, 5.0 / 6.0, 5.0 / 6.0, 1.0 / 6.0])
    derivative = np.zeros((4, 4))
    for target in range(4):
        for source in range(4):
            if target == source:
                derivative[target, source] = np.sum(
                    [
                        1.0 / (points[source] - points[others])
                        for others in range(4)
                        if others != source
                    ]
                )
            else:
                numer = np.prod(
                    [
                        points[target] - points[others]
                        for others in range(4)
                        if others != target and others != source
                    ]
                )
                denom = np.prod(
                    [points[source] - points[others] for others in range(4) if others != source]
                )
                derivative[target, source] = numer / denom
    massw = np.array([1.0 / 3.0, 5.0 / 6.0, 5.0 / 6.0, 1.0 / 3.0])
    return (derivative, weights, massw)


def mass_inverse(massw_np, xsize, ysize):
    return jnp.asarray(
        1.0 / (np.tile(massw_np, xsize // 4)[:, None] * np.tile(massw_np, ysize // 4)[None, :]),
        jnp.float32,
    )


def gather_kernel(index_ref, scale_ref, table_ref, out_ref, surface=False):
    fields, rows, lanes = table_ref.shape[0], table_ref.shape[-2], table_ref.shape[-1]
    tile = out_ref.shape[1]
    index = index_ref[...]
    onehot = (lax.broadcasted_iota(jnp.int32, (lanes, tile), 0) == (index % lanes)).astype(jnp.bfloat16)
    select = lax.broadcasted_iota(jnp.int32, (rows, tile), 0) == (index // lanes)
    if surface:
        bottom = table_ref[:, 0]
        rest = bottom * jnp.sqrt(1.0 + bottom[0] * bottom[0] + bottom[1] * bottom[1])
    else:
        rest = table_ref[...]
    parts = []
    for part in range(3):
        piece = rest.astype(jnp.bfloat16)
        rest = rest - piece.astype(jnp.float32)
        parts.append(piece)
    stacked = jnp.concatenate(parts, axis=2).reshape(fields * rows, 3 * lanes)
    picked = jnp.dot(stacked, jnp.concatenate([onehot] * 3, axis=0), preferred_element_type=jnp.float32)
    scale = scale_ref[...]
    values = jnp.concatenate(
        [jnp.sum(jnp.where(select, picked[f * rows : (f + 1) * rows], 0.0), axis=0, keepdims=True) for f in range(fields)],
        axis=0,
    ) * scale

    @pl.when(pl.program_id(1) == 0)
    def first():
        out_ref[...] = values

    @pl.when(pl.program_id(1) > 0)
    def rest_steps():
        out_ref[...] = out_ref[...] + values


def onehot_gather(table, index, scale, groups, level=None):
    fields, rows, lanes = table.shape[0], table.shape[-2], table.shape[-1]
    if level is None:
        table_spec = pl.BlockSpec((fields, rows, lanes), lambda step, group: (0, 0, 0))
    else:
        table_spec = pl.BlockSpec((fields, 1, rows, lanes), lambda step, group: (0, level, 0, 0))
    flat = index.reshape(1, -1)
    count = flat.shape[1]
    width = count // groups
    tile = 128
    while tile < 2048 and width % (2 * tile) == 0 and fields * rows * tile * 8 <= 4 * 2**20:
        tile *= 2
    blocks = width // tile
    return pl.pallas_call(
        functools.partial(gather_kernel, surface=level is not None),
        grid=(blocks, groups),
        in_specs=[
            pl.BlockSpec((1, tile), lambda step, group: (0, group * blocks + step)),
            pl.BlockSpec((1, tile), lambda step, group: (0, group * blocks + step)),
            table_spec,
        ],
        out_specs=pl.BlockSpec((fields, tile), lambda step, group: (0, step)),
        out_shape=jax.ShapeDtypeStruct((fields, width), jnp.float32),
    )(flat, scale.reshape(1, -1), table)


def per_device(
    atm_state,
    metric,
    send_idx,
    send_counts,
    ocean_tracers,
    ocean_velocity,
    remap_slots,
    remap_weights,
):
    fields, levels, xlocal, ylocal = atm_state.shape
    derivative_np, weights_np, massw_np = gll_tables()
    state_now = atm_state.reshape(fields * levels, xlocal, ylocal)
    inv_mass = mass_inverse(massw_np, xlocal, ylocal)
    for repeat in range(SUB):
        state_now = substep(state_now, metric, derivative_np, weights_np, inv_mass)
    atm_out = state_now.reshape(fields, levels, xlocal, ylocal)
    rank_total = send_idx.shape[1]
    slot_cap = send_idx.shape[2]
    count_row = send_counts[0]
    live_slots = (jnp.arange(slot_cap)[None, :] < count_row[:, None]).astype(jnp.float32)
    payload = onehot_gather(atm_out, send_idx[0], live_slots, 1, levels - 1).reshape(fields, rank_total, slot_cap)
    received = lax.all_to_all(payload, ("gx", "gy"), split_axis=1, concat_axis=1, tiled=True)
    source_count, ocean_x, ocean_y = remap_slots.shape
    ocean_flux = onehot_gather(received, remap_slots, remap_weights, source_count).reshape(fields, ocean_x, ocean_y)
    velocity = ocean_velocity.at[0, 0].add(wind_coef * jnp.tanh(ocean_flux[0]))
    velocity = velocity.at[1, 0].add(wind_coef * jnp.tanh(ocean_flux[1]))
    tracers = ocean_tracers.at[0, 0].add(surf_coef * ocean_flux[2])
    tracers = tracers.at[1, 0].add(surf_coef * ocean_flux[3])
    for repeat in range(OSTEPS):
        tracers = tracer_step(tracers, velocity)
    return (atm_out, tracers)


def solution(mesh):
    in_specs = (
        P(None, None, "gx", "gy"),
        P(None, "gx", "gy"),
        P(("gx", "gy"), None, None),
        P(("gx", "gy"), None),
        P(None, None, "gx", "gy"),
        P(None, None, "gx", "gy"),
        P(None, "gx", "gy"),
        P(None, "gx", "gy"),
    )
    out_specs = (P(None, None, "gx", "gy"), P(None, None, "gx", "gy"))
    return jax.shard_map(
        per_device, mesh=mesh, in_specs=in_specs, out_specs=out_specs, check_vma=False
    )
```

```python
import math

import jax
import jax.numpy as jnp
import numpy as np
from jax import lax
from jax.experimental import pallas as pl
from jax.sharding import PartitionSpec as P

SUB = 2
OSTEPS = 2


visc_coef = 0.01
diff_coef = 0.2
wind_coef = 0.1
surf_coef = 0.2


def neighbour(values, step_x, step_y):
    count_x, count_y = lax.axis_size("gx"), lax.axis_size("gy")
    if step_y == 0:
        return lax.ppermute(values, "gx", [(i, (i + step_x) % count_x) for i in range(count_x)])
    if step_x == 0:
        return lax.ppermute(values, "gy", [(j, (j + step_y) % count_y) for j in range(count_y)])
    pairs = [
        (i * count_y + j, ((i + step_x) % count_x) * count_y + (j + step_y) % count_y)
        for i in range(count_x)
        for j in range(count_y)
    ]
    return lax.ppermute(values, ("gx", "gy"), pairs)


def shifted(values, before, after, axis):
    size = values.shape[axis]
    layout = [1] * values.ndim
    layout[axis] = size
    position = jnp.arange(size).reshape(layout)
    prev = jnp.concatenate([lax.slice_in_dim(values, 0, 1, axis=axis), lax.slice_in_dim(values, 0, size - 1, axis=axis)], axis=axis)
    nxt = jnp.concatenate([lax.slice_in_dim(values, 1, size, axis=axis), lax.slice_in_dim(values, size - 1, size, axis=axis)], axis=axis)
    prev = jnp.where(position == 0, jnp.broadcast_to(before, values.shape), prev)
    nxt = jnp.where(position == size - 1, jnp.broadcast_to(after, values.shape), nxt)
    return prev, nxt


def packed(values):
    if values.size % 128:
        return values
    return values.reshape(-1, 128)


def exchange(values, step_x, step_y):
    return neighbour(packed(values), step_x, step_y).reshape(values.shape)


def pair_matrix(size):
    position = np.arange(size)
    starts = position[position % 4 == 0][1:]
    ends = position[position % 4 == 3][:-1]
    pair = np.eye(size)
    pair[starts - 1, starts] = 1.0
    pair[ends + 1, ends] = 1.0
    return pair


def substep(state_in, metric, derivative_np, weights_np, inv_mass):
    levels, xsize, ysize = state_in.shape
    precision = lax.Precision.HIGH
    block_x = np.kron(np.eye(xsize // 4), derivative_np)
    block_y = np.kron(np.eye(ysize // 4), derivative_np)
    weight_x = np.tile(weights_np, xsize // 4)
    weight_y = np.tile(weights_np, ysize // 4)
    pair_y = pair_matrix(ysize)
    term_x_right = jnp.asarray(weight_y[:, None] * pair_y, jnp.float32)
    term_y_right = jnp.asarray(block_y @ pair_y, jnp.float32)
    pair_x = jnp.asarray(pair_matrix(xsize).T, jnp.float32)
    block_x = jnp.asarray(block_x, jnp.float32)
    along_x = jnp.einsum("ab,lby->lay", block_x, state_in, precision=precision)
    scaled_x = jnp.asarray(weight_x[:, None], jnp.float32) * metric[0] * along_x
    term_x = jnp.einsum("ba,lby->lay", block_x, scaled_x, precision=precision)
    along_y = jnp.einsum("lxc,dc->lxd", state_in, jnp.asarray(block_y, jnp.float32), precision=precision)
    scaled_y = jnp.asarray(weight_y[None, :], jnp.float32) * metric[1] * along_y
    merged = jnp.einsum("lxc,cd->lxd", term_x, term_x_right, precision=precision) + jnp.einsum(
        "lxc,cd->lxd", scaled_y, term_y_right, precision=precision
    ) * jnp.asarray(weight_x[:, None], jnp.float32)
    last_x, last_y = xsize - 1, ysize - 1
    from_left = exchange(merged[:, :, last_y], 0, 1)[:, :, None]
    from_right = exchange(merged[:, :, 0], 0, -1)[:, :, None]
    column = jnp.arange(ysize)
    merged = merged + jnp.where(column == 0, from_left, jnp.where(column == last_y, from_right, 0.0))
    from_up = exchange(merged[:, last_x, :], 1, 0)[:, None, :]
    from_down = exchange(merged[:, 0, :], -1, 0)[:, None, :]
    row = jnp.arange(xsize)[:, None]
    total = jnp.einsum("ab,lby->lay", pair_x, merged, precision=precision) + jnp.where(
        row == 0, from_up, jnp.where(row == last_x, from_down, 0.0)
    )
    return state_in - visc_coef * total * inv_mass


def tracer_step(tracers, velocity):
    xsize, ysize = tracers.shape[-2], tracers.shape[-1]
    last_x, last_y = xsize - 1, ysize - 1
    precision = lax.Precision.HIGH
    from_up = exchange(tracers[..., last_x, :], 1, 0)[..., None, :]
    from_down = exchange(tracers[..., 0, :], -1, 0)[..., None, :]
    from_left = exchange(tracers[..., last_y], 0, 1)[..., None]
    from_right = exchange(tracers[..., 0], 0, -1)[..., None]
    above_x = np.eye(xsize, k=1)
    above_y = np.eye(ysize, k=1)
    sum_x = jnp.asarray(above_x + above_x.T, jnp.float32)
    diff_x = jnp.asarray(above_x - above_x.T, jnp.float32)
    sum_y = jnp.asarray(above_y + above_y.T, jnp.float32)
    diff_y = jnp.asarray(above_y.T - above_y, jnp.float32)
    row = jnp.arange(xsize)[:, None]
    column = jnp.arange(ysize)
    east = jnp.where(row == last_x, from_down, 0.0)
    west = jnp.where(row == 0, from_up, 0.0)
    north = jnp.where(column == last_y, from_right, 0.0)
    south = jnp.where(column == 0, from_left, 0.0)
    both_x = jnp.einsum("ab,...by->...ay", jnp.concatenate([sum_x, diff_x], axis=0), tracers, precision=precision)
    both_y = jnp.einsum("...xc,cd->...xd", tracers, jnp.concatenate([sum_y, diff_y], axis=1), precision=precision)
    across_x = both_x[..., :xsize, :] + (east + west)
    slope_x = both_x[..., xsize:, :] + (east - west)
    across_y = both_y[..., :ysize] + (north + south)
    slope_y = both_y[..., ysize:] + (north - south)
    return (
        tracers
        + diff_coef * (across_x + across_y - 4.0 * tracers)
        - 0.5 * velocity[0] * slope_x
        - 0.5 * velocity[1] * slope_y
    )


def gll_tables():
    points = np.array([-1.0, -1.0 / np.sqrt(5.0), 1.0 / np.sqrt(5.0), 1.0])
    weights = np.array([1.0 / 6.0, 5.0 / 6.0, 5.0 / 6.0, 1.0 / 6.0])
    derivative = np.zeros((4, 4))
    for target in range(4):
        for source in range(4):
            if target == source:
                derivative[target, source] = np.sum(
                    [
                        1.0 / (points[source] - points[others])
                        for others in range(4)
                        if others != source
                    ]
                )
            else:
                numer = np.prod(
                    [
                        points[target] - points[others]
                        for others in range(4)
                        if others != target and others != source
                    ]
                )
                denom = np.prod(
                    [points[source] - points[others] for others in range(4) if others != source]
                )
                derivative[target, source] = numer / denom
    massw = np.array([1.0 / 3.0, 5.0 / 6.0, 5.0 / 6.0, 1.0 / 3.0])
    return (derivative, weights, massw)


def mass_inverse(massw_np, xsize, ysize):
    return jnp.asarray(
        1.0 / (np.tile(massw_np, xsize // 4)[:, None] * np.tile(massw_np, ysize // 4)[None, :]),
        jnp.float32,
    )


def gather_kernel(index_ref, scale_ref, table_ref, out_ref):
    fields, rows, lanes = table_ref.shape
    tile = out_ref.shape[1]
    index = index_ref[...]
    onehot = (lax.broadcasted_iota(jnp.int32, (lanes, tile), 0) == (index % lanes)).astype(jnp.bfloat16)
    select = lax.broadcasted_iota(jnp.int32, (rows, tile), 0) == (index // lanes)
    rest = table_ref[...]
    parts = []
    for part in range(3):
        piece = rest.astype(jnp.bfloat16)
        rest = rest - piece.astype(jnp.float32)
        parts.append(piece)
    stacked = jnp.concatenate(parts, axis=2).reshape(fields * rows, 3 * lanes)
    picked = jnp.dot(stacked, jnp.concatenate([onehot] * 3, axis=0), preferred_element_type=jnp.float32)
    scale = scale_ref[...]
    values = jnp.concatenate(
        [jnp.sum(jnp.where(select, picked[f * rows : (f + 1) * rows], 0.0), axis=0, keepdims=True) for f in range(fields)],
        axis=0,
    ) * scale

    @pl.when(pl.program_id(1) == 0)
    def first():
        out_ref[...] = values

    @pl.when(pl.program_id(1) > 0)
    def rest_steps():
        out_ref[...] = out_ref[...] + values


def onehot_gather(table, index, scale, groups):
    fields, rows, lanes = table.shape
    flat = index.reshape(1, -1)
    count = flat.shape[1]
    width = count // groups
    tile = 128
    while tile < 2048 and width % (2 * tile) == 0 and fields * rows * tile * 8 <= 4 * 2**20:
        tile *= 2
    blocks = width // tile
    return pl.pallas_call(
        gather_kernel,
        grid=(blocks, groups),
        in_specs=[
            pl.BlockSpec((1, tile), lambda step, group: (0, group * blocks + step)),
            pl.BlockSpec((1, tile), lambda step, group: (0, group * blocks + step)),
            pl.BlockSpec((fields, rows, lanes), lambda step, group: (0, 0, 0)),
        ],
        out_specs=pl.BlockSpec((fields, tile), lambda step, group: (0, step)),
        out_shape=jax.ShapeDtypeStruct((fields, width), jnp.float32),
    )(flat, scale.reshape(1, -1), table)


def per_device(
    atm_state,
    metric,
    send_idx,
    send_counts,
    ocean_tracers,
    ocean_velocity,
    remap_slots,
    remap_weights,
):
    fields, levels, xlocal, ylocal = atm_state.shape
    derivative_np, weights_np, massw_np = gll_tables()
    state_now = atm_state.reshape(fields * levels, xlocal, ylocal)
    inv_mass = mass_inverse(massw_np, xlocal, ylocal)
    for repeat in range(SUB):
        state_now = substep(state_now, metric, derivative_np, weights_np, inv_mass)
    atm_out = state_now.reshape(fields, levels, xlocal, ylocal)
    bottom = atm_out[:, levels - 1]
    speed = jnp.sqrt(1.0 + bottom[0] * bottom[0] + bottom[1] * bottom[1])
    flux_flat = (bottom * speed).reshape(fields, xlocal * ylocal)
    node_total = xlocal * ylocal
    rank_total = send_idx.shape[1]
    slot_cap = send_idx.shape[2]
    count_row = send_counts[0]
    live_slots = (jnp.arange(slot_cap)[None, :] < count_row[:, None]).astype(jnp.float32)
    flux_table = flux_flat.reshape(fields, node_total // 128, 128)
    payload = onehot_gather(flux_table, send_idx[0], live_slots, 1).reshape(fields, rank_total, slot_cap)
    received = lax.all_to_all(payload, ("gx", "gy"), split_axis=1, concat_axis=1, tiled=True)
    source_count, ocean_x, ocean_y = remap_slots.shape
    ocean_flux = onehot_gather(received, remap_slots, remap_weights, source_count).reshape(fields, ocean_x, ocean_y)
    velocity = ocean_velocity.at[0, 0].add(wind_coef * jnp.tanh(ocean_flux[0]))
    velocity = velocity.at[1, 0].add(wind_coef * jnp.tanh(ocean_flux[1]))
    tracers = ocean_tracers.at[0, 0].add(surf_coef * ocean_flux[2])
    tracers = tracers.at[1, 0].add(surf_coef * ocean_flux[3])
    for repeat in range(OSTEPS):
        tracers = tracer_step(tracers, velocity)
    return (atm_out, tracers)


def solution(mesh):
    in_specs = (
        P(None, None, "gx", "gy"),
        P(None, "gx", "gy"),
        P(("gx", "gy"), None, None),
        P(("gx", "gy"), None),
        P(None, None, "gx", "gy"),
        P(None, None, "gx", "gy"),
        P(None, "gx", "gy"),
        P(None, "gx", "gy"),
    )
    out_specs = (P(None, None, "gx", "gy"), P(None, None, "gx", "gy"))
    return jax.shard_map(
        per_device, mesh=mesh, in_specs=in_specs, out_specs=out_specs, check_vma=False
    )
```

```python
import math

import jax
import jax.numpy as jnp
import numpy as np
from jax import lax
from jax.experimental import pallas as pl
from jax.sharding import PartitionSpec as P

SUB = 2
OSTEPS = 2


visc_coef = 0.01
diff_coef = 0.2
wind_coef = 0.1
surf_coef = 0.2


def neighbour(values, step_x, step_y):
    count_x, count_y = lax.axis_size("gx"), lax.axis_size("gy")
    if step_y == 0:
        return lax.ppermute(values, "gx", [(i, (i + step_x) % count_x) for i in range(count_x)])
    if step_x == 0:
        return lax.ppermute(values, "gy", [(j, (j + step_y) % count_y) for j in range(count_y)])
    pairs = [
        (i * count_y + j, ((i + step_x) % count_x) * count_y + (j + step_y) % count_y)
        for i in range(count_x)
        for j in range(count_y)
    ]
    return lax.ppermute(values, ("gx", "gy"), pairs)


def shifted(values, before, after, axis):
    size = values.shape[axis]
    layout = [1] * values.ndim
    layout[axis] = size
    position = jnp.arange(size).reshape(layout)
    prev = jnp.concatenate([lax.slice_in_dim(values, 0, 1, axis=axis), lax.slice_in_dim(values, 0, size - 1, axis=axis)], axis=axis)
    nxt = jnp.concatenate([lax.slice_in_dim(values, 1, size, axis=axis), lax.slice_in_dim(values, size - 1, size, axis=axis)], axis=axis)
    prev = jnp.where(position == 0, jnp.broadcast_to(before, values.shape), prev)
    nxt = jnp.where(position == size - 1, jnp.broadcast_to(after, values.shape), nxt)
    return prev, nxt


def packed(values):
    if values.size % 128:
        return values
    return values.reshape(-1, 128)


def exchange(values, step_x, step_y):
    return neighbour(packed(values), step_x, step_y).reshape(values.shape)


def pair_matrix(size):
    position = np.arange(size)
    starts = position[position % 4 == 0][1:]
    ends = position[position % 4 == 3][:-1]
    pair = np.eye(size)
    pair[starts - 1, starts] = 1.0
    pair[ends + 1, ends] = 1.0
    return pair


def substep(state_in, metric, derivative_np, weights_np, inv_mass):
    levels, xsize, ysize = state_in.shape
    precision = lax.Precision.HIGH
    block_x = np.kron(np.eye(xsize // 4), derivative_np)
    block_y = np.kron(np.eye(ysize // 4), derivative_np)
    weight_x = np.tile(weights_np, xsize // 4)
    weight_y = np.tile(weights_np, ysize // 4)
    pair_y = pair_matrix(ysize)
    term_x_right = jnp.asarray(weight_y[:, None] * pair_y, jnp.float32)
    term_y_right = jnp.asarray(block_y @ pair_y, jnp.float32)
    pair_x = jnp.asarray(pair_matrix(xsize).T, jnp.float32)
    block_x = jnp.asarray(block_x, jnp.float32)
    along_x = jnp.einsum("ab,lby->lay", block_x, state_in, precision=precision)
    scaled_x = jnp.asarray(weight_x[:, None], jnp.float32) * metric[0] * along_x
    term_x = jnp.einsum("ba,lby->lay", block_x, scaled_x, precision=precision)
    along_y = jnp.einsum("lxc,dc->lxd", state_in, jnp.asarray(block_y, jnp.float32), precision=precision)
    scaled_y = jnp.asarray(weight_y[None, :], jnp.float32) * metric[1] * along_y
    merged = jnp.einsum("lxc,cd->lxd", term_x, term_x_right, precision=precision) + jnp.einsum(
        "lxc,cd->lxd", scaled_y, term_y_right, precision=precision
    ) * jnp.asarray(weight_x[:, None], jnp.float32)
    last_x, last_y = xsize - 1, ysize - 1
    from_left = exchange(merged[:, :, last_y], 0, 1)[:, :, None]
    from_right = exchange(merged[:, :, 0], 0, -1)[:, :, None]
    column = jnp.arange(ysize)
    merged = merged + jnp.where(column == 0, from_left, jnp.where(column == last_y, from_right, 0.0))
    from_up = exchange(merged[:, last_x, :], 1, 0)[:, None, :]
    from_down = exchange(merged[:, 0, :], -1, 0)[:, None, :]
    row = jnp.arange(xsize)[:, None]
    total = jnp.einsum("ab,lby->lay", pair_x, merged, precision=precision) + jnp.where(
        row == 0, from_up, jnp.where(row == last_x, from_down, 0.0)
    )
    return state_in - visc_coef * total * inv_mass


def tracer_step(tracers, velocity):
    xsize, ysize = tracers.shape[-2], tracers.shape[-1]
    last_x, last_y = xsize - 1, ysize - 1
    precision = lax.Precision.HIGH
    from_up = exchange(tracers[..., last_x, :], 1, 0)[..., None, :]
    from_down = exchange(tracers[..., 0, :], -1, 0)[..., None, :]
    from_left = exchange(tracers[..., last_y], 0, 1)[..., None]
    from_right = exchange(tracers[..., 0], 0, -1)[..., None]
    above_x = np.eye(xsize, k=1)
    above_y = np.eye(ysize, k=1)
    sum_x = jnp.asarray(above_x + above_x.T, jnp.float32)
    diff_x = jnp.asarray(above_x - above_x.T, jnp.float32)
    sum_y = jnp.asarray(above_y + above_y.T, jnp.float32)
    diff_y = jnp.asarray(above_y.T - above_y, jnp.float32)
    row = jnp.arange(xsize)[:, None]
    column = jnp.arange(ysize)
    east = jnp.where(row == last_x, from_down, 0.0)
    west = jnp.where(row == 0, from_up, 0.0)
    north = jnp.where(column == last_y, from_right, 0.0)
    south = jnp.where(column == 0, from_left, 0.0)
    across_x = jnp.einsum("ab,...by->...ay", sum_x, tracers, precision=precision) + (east + west)
    slope_x = jnp.einsum("ab,...by->...ay", diff_x, tracers, precision=precision) + (east - west)
    across_y = jnp.einsum("...xc,cd->...xd", tracers, sum_y, precision=precision) + (north + south)
    slope_y = jnp.einsum("...xc,cd->...xd", tracers, diff_y, precision=precision) + (north - south)
    return (
        tracers
        + diff_coef * (across_x + across_y - 4.0 * tracers)
        - 0.5 * velocity[0] * slope_x
        - 0.5 * velocity[1] * slope_y
    )


def gll_tables():
    points = np.array([-1.0, -1.0 / np.sqrt(5.0), 1.0 / np.sqrt(5.0), 1.0])
    weights = np.array([1.0 / 6.0, 5.0 / 6.0, 5.0 / 6.0, 1.0 / 6.0])
    derivative = np.zeros((4, 4))
    for target in range(4):
        for source in range(4):
            if target == source:
                derivative[target, source] = np.sum(
                    [
                        1.0 / (points[source] - points[others])
                        for others in range(4)
                        if others != source
                    ]
                )
            else:
                numer = np.prod(
                    [
                        points[target] - points[others]
                        for others in range(4)
                        if others != target and others != source
                    ]
                )
                denom = np.prod(
                    [points[source] - points[others] for others in range(4) if others != source]
                )
                derivative[target, source] = numer / denom
    massw = np.array([1.0 / 3.0, 5.0 / 6.0, 5.0 / 6.0, 1.0 / 3.0])
    return (derivative, weights, massw)


def mass_inverse(massw_np, xsize, ysize):
    return jnp.asarray(
        1.0 / (np.tile(massw_np, xsize // 4)[:, None] * np.tile(massw_np, ysize // 4)[None, :]),
        jnp.float32,
    )


def gather_kernel(index_ref, scale_ref, table_ref, out_ref):
    fields, rows, lanes = table_ref.shape
    tile = out_ref.shape[1]
    index = index_ref[...]
    onehot = (lax.broadcasted_iota(jnp.int32, (lanes, tile), 0) == (index % lanes)).astype(jnp.bfloat16)
    select = lax.broadcasted_iota(jnp.int32, (rows, tile), 0) == (index // lanes)
    rest = table_ref[...]
    parts = []
    for part in range(3):
        piece = rest.astype(jnp.bfloat16)
        rest = rest - piece.astype(jnp.float32)
        parts.append(piece)
    stacked = jnp.concatenate(parts, axis=2).reshape(fields * rows, 3 * lanes)
    picked = jnp.dot(stacked, jnp.concatenate([onehot] * 3, axis=0), preferred_element_type=jnp.float32)
    scale = scale_ref[...]
    values = jnp.concatenate(
        [jnp.sum(jnp.where(select, picked[f * rows : (f + 1) * rows], 0.0), axis=0, keepdims=True) for f in range(fields)],
        axis=0,
    ) * scale

    @pl.when(pl.program_id(1) == 0)
    def first():
        out_ref[...] = values

    @pl.when(pl.program_id(1) > 0)
    def rest_steps():
        out_ref[...] = out_ref[...] + values


def onehot_gather(table, index, scale, groups):
    fields, rows, lanes = table.shape
    flat = index.reshape(1, -1)
    count = flat.shape[1]
    width = count // groups
    tile = 128
    while tile < 2048 and width % (2 * tile) == 0 and fields * rows * tile * 8 <= 4 * 2**20:
        tile *= 2
    blocks = width // tile
    return pl.pallas_call(
        gather_kernel,
        grid=(blocks, groups),
        in_specs=[
            pl.BlockSpec((1, tile), lambda step, group: (0, group * blocks + step)),
            pl.BlockSpec((1, tile), lambda step, group: (0, group * blocks + step)),
            pl.BlockSpec((fields, rows, lanes), lambda step, group: (0, 0, 0)),
        ],
        out_specs=pl.BlockSpec((fields, tile), lambda step, group: (0, step)),
        out_shape=jax.ShapeDtypeStruct((fields, width), jnp.float32),
    )(flat, scale.reshape(1, -1), table)


def per_device(
    atm_state,
    metric,
    send_idx,
    send_counts,
    ocean_tracers,
    ocean_velocity,
    remap_slots,
    remap_weights,
):
    fields, levels, xlocal, ylocal = atm_state.shape
    derivative_np, weights_np, massw_np = gll_tables()
    state_now = atm_state.reshape(fields * levels, xlocal, ylocal)
    inv_mass = mass_inverse(massw_np, xlocal, ylocal)
    for repeat in range(SUB):
        state_now = substep(state_now, metric, derivative_np, weights_np, inv_mass)
    atm_out = state_now.reshape(fields, levels, xlocal, ylocal)
    bottom = atm_out[:, levels - 1]
    speed = jnp.sqrt(1.0 + bottom[0] * bottom[0] + bottom[1] * bottom[1])
    flux_flat = (bottom * speed).reshape(fields, xlocal * ylocal)
    node_total = xlocal * ylocal
    rank_total = send_idx.shape[1]
    slot_cap = send_idx.shape[2]
    count_row = send_counts[0]
    live_slots = (jnp.arange(slot_cap)[None, :] < count_row[:, None]).astype(jnp.float32)
    flux_table = flux_flat.reshape(fields, node_total // 128, 128)
    payload = onehot_gather(flux_table, send_idx[0], live_slots, 1).reshape(fields, rank_total, slot_cap)
    received = lax.all_to_all(payload, ("gx", "gy"), split_axis=1, concat_axis=1, tiled=True)
    source_count, ocean_x, ocean_y = remap_slots.shape
    ocean_flux = onehot_gather(received, remap_slots, remap_weights, source_count).reshape(fields, ocean_x, ocean_y)
    surface_level = (jnp.arange(ocean_velocity.shape[1]) == 0)[:, None, None]
    velocity = ocean_velocity + jnp.where(surface_level, wind_coef * jnp.tanh(ocean_flux[:2])[:, None], 0.0)
    tracers = ocean_tracers.at[0, 0].add(surf_coef * ocean_flux[2])
    tracers = tracers.at[1, 0].add(surf_coef * ocean_flux[3])
    for repeat in range(OSTEPS):
        tracers = tracer_step(tracers, velocity)
    return (atm_out, tracers)


def solution(mesh):
    in_specs = (
        P(None, None, "gx", "gy"),
        P(None, "gx", "gy"),
        P(("gx", "gy"), None, None),
        P(("gx", "gy"), None),
        P(None, None, "gx", "gy"),
        P(None, None, "gx", "gy"),
        P(None, "gx", "gy"),
        P(None, "gx", "gy"),
    )
    out_specs = (P(None, None, "gx", "gy"), P(None, None, "gx", "gy"))
    return jax.shard_map(
        per_device, mesh=mesh, in_specs=in_specs, out_specs=out_specs, check_vma=False
    )
```

```python
import math

import jax
import jax.numpy as jnp
import numpy as np
from jax import lax
from jax.experimental import pallas as pl
from jax.sharding import PartitionSpec as P

SUB = 2
OSTEPS = 2


visc_coef = 0.01
diff_coef = 0.2
wind_coef = 0.1
surf_coef = 0.2


def neighbour(values, step_x, step_y):
    count_x, count_y = lax.axis_size("gx"), lax.axis_size("gy")
    if step_y == 0:
        return lax.ppermute(values, "gx", [(i, (i + step_x) % count_x) for i in range(count_x)])
    if step_x == 0:
        return lax.ppermute(values, "gy", [(j, (j + step_y) % count_y) for j in range(count_y)])
    pairs = [
        (i * count_y + j, ((i + step_x) % count_x) * count_y + (j + step_y) % count_y)
        for i in range(count_x)
        for j in range(count_y)
    ]
    return lax.ppermute(values, ("gx", "gy"), pairs)


def shifted(values, before, after, axis):
    size = values.shape[axis]
    layout = [1] * values.ndim
    layout[axis] = size
    position = jnp.arange(size).reshape(layout)
    prev = jnp.concatenate([lax.slice_in_dim(values, 0, 1, axis=axis), lax.slice_in_dim(values, 0, size - 1, axis=axis)], axis=axis)
    nxt = jnp.concatenate([lax.slice_in_dim(values, 1, size, axis=axis), lax.slice_in_dim(values, size - 1, size, axis=axis)], axis=axis)
    prev = jnp.where(position == 0, jnp.broadcast_to(before, values.shape), prev)
    nxt = jnp.where(position == size - 1, jnp.broadcast_to(after, values.shape), nxt)
    return prev, nxt


def packed(values):
    if values.size % 128:
        return values
    return values.reshape(-1, 128)


def exchange(values, step_x, step_y):
    return neighbour(packed(values), step_x, step_y).reshape(values.shape)


def pair_matrix(size):
    position = np.arange(size)
    starts = position[position % 4 == 0][1:]
    ends = position[position % 4 == 3][:-1]
    pair = np.eye(size)
    pair[starts - 1, starts] = 1.0
    pair[ends + 1, ends] = 1.0
    return pair


def substep(state_in, metric, derivative_np, weights_np, inv_mass):
    levels, xsize, ysize = state_in.shape
    precision = lax.Precision.HIGH
    block_x = np.kron(np.eye(xsize // 4), derivative_np)
    block_y = np.kron(np.eye(ysize // 4), derivative_np)
    weight_x = np.tile(weights_np, xsize // 4)
    weight_y = np.tile(weights_np, ysize // 4)
    pair_y = pair_matrix(ysize)
    term_x_right = jnp.asarray(weight_y[:, None] * pair_y, jnp.float32)
    term_y_right = jnp.asarray(block_y @ pair_y, jnp.float32)
    pair_x = jnp.asarray(pair_matrix(xsize).T, jnp.float32)
    block_x = jnp.asarray(block_x, jnp.float32)
    along_x = jnp.einsum("ab,lby->lay", block_x, state_in, precision=precision)
    scaled_x = jnp.asarray(weight_x[:, None], jnp.float32) * metric[0] * along_x
    term_x = jnp.einsum("ba,lby->lay", block_x, scaled_x, precision=precision)
    along_y = jnp.einsum("lxc,dc->lxd", state_in, jnp.asarray(block_y, jnp.float32), precision=precision)
    scaled_y = jnp.asarray(weight_y[None, :], jnp.float32) * metric[1] * along_y
    merged = jnp.einsum("lxc,cd->lxd", term_x, term_x_right, precision=precision) + jnp.einsum(
        "lxc,cd->lxd", scaled_y, term_y_right, precision=precision
    ) * jnp.asarray(weight_x[:, None], jnp.float32)
    last_x, last_y = xsize - 1, ysize - 1
    from_left = exchange(merged[:, :, last_y], 0, 1)[:, :, None]
    from_right = exchange(merged[:, :, 0], 0, -1)[:, :, None]
    column = jnp.arange(ysize)
    merged = merged + jnp.where(column == 0, from_left, jnp.where(column == last_y, from_right, 0.0))
    from_up = exchange(merged[:, last_x, :], 1, 0)[:, None, :]
    from_down = exchange(merged[:, 0, :], -1, 0)[:, None, :]
    row = jnp.arange(xsize)[:, None]
    total = jnp.einsum("ab,lby->lay", pair_x, merged, precision=precision) + jnp.where(
        row == 0, from_up, jnp.where(row == last_x, from_down, 0.0)
    )
    return state_in - visc_coef * total * inv_mass


def tracer_step(tracers, velocity, edges=None):
    xsize, ysize = tracers.shape[-2], tracers.shape[-1]
    last_x, last_y = xsize - 1, ysize - 1
    precision = lax.Precision.HIGH
    if edges is None:
        edges = (tracers[..., last_x, :], tracers[..., 0, :], tracers[..., last_y], tracers[..., 0])
    from_up = exchange(edges[0], 1, 0)[..., None, :]
    from_down = exchange(edges[1], -1, 0)[..., None, :]
    from_left = exchange(edges[2], 0, 1)[..., None]
    from_right = exchange(edges[3], 0, -1)[..., None]
    above_x = np.eye(xsize, k=1)
    above_y = np.eye(ysize, k=1)
    sum_x = jnp.asarray(above_x + above_x.T, jnp.float32)
    diff_x = jnp.asarray(above_x - above_x.T, jnp.float32)
    sum_y = jnp.asarray(above_y + above_y.T, jnp.float32)
    diff_y = jnp.asarray(above_y.T - above_y, jnp.float32)
    row = jnp.arange(xsize)[:, None]
    column = jnp.arange(ysize)
    east = jnp.where(row == last_x, from_down, 0.0)
    west = jnp.where(row == 0, from_up, 0.0)
    north = jnp.where(column == last_y, from_right, 0.0)
    south = jnp.where(column == 0, from_left, 0.0)
    across_x = jnp.einsum("ab,...by->...ay", sum_x, tracers, precision=precision) + (east + west)
    slope_x = jnp.einsum("ab,...by->...ay", diff_x, tracers, precision=precision) + (east - west)
    across_y = jnp.einsum("...xc,cd->...xd", tracers, sum_y, precision=precision) + (north + south)
    slope_y = jnp.einsum("...xc,cd->...xd", tracers, diff_y, precision=precision) + (north - south)
    return (
        tracers
        + diff_coef * (across_x + across_y - 4.0 * tracers)
        - 0.5 * velocity[0] * slope_x
        - 0.5 * velocity[1] * slope_y
    )


def gll_tables():
    points = np.array([-1.0, -1.0 / np.sqrt(5.0), 1.0 / np.sqrt(5.0), 1.0])
    weights = np.array([1.0 / 6.0, 5.0 / 6.0, 5.0 / 6.0, 1.0 / 6.0])
    derivative = np.zeros((4, 4))
    for target in range(4):
        for source in range(4):
            if target == source:
                derivative[target, source] = np.sum(
                    [
                        1.0 / (points[source] - points[others])
                        for others in range(4)
                        if others != source
                    ]
                )
            else:
                numer = np.prod(
                    [
                        points[target] - points[others]
                        for others in range(4)
                        if others != target and others != source
                    ]
                )
                denom = np.prod(
                    [points[source] - points[others] for others in range(4) if others != source]
                )
                derivative[target, source] = numer / denom
    massw = np.array([1.0 / 3.0, 5.0 / 6.0, 5.0 / 6.0, 1.0 / 3.0])
    return (derivative, weights, massw)


def mass_inverse(massw_np, xsize, ysize):
    return jnp.asarray(
        1.0 / (np.tile(massw_np, xsize // 4)[:, None] * np.tile(massw_np, ysize // 4)[None, :]),
        jnp.float32,
    )


def gather_kernel(index_ref, scale_ref, table_ref, out_ref):
    fields, rows, lanes = table_ref.shape
    tile = out_ref.shape[1]
    index = index_ref[...]
    onehot = (lax.broadcasted_iota(jnp.int32, (lanes, tile), 0) == (index % lanes)).astype(jnp.bfloat16)
    select = lax.broadcasted_iota(jnp.int32, (rows, tile), 0) == (index // lanes)
    rest = table_ref[...]
    parts = []
    for part in range(3):
        piece = rest.astype(jnp.bfloat16)
        rest = rest - piece.astype(jnp.float32)
        parts.append(piece)
    stacked = jnp.concatenate(parts, axis=2).reshape(fields * rows, 3 * lanes)
    picked = jnp.dot(stacked, jnp.concatenate([onehot] * 3, axis=0), preferred_element_type=jnp.float32)
    scale = scale_ref[...]
    values = jnp.concatenate(
        [jnp.sum(jnp.where(select, picked[f * rows : (f + 1) * rows], 0.0), axis=0, keepdims=True) for f in range(fields)],
        axis=0,
    ) * scale

    @pl.when(pl.program_id(1) == 0)
    def first():
        out_ref[...] = values

    @pl.when(pl.program_id(1) > 0)
    def rest_steps():
        out_ref[...] = out_ref[...] + values


def onehot_gather(table, index, scale, groups):
    fields, rows, lanes = table.shape
    flat = index.reshape(1, -1)
    count = flat.shape[1]
    width = count // groups
    tile = 128
    while tile < 2048 and width % (2 * tile) == 0 and fields * rows * tile * 8 <= 4 * 2**20:
        tile *= 2
    blocks = width // tile
    return pl.pallas_call(
        gather_kernel,
        grid=(blocks, groups),
        in_specs=[
            pl.BlockSpec((1, tile), lambda step, group: (0, group * blocks + step)),
            pl.BlockSpec((1, tile), lambda step, group: (0, group * blocks + step)),
            pl.BlockSpec((fields, rows, lanes), lambda step, group: (0, 0, 0)),
        ],
        out_specs=pl.BlockSpec((fields, tile), lambda step, group: (0, step)),
        out_shape=jax.ShapeDtypeStruct((fields, width), jnp.float32),
    )(flat, scale.reshape(1, -1), table)


def per_device(
    atm_state,
    metric,
    send_idx,
    send_counts,
    ocean_tracers,
    ocean_velocity,
    remap_slots,
    remap_weights,
):
    fields, levels, xlocal, ylocal = atm_state.shape
    derivative_np, weights_np, massw_np = gll_tables()
    state_now = atm_state.reshape(fields * levels, xlocal, ylocal)
    inv_mass = mass_inverse(massw_np, xlocal, ylocal)
    for repeat in range(SUB):
        state_now = substep(state_now, metric, derivative_np, weights_np, inv_mass)
    atm_out = state_now.reshape(fields, levels, xlocal, ylocal)
    bottom = atm_out[:, levels - 1]
    speed = jnp.sqrt(1.0 + bottom[0] * bottom[0] + bottom[1] * bottom[1])
    flux_flat = (bottom * speed).reshape(fields, xlocal * ylocal)
    node_total = xlocal * ylocal
    rank_total = send_idx.shape[1]
    slot_cap = send_idx.shape[2]
    count_row = send_counts[0]
    live_slots = (jnp.arange(slot_cap)[None, :] < count_row[:, None]).astype(jnp.float32)
    flux_table = flux_flat.reshape(fields, node_total // 128, 128)
    payload = onehot_gather(flux_table, send_idx[0], live_slots, 1).reshape(fields, rank_total, slot_cap)
    received = lax.all_to_all(payload, ("gx", "gy"), split_axis=1, concat_axis=1, tiled=True)
    source_count, ocean_x, ocean_y = remap_slots.shape
    ocean_flux = onehot_gather(received, remap_slots, remap_weights, source_count).reshape(fields, ocean_x, ocean_y)
    velocity = ocean_velocity.at[0, 0].add(wind_coef * jnp.tanh(ocean_flux[0]))
    velocity = velocity.at[1, 0].add(wind_coef * jnp.tanh(ocean_flux[1]))
    surface = surf_coef * ocean_flux[2:]
    tracers = ocean_tracers.at[:, 0].add(surface)
    last_x, last_y = ocean_x - 1, ocean_y - 1
    edges = (
        ocean_tracers[..., last_x, :].at[:, 0].add(surface[:, last_x, :]),
        ocean_tracers[..., 0, :].at[:, 0].add(surface[:, 0, :]),
        ocean_tracers[..., last_y].at[:, 0].add(surface[:, :, last_y]),
        ocean_tracers[..., 0].at[:, 0].add(surface[:, :, 0]),
    )
    for repeat in range(OSTEPS):
        tracers = tracer_step(tracers, velocity, edges)
        edges = None
    return (atm_out, tracers)


def solution(mesh):
    in_specs = (
        P(None, None, "gx", "gy"),
        P(None, "gx", "gy"),
        P(("gx", "gy"), None, None),
        P(("gx", "gy"), None),
        P(None, None, "gx", "gy"),
        P(None, None, "gx", "gy"),
        P(None, "gx", "gy"),
        P(None, "gx", "gy"),
    )
    out_specs = (P(None, None, "gx", "gy"), P(None, None, "gx", "gy"))
    return jax.shard_map(
        per_device, mesh=mesh, in_specs=in_specs, out_specs=out_specs, check_vma=False
    )
```

```python
import math

import jax
import jax.numpy as jnp
import numpy as np
from jax import lax
from jax.experimental import pallas as pl
from jax.sharding import PartitionSpec as P

SUB = 2
OSTEPS = 2


visc_coef = 0.01
diff_coef = 0.2
wind_coef = 0.1
surf_coef = 0.2


def neighbour(values, step_x, step_y):
    count_x, count_y = lax.axis_size("gx"), lax.axis_size("gy")
    if step_y == 0:
        return lax.ppermute(values, "gx", [(i, (i + step_x) % count_x) for i in range(count_x)])
    if step_x == 0:
        return lax.ppermute(values, "gy", [(j, (j + step_y) % count_y) for j in range(count_y)])
    pairs = [
        (i * count_y + j, ((i + step_x) % count_x) * count_y + (j + step_y) % count_y)
        for i in range(count_x)
        for j in range(count_y)
    ]
    return lax.ppermute(values, ("gx", "gy"), pairs)


def shifted(values, before, after, axis):
    size = values.shape[axis]
    layout = [1] * values.ndim
    layout[axis] = size
    position = jnp.arange(size).reshape(layout)
    prev = jnp.concatenate([lax.slice_in_dim(values, 0, 1, axis=axis), lax.slice_in_dim(values, 0, size - 1, axis=axis)], axis=axis)
    nxt = jnp.concatenate([lax.slice_in_dim(values, 1, size, axis=axis), lax.slice_in_dim(values, size - 1, size, axis=axis)], axis=axis)
    prev = jnp.where(position == 0, jnp.broadcast_to(before, values.shape), prev)
    nxt = jnp.where(position == size - 1, jnp.broadcast_to(after, values.shape), nxt)
    return prev, nxt


def packed(values):
    if values.size % 128:
        return values
    return values.reshape(-1, 128)


def exchange(values, step_x, step_y):
    return neighbour(packed(values), step_x, step_y).reshape(values.shape)


def pair_matrix(size):
    position = np.arange(size)
    starts = position[position % 4 == 0][1:]
    ends = position[position % 4 == 3][:-1]
    pair = np.eye(size)
    pair[starts - 1, starts] = 1.0
    pair[ends + 1, ends] = 1.0
    return pair


def substep(state_in, metric, derivative_np, weights_np, inv_mass):
    levels, xsize, ysize = state_in.shape
    precision = lax.Precision.HIGH
    block_x = np.kron(np.eye(xsize // 4), derivative_np)
    block_y = np.kron(np.eye(ysize // 4), derivative_np)
    weight_x = np.tile(weights_np, xsize // 4)
    weight_y = np.tile(weights_np, ysize // 4)
    pair_y = pair_matrix(ysize)
    term_x_right = jnp.asarray(weight_y[:, None] * pair_y, jnp.float32)
    term_y_right = jnp.asarray(block_y @ pair_y, jnp.float32)
    pair_x = jnp.asarray(pair_matrix(xsize).T, jnp.float32)
    block_x = jnp.asarray(block_x, jnp.float32)
    along_x = jnp.einsum("ab,lby->lay", block_x, state_in, precision=precision)
    scaled_x = jnp.asarray(weight_x[:, None], jnp.float32) * metric[0] * along_x
    term_x = jnp.einsum("ba,lby->lay", block_x, scaled_x, precision=precision)
    along_y = jnp.einsum("lxc,dc->lxd", state_in, jnp.asarray(block_y, jnp.float32), precision=precision)
    scaled_y = jnp.asarray(weight_y[None, :], jnp.float32) * metric[1] * along_y
    merged = jnp.einsum("lxc,cd->lxd", term_x, term_x_right, precision=precision) + jnp.einsum(
        "lxc,cd->lxd", scaled_y, term_y_right, precision=precision
    ) * jnp.asarray(weight_x[:, None], jnp.float32)
    last_x, last_y = xsize - 1, ysize - 1
    from_left = exchange(merged[:, :, last_y], 0, 1)[:, :, None]
    from_right = exchange(merged[:, :, 0], 0, -1)[:, :, None]
    column = jnp.arange(ysize)
    edge_add = jnp.where(column == 0, from_left, jnp.where(column == last_y, from_right, 0.0))
    from_up = exchange(merged[:, last_x, :] + edge_add[:, last_x, :], 1, 0)[:, None, :]
    from_down = exchange(merged[:, 0, :] + edge_add[:, 0, :], -1, 0)[:, None, :]
    merged = merged + edge_add
    row = jnp.arange(xsize)[:, None]
    total = jnp.einsum("ab,lby->lay", pair_x, merged, precision=precision) + jnp.where(
        row == 0, from_up, jnp.where(row == last_x, from_down, 0.0)
    )
    return state_in - visc_coef * total * inv_mass


def tracer_step(tracers, velocity):
    xsize, ysize = tracers.shape[-2], tracers.shape[-1]
    last_x, last_y = xsize - 1, ysize - 1
    precision = lax.Precision.HIGH
    from_up = exchange(tracers[..., last_x, :], 1, 0)[..., None, :]
    from_down = exchange(tracers[..., 0, :], -1, 0)[..., None, :]
    from_left = exchange(tracers[..., last_y], 0, 1)[..., None]
    from_right = exchange(tracers[..., 0], 0, -1)[..., None]
    above_x = np.eye(xsize, k=1)
    above_y = np.eye(ysize, k=1)
    sum_x = jnp.asarray(above_x + above_x.T, jnp.float32)
    diff_x = jnp.asarray(above_x - above_x.T, jnp.float32)
    sum_y = jnp.asarray(above_y + above_y.T, jnp.float32)
    diff_y = jnp.asarray(above_y.T - above_y, jnp.float32)
    row = jnp.arange(xsize)[:, None]
    column = jnp.arange(ysize)
    east = jnp.where(row == last_x, from_down, 0.0)
    west = jnp.where(row == 0, from_up, 0.0)
    north = jnp.where(column == last_y, from_right, 0.0)
    south = jnp.where(column == 0, from_left, 0.0)
    across_x = jnp.einsum("ab,...by->...ay", sum_x, tracers, precision=precision) + (east + west)
    slope_x = jnp.einsum("ab,...by->...ay", diff_x, tracers, precision=precision) + (east - west)
    across_y = jnp.einsum("...xc,cd->...xd", tracers, sum_y, precision=precision) + (north + south)
    slope_y = jnp.einsum("...xc,cd->...xd", tracers, diff_y, precision=precision) + (north - south)
    return (
        tracers
        + diff_coef * (across_x + across_y - 4.0 * tracers)
        - 0.5 * velocity[0] * slope_x
        - 0.5 * velocity[1] * slope_y
    )


def gll_tables():
    points = np.array([-1.0, -1.0 / np.sqrt(5.0), 1.0 / np.sqrt(5.0), 1.0])
    weights = np.array([1.0 / 6.0, 5.0 / 6.0, 5.0 / 6.0, 1.0 / 6.0])
    derivative = np.zeros((4, 4))
    for target in range(4):
        for source in range(4):
            if target == source:
                derivative[target, source] = np.sum(
                    [
                        1.0 / (points[source] - points[others])
                        for others in range(4)
                        if others != source
                    ]
                )
            else:
                numer = np.prod(
                    [
                        points[target] - points[others]
                        for others in range(4)
                        if others != target and others != source
                    ]
                )
                denom = np.prod(
                    [points[source] - points[others] for others in range(4) if others != source]
                )
                derivative[target, source] = numer / denom
    massw = np.array([1.0 / 3.0, 5.0 / 6.0, 5.0 / 6.0, 1.0 / 3.0])
    return (derivative, weights, massw)


def mass_inverse(massw_np, xsize, ysize):
    return jnp.asarray(
        1.0 / (np.tile(massw_np, xsize // 4)[:, None] * np.tile(massw_np, ysize // 4)[None, :]),
        jnp.float32,
    )


def gather_kernel(index_ref, scale_ref, table_ref, out_ref):
    fields, rows, lanes = table_ref.shape
    tile = out_ref.shape[1]
    index = index_ref[...]
    onehot = (lax.broadcasted_iota(jnp.int32, (lanes, tile), 0) == (index % lanes)).astype(jnp.bfloat16)
    select = lax.broadcasted_iota(jnp.int32, (rows, tile), 0) == (index // lanes)
    rest = table_ref[...]
    parts = []
    for part in range(3):
        piece = rest.astype(jnp.bfloat16)
        rest = rest - piece.astype(jnp.float32)
        parts.append(piece)
    stacked = jnp.concatenate(parts, axis=2).reshape(fields * rows, 3 * lanes)
    picked = jnp.dot(stacked, jnp.concatenate([onehot] * 3, axis=0), preferred_element_type=jnp.float32)
    scale = scale_ref[...]
    values = jnp.concatenate(
        [jnp.sum(jnp.where(select, picked[f * rows : (f + 1) * rows], 0.0), axis=0, keepdims=True) for f in range(fields)],
        axis=0,
    ) * scale

    @pl.when(pl.program_id(1) == 0)
    def first():
        out_ref[...] = values

    @pl.when(pl.program_id(1) > 0)
    def rest_steps():
        out_ref[...] = out_ref[...] + values


def onehot_gather(table, index, scale, groups):
    fields, rows, lanes = table.shape
    flat = index.reshape(1, -1)
    count = flat.shape[1]
    width = count // groups
    tile = 128
    while tile < 2048 and width % (2 * tile) == 0 and fields * rows * tile * 8 <= 4 * 2**20:
        tile *= 2
    blocks = width // tile
    return pl.pallas_call(
        gather_kernel,
        grid=(blocks, groups),
        in_specs=[
            pl.BlockSpec((1, tile), lambda step, group: (0, group * blocks + step)),
            pl.BlockSpec((1, tile), lambda step, group: (0, group * blocks + step)),
            pl.BlockSpec((fields, rows, lanes), lambda step, group: (0, 0, 0)),
        ],
        out_specs=pl.BlockSpec((fields, tile), lambda step, group: (0, step)),
        out_shape=jax.ShapeDtypeStruct((fields, width), jnp.float32),
    )(flat, scale.reshape(1, -1), table)


def per_device(
    atm_state,
    metric,
    send_idx,
    send_counts,
    ocean_tracers,
    ocean_velocity,
    remap_slots,
    remap_weights,
):
    fields, levels, xlocal, ylocal = atm_state.shape
    derivative_np, weights_np, massw_np = gll_tables()
    state_now = atm_state.reshape(fields * levels, xlocal, ylocal)
    inv_mass = mass_inverse(massw_np, xlocal, ylocal)
    for repeat in range(SUB):
        state_now = substep(state_now, metric, derivative_np, weights_np, inv_mass)
    atm_out = state_now.reshape(fields, levels, xlocal, ylocal)
    bottom = atm_out[:, levels - 1]
    speed = jnp.sqrt(1.0 + bottom[0] * bottom[0] + bottom[1] * bottom[1])
    flux_flat = (bottom * speed).reshape(fields, xlocal * ylocal)
    node_total = xlocal * ylocal
    rank_total = send_idx.shape[1]
    slot_cap = send_idx.shape[2]
    count_row = send_counts[0]
    live_slots = (jnp.arange(slot_cap)[None, :] < count_row[:, None]).astype(jnp.float32)
    flux_table = flux_flat.reshape(fields, node_total // 128, 128)
    payload = onehot_gather(flux_table, send_idx[0], live_slots, 1).reshape(fields, rank_total, slot_cap)
    received = lax.all_to_all(payload, ("gx", "gy"), split_axis=1, concat_axis=1, tiled=True)
    source_count, ocean_x, ocean_y = remap_slots.shape
    ocean_flux = onehot_gather(received, remap_slots, remap_weights, source_count).reshape(fields, ocean_x, ocean_y)
    velocity = ocean_velocity.at[0, 0].add(wind_coef * jnp.tanh(ocean_flux[0]))
    velocity = velocity.at[1, 0].add(wind_coef * jnp.tanh(ocean_flux[1]))
    tracers = ocean_tracers.at[0, 0].add(surf_coef * ocean_flux[2])
    tracers = tracers.at[1, 0].add(surf_coef * ocean_flux[3])
    for repeat in range(OSTEPS):
        tracers = tracer_step(tracers, velocity)
    return (atm_out, tracers)


def solution(mesh):
    in_specs = (
        P(None, None, "gx", "gy"),
        P(None, "gx", "gy"),
        P(("gx", "gy"), None, None),
        P(("gx", "gy"), None),
        P(None, None, "gx", "gy"),
        P(None, None, "gx", "gy"),
        P(None, "gx", "gy"),
        P(None, "gx", "gy"),
    )
    out_specs = (P(None, None, "gx", "gy"), P(None, None, "gx", "gy"))
    return jax.shard_map(
        per_device, mesh=mesh, in_specs=in_specs, out_specs=out_specs, check_vma=False
    )
```

```python
import math

import jax
import jax.numpy as jnp
import numpy as np
from jax import lax
from jax.experimental import pallas as pl
from jax.sharding import PartitionSpec as P

SUB = 2
OSTEPS = 2


visc_coef = 0.01
diff_coef = 0.2
wind_coef = 0.1
surf_coef = 0.2


def neighbour(values, step_x, step_y):
    count_x, count_y = lax.axis_size("gx"), lax.axis_size("gy")
    if step_y == 0:
        return lax.ppermute(values, "gx", [(i, (i + step_x) % count_x) for i in range(count_x)])
    if step_x == 0:
        return lax.ppermute(values, "gy", [(j, (j + step_y) % count_y) for j in range(count_y)])
    pairs = [
        (i * count_y + j, ((i + step_x) % count_x) * count_y + (j + step_y) % count_y)
        for i in range(count_x)
        for j in range(count_y)
    ]
    return lax.ppermute(values, ("gx", "gy"), pairs)


def shifted(values, before, after, axis):
    size = values.shape[axis]
    layout = [1] * values.ndim
    layout[axis] = size
    position = jnp.arange(size).reshape(layout)
    prev = jnp.concatenate([lax.slice_in_dim(values, 0, 1, axis=axis), lax.slice_in_dim(values, 0, size - 1, axis=axis)], axis=axis)
    nxt = jnp.concatenate([lax.slice_in_dim(values, 1, size, axis=axis), lax.slice_in_dim(values, size - 1, size, axis=axis)], axis=axis)
    prev = jnp.where(position == 0, jnp.broadcast_to(before, values.shape), prev)
    nxt = jnp.where(position == size - 1, jnp.broadcast_to(after, values.shape), nxt)
    return prev, nxt


def packed(values):
    if values.size % 128:
        return values
    return values.reshape(-1, 128)


def exchange(values, step_x, step_y):
    return neighbour(packed(values), step_x, step_y).reshape(values.shape)


def pair_matrix(size):
    position = np.arange(size)
    starts = position[position % 4 == 0][1:]
    ends = position[position % 4 == 3][:-1]
    pair = np.eye(size)
    pair[starts - 1, starts] = 1.0
    pair[ends + 1, ends] = 1.0
    return pair


def substep(state_in, metric, derivative_np, weights_np, inv_mass):
    levels, xsize, ysize = state_in.shape
    precision = lax.Precision.HIGH
    block_x = np.kron(np.eye(xsize // 4), derivative_np)
    block_y = np.kron(np.eye(ysize // 4), derivative_np)
    weight_x = np.tile(weights_np, xsize // 4)
    weight_y = np.tile(weights_np, ysize // 4)
    pair_y = pair_matrix(ysize)
    term_x_right = jnp.asarray(weight_y[:, None] * pair_y, jnp.float32)
    term_y_right = jnp.asarray(block_y @ pair_y, jnp.float32)
    pair_x = jnp.asarray(pair_matrix(xsize).T, jnp.float32)
    block_x = jnp.asarray(block_x, jnp.float32)
    along_x = jnp.einsum("ab,lby->lay", block_x, state_in, precision=precision)
    scaled_x = jnp.asarray(weight_x[:, None], jnp.float32) * metric[0] * along_x
    term_x = jnp.einsum("ba,lby->lay", block_x, scaled_x, precision=precision)
    along_y = jnp.einsum("lxc,dc->lxd", state_in, jnp.asarray(block_y, jnp.float32), precision=precision)
    scaled_y = jnp.asarray(weight_y[None, :], jnp.float32) * metric[1] * along_y
    merged = jnp.einsum("lxc,cd->lxd", term_x, term_x_right, precision=precision) + jnp.einsum(
        "lxc,cd->lxd", scaled_y, term_y_right, precision=precision
    ) * jnp.asarray(weight_x[:, None], jnp.float32)
    last_x, last_y = xsize - 1, ysize - 1
    from_left = exchange(merged[:, :, last_y], 0, 1)[:, :, None]
    from_right = exchange(merged[:, :, 0], 0, -1)[:, :, None]
    column = jnp.arange(ysize)
    merged = merged + jnp.where(column == 0, from_left, jnp.where(column == last_y, from_right, 0.0))
    from_up = exchange(merged[:, last_x, :], 1, 0)[:, None, :]
    from_down = exchange(merged[:, 0, :], -1, 0)[:, None, :]
    row = jnp.arange(xsize)[:, None]
    total = jnp.einsum("ab,lby->lay", pair_x, merged, precision=precision) + jnp.where(
        row == 0, from_up, jnp.where(row == last_x, from_down, 0.0)
    )
    return state_in - visc_coef * total * inv_mass


def tracer_step(tracers, velocity):
    xsize, ysize = tracers.shape[-2], tracers.shape[-1]
    last_x, last_y = xsize - 1, ysize - 1
    precision = lax.Precision.HIGH
    from_up = exchange(tracers[..., last_x, :], 1, 0)[..., None, :]
    from_down = exchange(tracers[..., 0, :], -1, 0)[..., None, :]
    from_left = exchange(tracers[..., last_y], 0, 1)[..., None]
    from_right = exchange(tracers[..., 0], 0, -1)[..., None]
    above_x = np.eye(xsize, k=1)
    above_y = np.eye(ysize, k=1)
    sum_x = jnp.asarray(above_x + above_x.T, jnp.float32)
    diff_x = jnp.asarray(above_x - above_x.T, jnp.float32)
    sum_y = jnp.asarray(above_y + above_y.T, jnp.float32)
    diff_y = jnp.asarray(above_y.T - above_y, jnp.float32)
    row = jnp.arange(xsize)[:, None]
    column = jnp.arange(ysize)
    east = jnp.where(row == last_x, from_down, 0.0)
    west = jnp.where(row == 0, from_up, 0.0)
    north = jnp.where(column == last_y, from_right, 0.0)
    south = jnp.where(column == 0, from_left, 0.0)
    across_x = jnp.einsum("ab,...by->...ay", sum_x, tracers, precision=precision) + (east + west)
    slope_x = jnp.einsum("ab,...by->...ay", diff_x, tracers, precision=precision) + (east - west)
    across_y = jnp.einsum("...xc,cd->...xd", tracers, sum_y, precision=precision) + (north + south)
    slope_y = jnp.einsum("...xc,cd->...xd", tracers, diff_y, precision=precision) + (north - south)
    return (
        tracers
        + diff_coef * (across_x + across_y - 4.0 * tracers)
        - 0.5 * velocity[0] * slope_x
        - 0.5 * velocity[1] * slope_y
    )


def gll_tables():
    points = np.array([-1.0, -1.0 / np.sqrt(5.0), 1.0 / np.sqrt(5.0), 1.0])
    weights = np.array([1.0 / 6.0, 5.0 / 6.0, 5.0 / 6.0, 1.0 / 6.0])
    derivative = np.zeros((4, 4))
    for target in range(4):
        for source in range(4):
            if target == source:
                derivative[target, source] = np.sum(
                    [
                        1.0 / (points[source] - points[others])
                        for others in range(4)
                        if others != source
                    ]
                )
            else:
                numer = np.prod(
                    [
                        points[target] - points[others]
                        for others in range(4)
                        if others != target and others != source
                    ]
                )
                denom = np.prod(
                    [points[source] - points[others] for others in range(4) if others != source]
                )
                derivative[target, source] = numer / denom
    massw = np.array([1.0 / 3.0, 5.0 / 6.0, 5.0 / 6.0, 1.0 / 3.0])
    return (derivative, weights, massw)


def mass_inverse(massw_np, xsize, ysize):
    return jnp.asarray(
        1.0 / (np.tile(massw_np, xsize // 4)[:, None] * np.tile(massw_np, ysize // 4)[None, :]),
        jnp.float32,
    )


def gather_kernel(index_ref, scale_ref, table_ref, out_ref):
    fields, rows, lanes = table_ref.shape
    tile = out_ref.shape[1]
    index = index_ref[...]
    onehot = (lax.broadcasted_iota(jnp.int32, (lanes, tile), 0) == (index % lanes)).astype(jnp.bfloat16)
    select = lax.broadcasted_iota(jnp.int32, (rows, tile), 0) == (index // lanes)
    rest = table_ref[...]
    parts = []
    for part in range(3):
        piece = rest.astype(jnp.bfloat16)
        rest = rest - piece.astype(jnp.float32)
        parts.append(piece)
    stacked = jnp.concatenate(parts, axis=2).reshape(fields * rows, 3 * lanes)
    picked = jnp.dot(stacked, jnp.concatenate([onehot] * 3, axis=0), preferred_element_type=jnp.float32)
    scale = scale_ref[...]
    values = jnp.concatenate(
        [jnp.sum(jnp.where(select, picked[f * rows : (f + 1) * rows], 0.0), axis=0, keepdims=True) for f in range(fields)],
        axis=0,
    ) * scale

    @pl.when(pl.program_id(1) == 0)
    def first():
        out_ref[...] = values

    @pl.when(pl.program_id(1) > 0)
    def rest_steps():
        out_ref[...] = out_ref[...] + values


def onehot_gather(table, index, scale, groups):
    fields, rows, lanes = table.shape
    flat = index.reshape(1, -1)
    count = flat.shape[1]
    width = count // groups
    tile = 128
    while tile < 8192 and width % (2 * tile) == 0 and fields * rows * tile * 8 <= 4 * 2**20:
        tile *= 2
    blocks = width // tile
    return pl.pallas_call(
        gather_kernel,
        grid=(blocks, groups),
        in_specs=[
            pl.BlockSpec((1, tile), lambda step, group: (0, group * blocks + step)),
            pl.BlockSpec((1, tile), lambda step, group: (0, group * blocks + step)),
            pl.BlockSpec((fields, rows, lanes), lambda step, group: (0, 0, 0)),
        ],
        out_specs=pl.BlockSpec((fields, tile), lambda step, group: (0, step)),
        out_shape=jax.ShapeDtypeStruct((fields, width), jnp.float32),
    )(flat, scale.reshape(1, -1), table)


def per_device(
    atm_state,
    metric,
    send_idx,
    send_counts,
    ocean_tracers,
    ocean_velocity,
    remap_slots,
    remap_weights,
):
    fields, levels, xlocal, ylocal = atm_state.shape
    derivative_np, weights_np, massw_np = gll_tables()
    state_now = atm_state.reshape(fields * levels, xlocal, ylocal)
    inv_mass = mass_inverse(massw_np, xlocal, ylocal)
    for repeat in range(SUB):
        state_now = substep(state_now, metric, derivative_np, weights_np, inv_mass)
    atm_out = state_now.reshape(fields, levels, xlocal, ylocal)
    bottom = atm_out[:, levels - 1]
    speed = jnp.sqrt(1.0 + bottom[0] * bottom[0] + bottom[1] * bottom[1])
    flux_flat = (bottom * speed).reshape(fields, xlocal * ylocal)
    node_total = xlocal * ylocal
    rank_total = send_idx.shape[1]
    slot_cap = send_idx.shape[2]
    count_row = send_counts[0]
    live_slots = (jnp.arange(slot_cap)[None, :] < count_row[:, None]).astype(jnp.float32)
    flux_table = flux_flat.reshape(fields, node_total // 128, 128)
    payload = onehot_gather(flux_table, send_idx[0], live_slots, 1).reshape(fields, rank_total, slot_cap)
    received = lax.all_to_all(payload, ("gx", "gy"), split_axis=1, concat_axis=1, tiled=True)
    source_count, ocean_x, ocean_y = remap_slots.shape
    ocean_flux = onehot_gather(received, remap_slots, remap_weights, source_count).reshape(fields, ocean_x, ocean_y)
    velocity = ocean_velocity.at[0, 0].add(wind_coef * jnp.tanh(ocean_flux[0]))
    velocity = velocity.at[1, 0].add(wind_coef * jnp.tanh(ocean_flux[1]))
    tracers = ocean_tracers.at[0, 0].add(surf_coef * ocean_flux[2])
    tracers = tracers.at[1, 0].add(surf_coef * ocean_flux[3])
    for repeat in range(OSTEPS):
        tracers = tracer_step(tracers, velocity)
    return (atm_out, tracers)


def solution(mesh):
    in_specs = (
        P(None, None, "gx", "gy"),
        P(None, "gx", "gy"),
        P(("gx", "gy"), None, None),
        P(("gx", "gy"), None),
        P(None, None, "gx", "gy"),
        P(None, None, "gx", "gy"),
        P(None, "gx", "gy"),
        P(None, "gx", "gy"),
    )
    out_specs = (P(None, None, "gx", "gy"), P(None, None, "gx", "gy"))
    return jax.shard_map(
        per_device, mesh=mesh, in_specs=in_specs, out_specs=out_specs, check_vma=False
    )
```

```python
import functools
import math

import jax
import jax.numpy as jnp
import numpy as np
from jax import lax
from jax.experimental import pallas as pl
from jax.sharding import PartitionSpec as P

SUB = 2
OSTEPS = 2


visc_coef = 0.01
diff_coef = 0.2
wind_coef = 0.1
surf_coef = 0.2


def neighbour(values, step_x, step_y):
    count_x, count_y = lax.axis_size("gx"), lax.axis_size("gy")
    if step_y == 0:
        return lax.ppermute(values, "gx", [(i, (i + step_x) % count_x) for i in range(count_x)])
    if step_x == 0:
        return lax.ppermute(values, "gy", [(j, (j + step_y) % count_y) for j in range(count_y)])
    pairs = [
        (i * count_y + j, ((i + step_x) % count_x) * count_y + (j + step_y) % count_y)
        for i in range(count_x)
        for j in range(count_y)
    ]
    return lax.ppermute(values, ("gx", "gy"), pairs)


def shifted(values, before, after, axis):
    size = values.shape[axis]
    layout = [1] * values.ndim
    layout[axis] = size
    position = jnp.arange(size).reshape(layout)
    prev = jnp.concatenate([lax.slice_in_dim(values, 0, 1, axis=axis), lax.slice_in_dim(values, 0, size - 1, axis=axis)], axis=axis)
    nxt = jnp.concatenate([lax.slice_in_dim(values, 1, size, axis=axis), lax.slice_in_dim(values, size - 1, size, axis=axis)], axis=axis)
    prev = jnp.where(position == 0, jnp.broadcast_to(before, values.shape), prev)
    nxt = jnp.where(position == size - 1, jnp.broadcast_to(after, values.shape), nxt)
    return prev, nxt


def packed(values):
    if values.size % 128:
        return values
    return values.reshape(-1, 128)


def exchange(values, step_x, step_y):
    return neighbour(packed(values), step_x, step_y).reshape(values.shape)


def pair_matrix(size):
    position = np.arange(size)
    starts = position[position % 4 == 0][1:]
    ends = position[position % 4 == 3][:-1]
    pair = np.eye(size)
    pair[starts - 1, starts] = 1.0
    pair[ends + 1, ends] = 1.0
    return pair


def substep(state_in, metric, derivative_np, weights_np, inv_mass):
    levels, xsize, ysize = state_in.shape
    precision = lax.Precision.HIGH
    block_x = np.kron(np.eye(xsize // 4), derivative_np)
    block_y = np.kron(np.eye(ysize // 4), derivative_np)
    weight_x = np.tile(weights_np, xsize // 4)
    weight_y = np.tile(weights_np, ysize // 4)
    pair_y = pair_matrix(ysize)
    term_x_right = jnp.asarray(weight_y[:, None] * pair_y, jnp.float32)
    term_y_right = jnp.asarray(block_y @ pair_y, jnp.float32)
    pair_x = jnp.asarray(pair_matrix(xsize).T, jnp.float32)
    block_x = jnp.asarray(block_x, jnp.float32)
    along_x = jnp.einsum("ab,lby->lay", block_x, state_in, precision=precision)
    scaled_x = jnp.asarray(weight_x[:, None], jnp.float32) * metric[0] * along_x
    term_x = jnp.einsum("ba,lby->lay", block_x, scaled_x, precision=precision)
    along_y = jnp.einsum("lxc,dc->lxd", state_in, jnp.asarray(block_y, jnp.float32), precision=precision)
    scaled_y = jnp.asarray(weight_y[None, :], jnp.float32) * metric[1] * along_y
    merged = jnp.einsum("lxc,cd->lxd", term_x, term_x_right, precision=precision) + jnp.einsum(
        "lxc,cd->lxd", scaled_y, term_y_right, precision=precision
    ) * jnp.asarray(weight_x[:, None], jnp.float32)
    last_x, last_y = xsize - 1, ysize - 1
    from_left = exchange(merged[:, :, last_y], 0, 1)[:, :, None]
    from_right = exchange(merged[:, :, 0], 0, -1)[:, :, None]
    column = jnp.arange(ysize)
    merged = merged + jnp.where(column == 0, from_left, jnp.where(column == last_y, from_right, 0.0))
    from_up = exchange(merged[:, last_x, :], 1, 0)[:, None, :]
    from_down = exchange(merged[:, 0, :], -1, 0)[:, None, :]
    row = jnp.arange(xsize)[:, None]
    total = jnp.einsum("ab,lby->lay", pair_x, merged, precision=precision) + jnp.where(
        row == 0, from_up, jnp.where(row == last_x, from_down, 0.0)
    )
    return state_in - visc_coef * total * inv_mass


def tracer_step(tracers, velocity):
    xsize, ysize = tracers.shape[-2], tracers.shape[-1]
    last_x, last_y = xsize - 1, ysize - 1
    precision = lax.Precision.HIGH
    from_up = exchange(tracers[..., last_x, :], 1, 0)[..., None, :]
    from_down = exchange(tracers[..., 0, :], -1, 0)[..., None, :]
    from_left = exchange(tracers[..., last_y], 0, 1)[..., None]
    from_right = exchange(tracers[..., 0], 0, -1)[..., None]
    above_x = np.eye(xsize, k=1)
    above_y = np.eye(ysize, k=1)
    sum_x = jnp.asarray(above_x + above_x.T, jnp.float32)
    diff_x = jnp.asarray(above_x - above_x.T, jnp.float32)
    sum_y = jnp.asarray(above_y + above_y.T, jnp.float32)
    diff_y = jnp.asarray(above_y.T - above_y, jnp.float32)
    row = jnp.arange(xsize)[:, None]
    column = jnp.arange(ysize)
    east = jnp.where(row == last_x, from_down, 0.0)
    west = jnp.where(row == 0, from_up, 0.0)
    north = jnp.where(column == last_y, from_right, 0.0)
    south = jnp.where(column == 0, from_left, 0.0)
    across_x = jnp.einsum("ab,...by->...ay", sum_x, tracers, precision=precision) + (east + west)
    slope_x = jnp.einsum("ab,...by->...ay", diff_x, tracers, precision=precision) + (east - west)
    across_y = jnp.einsum("...xc,cd->...xd", tracers, sum_y, precision=precision) + (north + south)
    slope_y = jnp.einsum("...xc,cd->...xd", tracers, diff_y, precision=precision) + (north - south)
    return (
        tracers
        + diff_coef * (across_x + across_y - 4.0 * tracers)
        - 0.5 * velocity[0] * slope_x
        - 0.5 * velocity[1] * slope_y
    )


def gll_tables():
    points = np.array([-1.0, -1.0 / np.sqrt(5.0), 1.0 / np.sqrt(5.0), 1.0])
    weights = np.array([1.0 / 6.0, 5.0 / 6.0, 5.0 / 6.0, 1.0 / 6.0])
    derivative = np.zeros((4, 4))
    for target in range(4):
        for source in range(4):
            if target == source:
                derivative[target, source] = np.sum(
                    [
                        1.0 / (points[source] - points[others])
                        for others in range(4)
                        if others != source
                    ]
                )
            else:
                numer = np.prod(
                    [
                        points[target] - points[others]
                        for others in range(4)
                        if others != target and others != source
                    ]
                )
                denom = np.prod(
                    [points[source] - points[others] for others in range(4) if others != source]
                )
                derivative[target, source] = numer / denom
    massw = np.array([1.0 / 3.0, 5.0 / 6.0, 5.0 / 6.0, 1.0 / 3.0])
    return (derivative, weights, massw)


def mass_inverse(massw_np, xsize, ysize):
    return jnp.asarray(
        1.0 / (np.tile(massw_np, xsize // 4)[:, None] * np.tile(massw_np, ysize // 4)[None, :]),
        jnp.float32,
    )


def gather_kernel(index_ref, scale_ref, table_ref, out_ref, per=1):
    fields, rows, lanes = table_ref.shape
    tile = index_ref.shape[1]
    index = index_ref[...]
    onehot = (lax.broadcasted_iota(jnp.int32, (lanes, tile), 0) == (index % lanes)).astype(jnp.bfloat16)
    select = lax.broadcasted_iota(jnp.int32, (rows, tile), 0) == (index // lanes)
    rest = table_ref[...]
    parts = []
    for part in range(3):
        piece = rest.astype(jnp.bfloat16)
        rest = rest - piece.astype(jnp.float32)
        parts.append(piece)
    stacked = jnp.concatenate(parts, axis=2).reshape(fields * rows, 3 * lanes)
    picked = jnp.dot(stacked, jnp.concatenate([onehot] * 3, axis=0), preferred_element_type=jnp.float32)
    scale = scale_ref[...]
    values = jnp.concatenate(
        [jnp.sum(jnp.where(select, picked[f * rows : (f + 1) * rows], 0.0), axis=0, keepdims=True) for f in range(fields)],
        axis=0,
    ) * scale
    width = out_ref.shape[1]
    total = values[:, :width]
    for chunk in range(1, per):
        total = total + values[:, chunk * width : (chunk + 1) * width]
    values = total

    @pl.when(pl.program_id(1) == 0)
    def first():
        out_ref[...] = values

    @pl.when(pl.program_id(1) > 0)
    def rest_steps():
        out_ref[...] = out_ref[...] + values


def onehot_gather(table, index, scale, groups):
    fields, rows, lanes = table.shape
    flat = index.reshape(1, -1)
    count = flat.shape[1]
    width = count // groups
    tile = 128
    while tile < 8192 and width % (2 * tile) == 0 and fields * rows * tile * 8 <= 4 * 2**20:
        tile *= 2
    blocks = width // tile
    per = groups if blocks == 1 and fields * rows * count * 8 <= 16 * 2**20 else 1
    return pl.pallas_call(
        functools.partial(gather_kernel, per=per),
        grid=(blocks, groups // per),
        in_specs=[
            pl.BlockSpec((1, per * tile), lambda step, group: (0, group * blocks + step)),
            pl.BlockSpec((1, per * tile), lambda step, group: (0, group * blocks + step)),
            pl.BlockSpec((fields, rows, lanes), lambda step, group: (0, 0, 0)),
        ],
        out_specs=pl.BlockSpec((fields, tile), lambda step, group: (0, step)),
        out_shape=jax.ShapeDtypeStruct((fields, width), jnp.float32),
    )(flat, scale.reshape(1, -1), table)


def per_device(
    atm_state,
    metric,
    send_idx,
    send_counts,
    ocean_tracers,
    ocean_velocity,
    remap_slots,
    remap_weights,
):
    fields, levels, xlocal, ylocal = atm_state.shape
    derivative_np, weights_np, massw_np = gll_tables()
    state_now = atm_state.reshape(fields * levels, xlocal, ylocal)
    inv_mass = mass_inverse(massw_np, xlocal, ylocal)
    for repeat in range(SUB):
        state_now = substep(state_now, metric, derivative_np, weights_np, inv_mass)
    atm_out = state_now.reshape(fields, levels, xlocal, ylocal)
    bottom = atm_out[:, levels - 1]
    speed = jnp.sqrt(1.0 + bottom[0] * bottom[0] + bottom[1] * bottom[1])
    flux_flat = (bottom * speed).reshape(fields, xlocal * ylocal)
    node_total = xlocal * ylocal
    rank_total = send_idx.shape[1]
    slot_cap = send_idx.shape[2]
    count_row = send_counts[0]
    live_slots = (jnp.arange(slot_cap)[None, :] < count_row[:, None]).astype(jnp.float32)
    flux_table = flux_flat.reshape(fields, node_total // 128, 128)
    payload = onehot_gather(flux_table, send_idx[0], live_slots, 1).reshape(fields, rank_total, slot_cap)
    received = lax.all_to_all(payload, ("gx", "gy"), split_axis=1, concat_axis=1, tiled=True)
    source_count, ocean_x, ocean_y = remap_slots.shape
    ocean_flux = onehot_gather(received, remap_slots, remap_weights, source_count).reshape(fields, ocean_x, ocean_y)
    velocity = ocean_velocity.at[0, 0].add(wind_coef * jnp.tanh(ocean_flux[0]))
    velocity = velocity.at[1, 0].add(wind_coef * jnp.tanh(ocean_flux[1]))
    tracers = ocean_tracers.at[0, 0].add(surf_coef * ocean_flux[2])
    tracers = tracers.at[1, 0].add(surf_coef * ocean_flux[3])
    for repeat in range(OSTEPS):
        tracers = tracer_step(tracers, velocity)
    return (atm_out, tracers)


def solution(mesh):
    in_specs = (
        P(None, None, "gx", "gy"),
        P(None, "gx", "gy"),
        P(("gx", "gy"), None, None),
        P(("gx", "gy"), None),
        P(None, None, "gx", "gy"),
        P(None, None, "gx", "gy"),
        P(None, "gx", "gy"),
        P(None, "gx", "gy"),
    )
    out_specs = (P(None, None, "gx", "gy"), P(None, None, "gx", "gy"))
    return jax.shard_map(
        per_device, mesh=mesh, in_specs=in_specs, out_specs=out_specs, check_vma=False
    )
```

```python
import functools
import math

import jax
import jax.numpy as jnp
import numpy as np
from jax import lax
from jax.experimental import pallas as pl
from jax.sharding import PartitionSpec as P

SUB = 2
OSTEPS = 2


visc_coef = 0.01
diff_coef = 0.2
wind_coef = 0.1
surf_coef = 0.2


def neighbour(values, step_x, step_y):
    count_x, count_y = lax.axis_size("gx"), lax.axis_size("gy")
    if step_y == 0:
        return lax.ppermute(values, "gx", [(i, (i + step_x) % count_x) for i in range(count_x)])
    if step_x == 0:
        return lax.ppermute(values, "gy", [(j, (j + step_y) % count_y) for j in range(count_y)])
    pairs = [
        (i * count_y + j, ((i + step_x) % count_x) * count_y + (j + step_y) % count_y)
        for i in range(count_x)
        for j in range(count_y)
    ]
    return lax.ppermute(values, ("gx", "gy"), pairs)


def shifted(values, before, after, axis):
    size = values.shape[axis]
    layout = [1] * values.ndim
    layout[axis] = size
    position = jnp.arange(size).reshape(layout)
    prev = jnp.concatenate([lax.slice_in_dim(values, 0, 1, axis=axis), lax.slice_in_dim(values, 0, size - 1, axis=axis)], axis=axis)
    nxt = jnp.concatenate([lax.slice_in_dim(values, 1, size, axis=axis), lax.slice_in_dim(values, size - 1, size, axis=axis)], axis=axis)
    prev = jnp.where(position == 0, jnp.broadcast_to(before, values.shape), prev)
    nxt = jnp.where(position == size - 1, jnp.broadcast_to(after, values.shape), nxt)
    return prev, nxt


def packed(values):
    if values.size % 128:
        return values
    return values.reshape(-1, 128)


def exchange(values, step_x, step_y):
    return neighbour(packed(values), step_x, step_y).reshape(values.shape)


def pair_matrix(size):
    position = np.arange(size)
    starts = position[position % 4 == 0][1:]
    ends = position[position % 4 == 3][:-1]
    pair = np.eye(size)
    pair[starts - 1, starts] = 1.0
    pair[ends + 1, ends] = 1.0
    return pair


def substep(state_in, metric, derivative_np, weights_np, inv_mass):
    levels, xsize, ysize = state_in.shape
    precision = lax.Precision.HIGH
    block_x = np.kron(np.eye(xsize // 4), derivative_np)
    block_y = np.kron(np.eye(ysize // 4), derivative_np)
    weight_x = np.tile(weights_np, xsize // 4)
    weight_y = np.tile(weights_np, ysize // 4)
    pair_y = pair_matrix(ysize)
    term_x_right = jnp.asarray(weight_y[:, None] * pair_y, jnp.float32)
    term_y_right = jnp.asarray(block_y @ pair_y, jnp.float32)
    pair_x = jnp.asarray(pair_matrix(xsize).T, jnp.float32)
    block_x = jnp.asarray(block_x, jnp.float32)
    along_x = jnp.einsum("ab,lby->lay", block_x, state_in, precision=precision)
    scaled_x = jnp.asarray(weight_x[:, None], jnp.float32) * metric[0] * along_x
    term_x = jnp.einsum("ba,lby->lay", block_x, scaled_x, precision=precision)
    along_y = jnp.einsum("lxc,dc->lxd", state_in, jnp.asarray(block_y, jnp.float32), precision=precision)
    scaled_y = jnp.asarray(weight_y[None, :], jnp.float32) * metric[1] * along_y
    merged = jnp.einsum("lxc,cd->lxd", term_x, term_x_right, precision=precision) + jnp.einsum(
        "lxc,cd->lxd", scaled_y, term_y_right, precision=precision
    ) * jnp.asarray(weight_x[:, None], jnp.float32)
    last_x, last_y = xsize - 1, ysize - 1
    from_left = exchange(merged[:, :, last_y], 0, 1)[:, :, None]
    from_right = exchange(merged[:, :, 0], 0, -1)[:, :, None]
    column = jnp.arange(ysize)
    merged = merged + jnp.where(column == 0, from_left, jnp.where(column == last_y, from_right, 0.0))
    from_up = exchange(merged[:, last_x, :], 1, 0)[:, None, :]
    from_down = exchange(merged[:, 0, :], -1, 0)[:, None, :]
    row = jnp.arange(xsize)[:, None]
    total = jnp.einsum("ab,lby->lay", pair_x, merged, precision=precision) + jnp.where(
        row == 0, from_up, jnp.where(row == last_x, from_down, 0.0)
    )
    return state_in - visc_coef * total * inv_mass


def tracer_step(tracers, velocity):
    xsize, ysize = tracers.shape[-2], tracers.shape[-1]
    last_x, last_y = xsize - 1, ysize - 1
    precision = lax.Precision.HIGH
    from_up = exchange(tracers[..., last_x, :], 1, 0)[..., None, :]
    from_down = exchange(tracers[..., 0, :], -1, 0)[..., None, :]
    from_left = exchange(tracers[..., last_y], 0, 1)[..., None]
    from_right = exchange(tracers[..., 0], 0, -1)[..., None]
    above_x = np.eye(xsize, k=1)
    above_y = np.eye(ysize, k=1)
    sum_x = jnp.asarray(above_x + above_x.T, jnp.float32)
    diff_x = jnp.asarray(above_x - above_x.T, jnp.float32)
    sum_y = jnp.asarray(above_y + above_y.T, jnp.float32)
    diff_y = jnp.asarray(above_y.T - above_y, jnp.float32)
    row = jnp.arange(xsize)[:, None]
    column = jnp.arange(ysize)
    east = jnp.where(row == last_x, from_down, 0.0)
    west = jnp.where(row == 0, from_up, 0.0)
    north = jnp.where(column == last_y, from_right, 0.0)
    south = jnp.where(column == 0, from_left, 0.0)
    across_x = jnp.einsum("ab,...by->...ay", sum_x, tracers, precision=precision) + (east + west)
    slope_x = jnp.einsum("ab,...by->...ay", diff_x, tracers, precision=precision) + (east - west)
    across_y = jnp.einsum("...xc,cd->...xd", tracers, sum_y, precision=precision) + (north + south)
    slope_y = jnp.einsum("...xc,cd->...xd", tracers, diff_y, precision=precision) + (north - south)
    return (
        tracers
        + diff_coef * (across_x + across_y - 4.0 * tracers)
        - 0.5 * velocity[0] * slope_x
        - 0.5 * velocity[1] * slope_y
    )


def gll_tables():
    points = np.array([-1.0, -1.0 / np.sqrt(5.0), 1.0 / np.sqrt(5.0), 1.0])
    weights = np.array([1.0 / 6.0, 5.0 / 6.0, 5.0 / 6.0, 1.0 / 6.0])
    derivative = np.zeros((4, 4))
    for target in range(4):
        for source in range(4):
            if target == source:
                derivative[target, source] = np.sum(
                    [
                        1.0 / (points[source] - points[others])
                        for others in range(4)
                        if others != source
                    ]
                )
            else:
                numer = np.prod(
                    [
                        points[target] - points[others]
                        for others in range(4)
                        if others != target and others != source
                    ]
                )
                denom = np.prod(
                    [points[source] - points[others] for others in range(4) if others != source]
                )
                derivative[target, source] = numer / denom
    massw = np.array([1.0 / 3.0, 5.0 / 6.0, 5.0 / 6.0, 1.0 / 3.0])
    return (derivative, weights, massw)


def mass_inverse(massw_np, xsize, ysize):
    return jnp.asarray(
        1.0 / (np.tile(massw_np, xsize // 4)[:, None] * np.tile(massw_np, ysize // 4)[None, :]),
        jnp.float32,
    )


def gather_kernel(index_ref, scale_ref, table_ref, out_ref, per=1):
    fields, rows, lanes = table_ref.shape
    tile = index_ref.shape[0] * index_ref.shape[1]
    index = jnp.concatenate([index_ref[pl.ds(r, 1), :] for r in range(index_ref.shape[0])], axis=1)
    onehot = (lax.broadcasted_iota(jnp.int32, (lanes, tile), 0) == (index % lanes)).astype(jnp.bfloat16)
    select = lax.broadcasted_iota(jnp.int32, (rows, tile), 0) == (index // lanes)
    rest = table_ref[...]
    parts = []
    for part in range(3):
        piece = rest.astype(jnp.bfloat16)
        rest = rest - piece.astype(jnp.float32)
        parts.append(piece)
    stacked = jnp.concatenate(parts, axis=2).reshape(fields * rows, 3 * lanes)
    picked = jnp.dot(stacked, jnp.concatenate([onehot] * 3, axis=0), preferred_element_type=jnp.float32)
    scale = jnp.concatenate([scale_ref[pl.ds(r, 1), :] for r in range(scale_ref.shape[0])], axis=1)
    values = jnp.concatenate(
        [jnp.sum(jnp.where(select, picked[f * rows : (f + 1) * rows], 0.0), axis=0, keepdims=True) for f in range(fields)],
        axis=0,
    ) * scale
    width = out_ref.shape[1]
    total = values[:, :width]
    for chunk in range(1, per):
        total = total + values[:, chunk * width : (chunk + 1) * width]
    values = total

    @pl.when(pl.program_id(1) == 0)
    def first():
        out_ref[...] = values

    @pl.when(pl.program_id(1) > 0)
    def rest_steps():
        out_ref[...] = out_ref[...] + values


def onehot_gather(table, index, scale, groups):
    fields, rows, lanes = table.shape
    flat = index.reshape(-1, index.shape[-1])
    columns = flat.shape[1]
    count = flat.size
    width = count // groups
    tile = 128
    while tile < 8192 and width % (2 * tile) == 0 and fields * rows * tile * 8 <= 4 * 2**20:
        tile *= 2
    blocks = width // tile
    per = groups if blocks == 1 and fields * rows * count * 8 <= 16 * 2**20 else 1
    return pl.pallas_call(
        functools.partial(gather_kernel, per=per),
        grid=(blocks, groups // per),
        in_specs=[
            pl.BlockSpec((per * tile // columns, columns), lambda step, group: (group * blocks + step, 0)),
            pl.BlockSpec((per * tile // columns, columns), lambda step, group: (group * blocks + step, 0)),
            pl.BlockSpec((fields, rows, lanes), lambda step, group: (0, 0, 0)),
        ],
        out_specs=pl.BlockSpec((fields, tile), lambda step, group: (0, step)),
        out_shape=jax.ShapeDtypeStruct((fields, width), jnp.float32),
    )(flat, scale.reshape(flat.shape), table)


def per_device(
    atm_state,
    metric,
    send_idx,
    send_counts,
    ocean_tracers,
    ocean_velocity,
    remap_slots,
    remap_weights,
):
    fields, levels, xlocal, ylocal = atm_state.shape
    derivative_np, weights_np, massw_np = gll_tables()
    state_now = atm_state.reshape(fields * levels, xlocal, ylocal)
    inv_mass = mass_inverse(massw_np, xlocal, ylocal)
    for repeat in range(SUB):
        state_now = substep(state_now, metric, derivative_np, weights_np, inv_mass)
    atm_out = state_now.reshape(fields, levels, xlocal, ylocal)
    bottom = atm_out[:, levels - 1]
    speed = jnp.sqrt(1.0 + bottom[0] * bottom[0] + bottom[1] * bottom[1])
    flux_flat = (bottom * speed).reshape(fields, xlocal * ylocal)
    node_total = xlocal * ylocal
    rank_total = send_idx.shape[1]
    slot_cap = send_idx.shape[2]
    count_row = send_counts[0]
    live_slots = (jnp.arange(slot_cap)[None, :] < count_row[:, None]).astype(jnp.float32)
    flux_table = flux_flat.reshape(fields, node_total // 128, 128)
    payload = onehot_gather(flux_table, send_idx[0], live_slots, 1).reshape(fields, rank_total, slot_cap)
    received = lax.all_to_all(payload, ("gx", "gy"), split_axis=1, concat_axis=1, tiled=True)
    source_count, ocean_x, ocean_y = remap_slots.shape
    ocean_flux = onehot_gather(received, remap_slots, remap_weights, source_count).reshape(fields, ocean_x, ocean_y)
    velocity = ocean_velocity.at[0, 0].add(wind_coef * jnp.tanh(ocean_flux[0]))
    velocity = velocity.at[1, 0].add(wind_coef * jnp.tanh(ocean_flux[1]))
    tracers = ocean_tracers.at[0, 0].add(surf_coef * ocean_flux[2])
    tracers = tracers.at[1, 0].add(surf_coef * ocean_flux[3])
    for repeat in range(OSTEPS):
        tracers = tracer_step(tracers, velocity)
    return (atm_out, tracers)


def solution(mesh):
    in_specs = (
        P(None, None, "gx", "gy"),
        P(None, "gx", "gy"),
        P(("gx", "gy"), None, None),
        P(("gx", "gy"), None),
        P(None, None, "gx", "gy"),
        P(None, None, "gx", "gy"),
        P(None, "gx", "gy"),
        P(None, "gx", "gy"),
    )
    out_specs = (P(None, None, "gx", "gy"), P(None, None, "gx", "gy"))
    return jax.shard_map(
        per_device, mesh=mesh, in_specs=in_specs, out_specs=out_specs, check_vma=False
    )
```

```python
import functools
import math

import jax
import jax.numpy as jnp
import numpy as np
from jax import lax
from jax.experimental import pallas as pl
from jax.sharding import PartitionSpec as P

SUB = 2
OSTEPS = 2


visc_coef = 0.01
diff_coef = 0.2
wind_coef = 0.1
surf_coef = 0.2


def neighbour(values, step_x, step_y):
    count_x, count_y = lax.axis_size("gx"), lax.axis_size("gy")
    if step_y == 0:
        return lax.ppermute(values, "gx", [(i, (i + step_x) % count_x) for i in range(count_x)])
    if step_x == 0:
        return lax.ppermute(values, "gy", [(j, (j + step_y) % count_y) for j in range(count_y)])
    pairs = [
        (i * count_y + j, ((i + step_x) % count_x) * count_y + (j + step_y) % count_y)
        for i in range(count_x)
        for j in range(count_y)
    ]
    return lax.ppermute(values, ("gx", "gy"), pairs)


def shifted(values, before, after, axis):
    size = values.shape[axis]
    layout = [1] * values.ndim
    layout[axis] = size
    position = jnp.arange(size).reshape(layout)
    prev = jnp.concatenate([lax.slice_in_dim(values, 0, 1, axis=axis), lax.slice_in_dim(values, 0, size - 1, axis=axis)], axis=axis)
    nxt = jnp.concatenate([lax.slice_in_dim(values, 1, size, axis=axis), lax.slice_in_dim(values, size - 1, size, axis=axis)], axis=axis)
    prev = jnp.where(position == 0, jnp.broadcast_to(before, values.shape), prev)
    nxt = jnp.where(position == size - 1, jnp.broadcast_to(after, values.shape), nxt)
    return prev, nxt


def packed(values):
    if values.size % 128:
        return values
    return values.reshape(-1, 128)


def exchange(values, step_x, step_y):
    return neighbour(packed(values), step_x, step_y).reshape(values.shape)


def pair_matrix(size):
    position = np.arange(size)
    starts = position[position % 4 == 0][1:]
    ends = position[position % 4 == 3][:-1]
    pair = np.eye(size)
    pair[starts - 1, starts] = 1.0
    pair[ends + 1, ends] = 1.0
    return pair


def substep(state_in, metric, derivative_np, weights_np, inv_mass):
    levels, xsize, ysize = state_in.shape
    precision = lax.Precision.HIGH
    block_x = np.kron(np.eye(xsize // 4), derivative_np)
    block_y = np.kron(np.eye(ysize // 4), derivative_np)
    weight_x = np.tile(weights_np, xsize // 4)
    weight_y = np.tile(weights_np, ysize // 4)
    pair_y = pair_matrix(ysize)
    term_x_right = jnp.asarray(weight_y[:, None] * pair_y, jnp.float32)
    term_y_right = jnp.asarray(block_y @ pair_y, jnp.float32)
    pair_x = jnp.asarray(pair_matrix(xsize).T, jnp.float32)
    block_x = jnp.asarray(block_x, jnp.float32)
    along_x = jnp.einsum("ab,lby->lay", block_x, state_in, precision=precision)
    scaled_x = jnp.asarray(weight_x[:, None], jnp.float32) * metric[0] * along_x
    term_x = jnp.einsum("ba,lby->lay", block_x, scaled_x, precision=precision)
    along_y = jnp.einsum("lxc,dc->lxd", state_in, jnp.asarray(block_y, jnp.float32), precision=precision)
    scaled_y = jnp.asarray(weight_y[None, :], jnp.float32) * metric[1] * along_y
    merged = jnp.einsum("lxc,cd->lxd", term_x, term_x_right, precision=precision) + jnp.einsum(
        "lxc,cd->lxd", scaled_y, term_y_right, precision=precision
    ) * jnp.asarray(weight_x[:, None], jnp.float32)
    last_x, last_y = xsize - 1, ysize - 1
    from_left = exchange(merged[:, :, last_y], 0, 1)[:, :, None]
    from_right = exchange(merged[:, :, 0], 0, -1)[:, :, None]
    column = jnp.arange(ysize)
    merged = merged + jnp.where(column == 0, from_left, jnp.where(column == last_y, from_right, 0.0))
    from_up = exchange(merged[:, last_x, :], 1, 0)[:, None, :]
    from_down = exchange(merged[:, 0, :], -1, 0)[:, None, :]
    row = jnp.arange(xsize)[:, None]
    total = jnp.einsum("ab,lby->lay", pair_x, merged, precision=precision) + jnp.where(
        row == 0, from_up, jnp.where(row == last_x, from_down, 0.0)
    )
    return state_in - visc_coef * total * inv_mass


def tracer_step(tracers, velocity):
    xsize, ysize = tracers.shape[-2], tracers.shape[-1]
    last_x, last_y = xsize - 1, ysize - 1
    precision = lax.Precision.HIGH
    from_up = exchange(tracers[..., last_x, :], 1, 0)[..., None, :]
    from_down = exchange(tracers[..., 0, :], -1, 0)[..., None, :]
    from_left = exchange(tracers[..., last_y], 0, 1)[..., None]
    from_right = exchange(tracers[..., 0], 0, -1)[..., None]
    above_x = np.eye(xsize, k=1)
    above_y = np.eye(ysize, k=1)
    sum_x = jnp.asarray(above_x + above_x.T, jnp.float32)
    diff_x = jnp.asarray(above_x - above_x.T, jnp.float32)
    sum_y = jnp.asarray(above_y + above_y.T, jnp.float32)
    diff_y = jnp.asarray(above_y.T - above_y, jnp.float32)
    row = jnp.arange(xsize)[:, None]
    column = jnp.arange(ysize)
    east = jnp.where(row == last_x, from_down, 0.0)
    west = jnp.where(row == 0, from_up, 0.0)
    north = jnp.where(column == last_y, from_right, 0.0)
    south = jnp.where(column == 0, from_left, 0.0)
    across_x = jnp.einsum("ab,...by->...ay", sum_x, tracers, precision=precision) + (east + west)
    slope_x = jnp.einsum("ab,...by->...ay", diff_x, tracers, precision=precision) + (east - west)
    across_y = jnp.einsum("...xc,cd->...xd", tracers, sum_y, precision=precision) + (north + south)
    slope_y = jnp.einsum("...xc,cd->...xd", tracers, diff_y, precision=precision) + (north - south)
    return (
        tracers
        + diff_coef * (across_x + across_y - 4.0 * tracers)
        - 0.5 * velocity[0] * slope_x
        - 0.5 * velocity[1] * slope_y
    )


def gll_tables():
    points = np.array([-1.0, -1.0 / np.sqrt(5.0), 1.0 / np.sqrt(5.0), 1.0])
    weights = np.array([1.0 / 6.0, 5.0 / 6.0, 5.0 / 6.0, 1.0 / 6.0])
    derivative = np.zeros((4, 4))
    for target in range(4):
        for source in range(4):
            if target == source:
                derivative[target, source] = np.sum(
                    [
                        1.0 / (points[source] - points[others])
                        for others in range(4)
                        if others != source
                    ]
                )
            else:
                numer = np.prod(
                    [
                        points[target] - points[others]
                        for others in range(4)
                        if others != target and others != source
                    ]
                )
                denom = np.prod(
                    [points[source] - points[others] for others in range(4) if others != source]
                )
                derivative[target, source] = numer / denom
    massw = np.array([1.0 / 3.0, 5.0 / 6.0, 5.0 / 6.0, 1.0 / 3.0])
    return (derivative, weights, massw)


def mass_inverse(massw_np, xsize, ysize):
    return jnp.asarray(
        1.0 / (np.tile(massw_np, xsize // 4)[:, None] * np.tile(massw_np, ysize // 4)[None, :]),
        jnp.float32,
    )


def gather_kernel(index_ref, scale_ref, table_ref, out_ref, per=1):
    fields, rows, lanes = table_ref.shape
    tile = index_ref.shape[1]
    index = index_ref[...]
    onehot = (lax.broadcasted_iota(jnp.int32, (lanes, tile), 0) == (index % lanes)).astype(jnp.bfloat16)
    select = lax.broadcasted_iota(jnp.int32, (rows, tile), 0) == (index // lanes)
    rest = table_ref[...]
    parts = []
    for part in range(3):
        piece = rest.astype(jnp.bfloat16)
        rest = rest - piece.astype(jnp.float32)
        parts.append(piece)
    picked = jnp.dot(parts[0].reshape(fields * rows, lanes), onehot, preferred_element_type=jnp.float32)
    for piece in parts[1:]:
        picked = picked + jnp.dot(piece.reshape(fields * rows, lanes), onehot, preferred_element_type=jnp.float32)
    scale = scale_ref[...]
    values = jnp.concatenate(
        [jnp.sum(jnp.where(select, picked[f * rows : (f + 1) * rows], 0.0), axis=0, keepdims=True) for f in range(fields)],
        axis=0,
    ) * scale
    width = out_ref.shape[1]
    total = values[:, :width]
    for chunk in range(1, per):
        total = total + values[:, chunk * width : (chunk + 1) * width]
    values = total

    @pl.when(pl.program_id(1) == 0)
    def first():
        out_ref[...] = values

    @pl.when(pl.program_id(1) > 0)
    def rest_steps():
        out_ref[...] = out_ref[...] + values


def onehot_gather(table, index, scale, groups):
    fields, rows, lanes = table.shape
    flat = index.reshape(1, -1)
    count = flat.shape[1]
    width = count // groups
    tile = 128
    while tile < 8192 and width % (2 * tile) == 0 and fields * rows * tile * 8 <= 4 * 2**20:
        tile *= 2
    blocks = width // tile
    per = groups if blocks == 1 and fields * rows * count * 8 <= 16 * 2**20 else 1
    return pl.pallas_call(
        functools.partial(gather_kernel, per=per),
        grid=(blocks, groups // per),
        in_specs=[
            pl.BlockSpec((1, per * tile), lambda step, group: (0, group * blocks + step)),
            pl.BlockSpec((1, per * tile), lambda step, group: (0, group * blocks + step)),
            pl.BlockSpec((fields, rows, lanes), lambda step, group: (0, 0, 0)),
        ],
        out_specs=pl.BlockSpec((fields, tile), lambda step, group: (0, step)),
        out_shape=jax.ShapeDtypeStruct((fields, width), jnp.float32),
    )(flat, scale.reshape(1, -1), table)


def per_device(
    atm_state,
    metric,
    send_idx,
    send_counts,
    ocean_tracers,
    ocean_velocity,
    remap_slots,
    remap_weights,
):
    fields, levels, xlocal, ylocal = atm_state.shape
    derivative_np, weights_np, massw_np = gll_tables()
    state_now = atm_state.reshape(fields * levels, xlocal, ylocal)
    inv_mass = mass_inverse(massw_np, xlocal, ylocal)
    for repeat in range(SUB):
        state_now = substep(state_now, metric, derivative_np, weights_np, inv_mass)
    atm_out = state_now.reshape(fields, levels, xlocal, ylocal)
    bottom = atm_out[:, levels - 1]
    speed = jnp.sqrt(1.0 + bottom[0] * bottom[0] + bottom[1] * bottom[1])
    flux_flat = (bottom * speed).reshape(fields, xlocal * ylocal)
    node_total = xlocal * ylocal
    rank_total = send_idx.shape[1]
    slot_cap = send_idx.shape[2]
    count_row = send_counts[0]
    live_slots = (jnp.arange(slot_cap)[None, :] < count_row[:, None]).astype(jnp.float32)
    flux_table = flux_flat.reshape(fields, node_total // 128, 128)
    payload = onehot_gather(flux_table, send_idx[0], live_slots, 1).reshape(fields, rank_total, slot_cap)
    received = lax.all_to_all(payload, ("gx", "gy"), split_axis=1, concat_axis=1, tiled=True)
    source_count, ocean_x, ocean_y = remap_slots.shape
    ocean_flux = onehot_gather(received, remap_slots, remap_weights, source_count).reshape(fields, ocean_x, ocean_y)
    velocity = ocean_velocity.at[0, 0].add(wind_coef * jnp.tanh(ocean_flux[0]))
    velocity = velocity.at[1, 0].add(wind_coef * jnp.tanh(ocean_flux[1]))
    tracers = ocean_tracers.at[0, 0].add(surf_coef * ocean_flux[2])
    tracers = tracers.at[1, 0].add(surf_coef * ocean_flux[3])
    for repeat in range(OSTEPS):
        tracers = tracer_step(tracers, velocity)
    return (atm_out, tracers)


def solution(mesh):
    in_specs = (
        P(None, None, "gx", "gy"),
        P(None, "gx", "gy"),
        P(("gx", "gy"), None, None),
        P(("gx", "gy"), None),
        P(None, None, "gx", "gy"),
        P(None, None, "gx", "gy"),
        P(None, "gx", "gy"),
        P(None, "gx", "gy"),
    )
    out_specs = (P(None, None, "gx", "gy"), P(None, None, "gx", "gy"))
    return jax.shard_map(
        per_device, mesh=mesh, in_specs=in_specs, out_specs=out_specs, check_vma=False
    )
```

```python
import functools
import math

import jax
import jax.numpy as jnp
import numpy as np
from jax import lax
from jax.experimental import pallas as pl
from jax.sharding import PartitionSpec as P

SUB = 2
OSTEPS = 2


visc_coef = 0.01
diff_coef = 0.2
wind_coef = 0.1
surf_coef = 0.2


def neighbour(values, step_x, step_y):
    count_x, count_y = lax.axis_size("gx"), lax.axis_size("gy")
    if step_y == 0:
        return lax.ppermute(values, "gx", [(i, (i + step_x) % count_x) for i in range(count_x)])
    if step_x == 0:
        return lax.ppermute(values, "gy", [(j, (j + step_y) % count_y) for j in range(count_y)])
    pairs = [
        (i * count_y + j, ((i + step_x) % count_x) * count_y + (j + step_y) % count_y)
        for i in range(count_x)
        for j in range(count_y)
    ]
    return lax.ppermute(values, ("gx", "gy"), pairs)


def shifted(values, before, after, axis):
    size = values.shape[axis]
    layout = [1] * values.ndim
    layout[axis] = size
    position = jnp.arange(size).reshape(layout)
    prev = jnp.concatenate([lax.slice_in_dim(values, 0, 1, axis=axis), lax.slice_in_dim(values, 0, size - 1, axis=axis)], axis=axis)
    nxt = jnp.concatenate([lax.slice_in_dim(values, 1, size, axis=axis), lax.slice_in_dim(values, size - 1, size, axis=axis)], axis=axis)
    prev = jnp.where(position == 0, jnp.broadcast_to(before, values.shape), prev)
    nxt = jnp.where(position == size - 1, jnp.broadcast_to(after, values.shape), nxt)
    return prev, nxt


def packed(values):
    if values.size % 128:
        return values
    return values.reshape(-1, 128)


def exchange(values, step_x, step_y):
    return neighbour(packed(values), step_x, step_y).reshape(values.shape)


def pair_matrix(size):
    position = np.arange(size)
    starts = position[position % 4 == 0][1:]
    ends = position[position % 4 == 3][:-1]
    pair = np.eye(size)
    pair[starts - 1, starts] = 1.0
    pair[ends + 1, ends] = 1.0
    return pair


def substep(state_in, metric, derivative_np, weights_np, inv_mass):
    levels, xsize, ysize = state_in.shape
    precision = lax.Precision.HIGH
    block_x = np.kron(np.eye(xsize // 4), derivative_np)
    block_y = np.kron(np.eye(ysize // 4), derivative_np)
    weight_x = np.tile(weights_np, xsize // 4)
    weight_y = np.tile(weights_np, ysize // 4)
    pair_y = pair_matrix(ysize)
    term_x_right = jnp.asarray(weight_y[:, None] * pair_y, jnp.float32)
    term_y_right = jnp.asarray(block_y @ pair_y, jnp.float32)
    pair_x = jnp.asarray(pair_matrix(xsize).T, jnp.float32)
    block_x = jnp.asarray(block_x, jnp.float32)
    along_x = jnp.einsum("ab,lby->lay", block_x, state_in, precision=precision)
    scaled_x = jnp.asarray(weight_x[:, None], jnp.float32) * metric[0] * along_x
    term_x = jnp.einsum("ba,lby->lay", block_x, scaled_x, precision=precision)
    along_y = jnp.einsum("lxc,dc->lxd", state_in, jnp.asarray(block_y, jnp.float32), precision=precision)
    scaled_y = jnp.asarray(weight_y[None, :], jnp.float32) * metric[1] * along_y
    merged = jnp.einsum("lxc,cd->lxd", term_x, term_x_right, precision=precision) + jnp.einsum(
        "lxc,cd->lxd", scaled_y, term_y_right, precision=precision
    ) * jnp.asarray(weight_x[:, None], jnp.float32)
    last_x, last_y = xsize - 1, ysize - 1
    from_left = exchange(merged[:, :, last_y], 0, 1)[:, :, None]
    from_right = exchange(merged[:, :, 0], 0, -1)[:, :, None]
    column = jnp.arange(ysize)
    merged = merged + jnp.where(column == 0, from_left, jnp.where(column == last_y, from_right, 0.0))
    from_up = exchange(merged[:, last_x, :], 1, 0)[:, None, :]
    from_down = exchange(merged[:, 0, :], -1, 0)[:, None, :]
    row = jnp.arange(xsize)[:, None]
    total = jnp.einsum("ab,lby->lay", pair_x, merged, precision=precision) + jnp.where(
        row == 0, from_up, jnp.where(row == last_x, from_down, 0.0)
    )
    return state_in - visc_coef * total * inv_mass


def tracer_step(tracers, velocity):
    xsize, ysize = tracers.shape[-2], tracers.shape[-1]
    last_x, last_y = xsize - 1, ysize - 1
    precision = lax.Precision.HIGH
    from_up = exchange(tracers[..., last_x, :], 1, 0)[..., None, :]
    from_down = exchange(tracers[..., 0, :], -1, 0)[..., None, :]
    from_left = exchange(tracers[..., last_y], 0, 1)[..., None]
    from_right = exchange(tracers[..., 0], 0, -1)[..., None]
    above_x = np.eye(xsize, k=1)
    above_y = np.eye(ysize, k=1)
    sum_x = jnp.asarray(above_x + above_x.T, jnp.float32)
    diff_x = jnp.asarray(above_x - above_x.T, jnp.float32)
    sum_y = jnp.asarray(above_y + above_y.T, jnp.float32)
    diff_y = jnp.asarray(above_y.T - above_y, jnp.float32)
    row = jnp.arange(xsize)[:, None]
    column = jnp.arange(ysize)
    east = jnp.where(row == last_x, from_down, 0.0)
    west = jnp.where(row == 0, from_up, 0.0)
    north = jnp.where(column == last_y, from_right, 0.0)
    south = jnp.where(column == 0, from_left, 0.0)
    across_x = jnp.einsum("ab,...by->...ay", sum_x, tracers, precision=precision) + (east + west)
    slope_x = jnp.einsum("ab,...by->...ay", diff_x, tracers, precision=precision) + (east - west)
    across_y = jnp.einsum("...xc,cd->...xd", tracers, sum_y, precision=precision) + (north + south)
    slope_y = jnp.einsum("...xc,cd->...xd", tracers, diff_y, precision=precision) + (north - south)
    return (
        tracers
        + diff_coef * (across_x + across_y - 4.0 * tracers)
        - 0.5 * velocity[0] * slope_x
        - 0.5 * velocity[1] * slope_y
    )


def gll_tables():
    points = np.array([-1.0, -1.0 / np.sqrt(5.0), 1.0 / np.sqrt(5.0), 1.0])
    weights = np.array([1.0 / 6.0, 5.0 / 6.0, 5.0 / 6.0, 1.0 / 6.0])
    derivative = np.zeros((4, 4))
    for target in range(4):
        for source in range(4):
            if target == source:
                derivative[target, source] = np.sum(
                    [
                        1.0 / (points[source] - points[others])
                        for others in range(4)
                        if others != source
                    ]
                )
            else:
                numer = np.prod(
                    [
                        points[target] - points[others]
                        for others in range(4)
                        if others != target and others != source
                    ]
                )
                denom = np.prod(
                    [points[source] - points[others] for others in range(4) if others != source]
                )
                derivative[target, source] = numer / denom
    massw = np.array([1.0 / 3.0, 5.0 / 6.0, 5.0 / 6.0, 1.0 / 3.0])
    return (derivative, weights, massw)


def mass_inverse(massw_np, xsize, ysize):
    return jnp.asarray(
        1.0 / (np.tile(massw_np, xsize // 4)[:, None] * np.tile(massw_np, ysize // 4)[None, :]),
        jnp.float32,
    )


def gather_kernel(index_ref, scale_ref, table_ref, out_ref, per=1):
    fields, rows, lanes = table_ref.shape
    tile = index_ref.shape[1]
    index = index_ref[...]
    onehot = (lax.broadcasted_iota(jnp.int32, (lanes, tile), 0) == (index % lanes)).astype(jnp.bfloat16)
    select = lax.broadcasted_iota(jnp.int32, (rows, tile), 0) == (index // lanes)
    rest = table_ref[...]
    parts = []
    for part in range(3):
        piece = rest.astype(jnp.bfloat16)
        rest = rest - piece.astype(jnp.float32)
        parts.append(piece)
    stacked = jnp.concatenate(parts, axis=2).reshape(fields * rows, 3 * lanes)
    picked = jnp.dot(stacked, jnp.concatenate([onehot] * 3, axis=0), preferred_element_type=jnp.float32)
    scale = scale_ref[...]
    values = jnp.concatenate(
        [jnp.sum(jnp.where(select, picked[f * rows : (f + 1) * rows], 0.0), axis=0, keepdims=True) for f in range(fields)],
        axis=0,
    ) * scale
    width = out_ref.shape[1] * out_ref.shape[2]
    total = values[:, :width]
    for chunk in range(1, per):
        total = total + values[:, chunk * width : (chunk + 1) * width]
    values = total

    @pl.when(pl.program_id(1) == 0)
    def first():
        out_ref[...] = values.reshape(out_ref.shape)

    @pl.when(pl.program_id(1) > 0)
    def rest_steps():
        out_ref[...] = out_ref[...] + values.reshape(out_ref.shape)


def onehot_gather(table, index, scale, groups):
    fields, rows, lanes = table.shape
    flat = index.reshape(1, -1)
    count = flat.shape[1]
    width = count // groups
    tile = 128
    while tile < 8192 and width % (2 * tile) == 0 and fields * rows * tile * 8 <= 4 * 2**20:
        tile *= 2
    blocks = width // tile
    per = groups if blocks == 1 and fields * rows * count * 8 <= 16 * 2**20 else 1
    return pl.pallas_call(
        functools.partial(gather_kernel, per=per),
        grid=(blocks, groups // per),
        in_specs=[
            pl.BlockSpec((1, per * tile), lambda step, group: (0, group * blocks + step)),
            pl.BlockSpec((1, per * tile), lambda step, group: (0, group * blocks + step)),
            pl.BlockSpec((fields, rows, lanes), lambda step, group: (0, 0, 0)),
        ],
        out_specs=pl.BlockSpec((fields, tile // 128, 128), lambda step, group: (0, step, 0)),
        out_shape=jax.ShapeDtypeStruct((fields, width // 128, 128), jnp.float32),
    )(flat, scale.reshape(1, -1), table)


def per_device(
    atm_state,
    metric,
    send_idx,
    send_counts,
    ocean_tracers,
    ocean_velocity,
    remap_slots,
    remap_weights,
):
    fields, levels, xlocal, ylocal = atm_state.shape
    derivative_np, weights_np, massw_np = gll_tables()
    state_now = atm_state.reshape(fields * levels, xlocal, ylocal)
    inv_mass = mass_inverse(massw_np, xlocal, ylocal)
    for repeat in range(SUB):
        state_now = substep(state_now, metric, derivative_np, weights_np, inv_mass)
    atm_out = state_now.reshape(fields, levels, xlocal, ylocal)
    bottom = atm_out[:, levels - 1]
    speed = jnp.sqrt(1.0 + bottom[0] * bottom[0] + bottom[1] * bottom[1])
    flux_flat = (bottom * speed).reshape(fields, xlocal * ylocal)
    node_total = xlocal * ylocal
    rank_total = send_idx.shape[1]
    slot_cap = send_idx.shape[2]
    count_row = send_counts[0]
    live_slots = (jnp.arange(slot_cap)[None, :] < count_row[:, None]).astype(jnp.float32)
    flux_table = flux_flat.reshape(fields, node_total // 128, 128)
    payload = onehot_gather(flux_table, send_idx[0], live_slots, 1).reshape(fields, rank_total, slot_cap)
    received = lax.all_to_all(payload, ("gx", "gy"), split_axis=1, concat_axis=1, tiled=True)
    source_count, ocean_x, ocean_y = remap_slots.shape
    ocean_flux = onehot_gather(received, remap_slots, remap_weights, source_count).reshape(fields, ocean_x, ocean_y)
    velocity = ocean_velocity.at[0, 0].add(wind_coef * jnp.tanh(ocean_flux[0]))
    velocity = velocity.at[1, 0].add(wind_coef * jnp.tanh(ocean_flux[1]))
    tracers = ocean_tracers.at[0, 0].add(surf_coef * ocean_flux[2])
    tracers = tracers.at[1, 0].add(surf_coef * ocean_flux[3])
    for repeat in range(OSTEPS):
        tracers = tracer_step(tracers, velocity)
    return (atm_out, tracers)


def solution(mesh):
    in_specs = (
        P(None, None, "gx", "gy"),
        P(None, "gx", "gy"),
        P(("gx", "gy"), None, None),
        P(("gx", "gy"), None),
        P(None, None, "gx", "gy"),
        P(None, None, "gx", "gy"),
        P(None, "gx", "gy"),
        P(None, "gx", "gy"),
    )
    out_specs = (P(None, None, "gx", "gy"), P(None, None, "gx", "gy"))
    return jax.shard_map(
        per_device, mesh=mesh, in_specs=in_specs, out_specs=out_specs, check_vma=False
    )
```
